32 devices in a mesh: pipe: 2 (over y), expert: 8 (over z, x), dp: 2 (over core).
Axes of the slice: x: 2, y: 2, z: 4, core: 2. Of those that a mesh axis runs over, the one named last changes fastest.
Arguments:
- saved_inputs: bfloat16 [2, 2, 1024, 2560], P('pipe', None, ('expert', 'dp')), may hold values from -30 to 30
- output_grads: bfloat16 [2, 1024, 2560], P(None, ('expert', 'dp')), may hold values from -6 to 6
- entry_grads: bfloat16 [2, 1024, 2560], P('pipe', ('expert', 'dp')), may hold values from -6 to 6
- norm_gain: float32 [2, 2560], P('pipe'), may hold values from 0.4 to 1.6
- expert_ids: int32 [2, 2, 1024, 1], P('pipe', None, ('expert', 'dp')), may hold values from 0 to 1; in each aligned block of 64 rows (0 to 63, 64 to 127, ..., all dimensions but the last counted through in order) at most 48 rows name the same one
- keep_flags: int32 [2, 2, 1024, 1], P('pipe', None, ('expert', 'dp')), may hold values 0 or 1
- combine_weights: bfloat16 [2, 2, 1024, 1], P('pipe', None, ('expert', 'dp')), may hold values from 0.29882812 to 3
- gate_weight: bfloat16 [2, 1536, 2560], P('pipe', 'expert', 'dp'), may hold values from -0.125 to 0.125
- up_weight: bfloat16 [2, 1536, 2560], P('pipe', 'expert', 'dp'), may hold values from -0.125 to 0.125
- down_weight: bfloat16 [2, 1536, 2560], P('pipe', 'expert', 'dp'), may hold values from -0.21875 to 0.21875
Outputs:
- input_grads: bfloat16 [2, 2, 1024, 2560], P('pipe', None, ('expert', 'dp'))
- combine_grads: float32 [2, 2, 1024, 1], P('pipe', None, ('expert', 'dp'))
- gate_grads: bfloat16 [2, 1536, 2560], P('pipe', 'expert', 'dp')
- up_grads: bfloat16 [2, 1536, 2560], P('pipe', 'expert', 'dp')
- down_grads: bfloat16 [2, 1536, 2560], P('pipe', 'expert', 'dp')
The draws below stay inside these ranges and needn't reach their ends.
Inputs may be any that keep to these rules, and one draw needn't show every extreme that they name: `expert_ids`: within the 64 rows of one device at one section and moment no expert is named more than 48 times; some such blocks reach 48.
All inputs are finite; a program needn't handle non-finite values. No bound on the sum of `keep_flags` on one device may be relied on, other than what follows from the above.
Results may differ from the reference program's by a relative error of at most 0.008.
Values may be sent and summed in bfloat16 or wider, within the bound.
No kernel may reach another device: no remote copies, remote signals or barrier semaphores. Data moves between devices by JAX's collectives and lax.ppermute only.
A program may use at most 64 MiB of HBM per device.

```python
import math
import jax
import jax.numpy as jnp
import numpy as np
from jax import lax

D = 2560
HID = 768
HSPLIT = 4
TOP = 1
MICRO = 2
ROWS = 64
HID_DEV = 192
EXPERTS = 2
CAP = 48
TOKENS = 1024
N_PIPE = 2
N_EXPERT = 8
N_DP = 2


def draw_saved_inputs(key, part):
    key_base, key_rows, key_columns = jax.random.split(key, 3)
    full_shape = (N_PIPE, MICRO, TOKENS, D)
    row_scale = jnp.exp(jax.random.uniform(key_rows, (N_PIPE, MICRO, TOKENS, 1), jnp.float32, -1.15, 1.15))
    column_scale = jnp.exp(jax.random.uniform(key_columns, (1, 1, 1, D), jnp.float32, -1.15, 1.15))
    values = jax.random.normal(key_base, full_shape, jnp.float32) * row_scale * column_scale
    return jnp.clip(values, -30.0, 30.0).astype(jnp.bfloat16)


def place_ends(entries, key, smallest, largest):
    dims = entries.shape
    spot = [jax.random.randint(jax.random.fold_in(key, axis), (), 0, dims[axis]) for axis in range(len(dims))]
    entries = entries.at[tuple(spot)].set(smallest)
    longest = dims.index(max(dims))
    spot[longest] = (spot[longest] + 1) % dims[longest]
    return entries.at[tuple(spot)].set(largest)


def steps_of(own_key, extent, cuts, least, top_value):
    def one(axis_at, blocks):
        draws = jax.random.uniform(jax.random.fold_in(jax.random.fold_in(own_key, 6), axis_at), (blocks,), jnp.float32, least / len(cuts), top_value / len(cuts))
        return jnp.repeat(jnp.exp(draws), extent[axis_at] // blocks).reshape((-1,) + (1,) * (len(extent) - axis_at - 1))

    level = one(*cuts[0])
    for cut in cuts[1:]:
        level = level * one(*cut)
    return level


def routed_block(key, own, number, rows, count, top, reach, slope):
    order = jax.random.permutation(key, count)
    crowded, ordinary = portions_of(count, rows * top, reach, slope, True), portions_of(count, rows * top, reach, slope, False)
    places = jnp.arange(count)

    def named(lengths, offset_by):
        used = int((lengths > 0).sum())
        fixed = max(1, used // 4)
        passed = fixed + (places - fixed + offset_by * (used - fixed)) % max(1, count - fixed)
        return jnp.zeros((count,), jnp.int32).at[order[jnp.where(places < fixed, places, passed)]].set(jnp.asarray(lengths, jnp.int32))

    lengths = jnp.where(number % 4 == 0, named(crowded, number // 4), named(ordinary, number - number // 4 - 1))
    mixed = jax.random.permutation(jax.random.fold_in(own, 3), count)
    giver, sink = mixed[0:count // 2 * 2:2], mixed[1:count // 2 * 2:2]
    margin = jnp.minimum(lengths[giver] - 1, reach - lengths[sink]) // 2
    margin = jnp.where((giver == order[0]) | (sink == order[0]) | (lengths[sink] == 0), 0, jnp.maximum(margin, 0))
    passed = jax.random.randint(jax.random.fold_in(own, 4), (count // 2,), 0, 1 << 20) % (margin + 1)
    lengths = lengths.at[giver].add(-passed).at[sink].add(passed)
    labels = jnp.searchsorted(jnp.cumsum(lengths), jnp.arange(rows * top), side="right").astype(jnp.int32)
    grid = labels.reshape(top, rows).T
    grid = grid[jax.random.permutation(jax.random.fold_in(own, 1), rows)]
    offset_by = jax.random.randint(jax.random.fold_in(own, 2), (rows, 1), 0, top)
    return jnp.take_along_axis(grid, (jnp.arange(top)[None, :] + offset_by) % top, axis=1)


def portions_of(count, total, limit, skew, full):
    portions = [(1 << 20) // math.isqrt(standing ** skew) + 1 for standing in range(1, count + 1)]
    largest = limit if full else min(limit, max(-(-total // count), total * portions[0] // sum(portions)))
    least = 1 if total - largest >= count - 1 else 0
    holding, rest = [largest] + [least] * (count - 1), total - largest - least * (count - 1)
    while rest > 0:
        candidates = [i for i in range(1, count) if holding[i] < largest] or [i for i in range(1, count) if holding[i] < limit]
        mass, left = sum([portions[i] for i in candidates]), rest
        for i in candidates:
            extra = min(limit - holding[i], max(1, left * portions[i] // mass), rest)
            holding[i] = holding[i] + extra
            rest = rest - extra
    return np.array(holding)


def bell_draw(key, shape, width, most, cuts=(), kind=jnp.bfloat16):
    entries = width * jax.random.normal(key, shape, jnp.float32)
    if cuts:
        entries = entries * steps_of(key, shape, cuts, -0.22, 0.18)
    return jnp.clip(entries, -most, most).astype(kind)


def setup_inputs(seed: int = 0) -> dict:
    arg_keys = jax.random.split(jax.random.key(seed), 11)
    saved_inputs = draw_saved_inputs(jax.random.fold_in(arg_keys[10], 71), 0)
    output_grads = bell_draw(arg_keys[1], (MICRO, TOKENS, D), 1.0, 6.0, ((1, 16),))
    entry_grads = bell_draw(arg_keys[2], (N_PIPE, TOKENS, D), 1.0, 6.0, ((0, 2), (1, 16)))
    norm_gain = jnp.clip(1.0 + 0.12 * jax.random.normal(arg_keys[3], (N_PIPE, D), jnp.float32), 0.4, 1.6)
    expert_ids_keys = jax.random.split(jax.random.fold_in(arg_keys[4], 1), N_PIPE * MICRO * TOKENS // ROWS)
    expert_ids_turns = jax.random.permutation(jax.random.fold_in(arg_keys[4], 3), N_PIPE * MICRO * TOKENS // ROWS)
    expert_ids = jax.vmap(lambda own, number: routed_block(jax.random.fold_in(arg_keys[4], 2), own, number, ROWS, EXPERTS, TOP, CAP, 2))(expert_ids_keys, expert_ids_turns).reshape((N_PIPE, MICRO, TOKENS, TOP))
    keep_flags = place_ends((jax.random.randint(arg_keys[5], (N_PIPE, MICRO, TOKENS, TOP), 0, 4) < 3).astype(jnp.int32), jax.random.fold_in(arg_keys[5], 1), 0, 1)
    combine_weights = jnp.clip(jnp.exp(math.log(3.0) - 2.306499 * jax.random.uniform(arg_keys[6], (N_PIPE, MICRO, TOKENS, TOP), jnp.float32) ** steps_of(arg_keys[6], (N_PIPE, MICRO, TOKENS, TOP), ((0, 2), (2, 16)), -0.2, 0.2)), 0.29882812, 3.0).astype(jnp.bfloat16)
    gate_weight = bell_draw(arg_keys[7], (N_PIPE, EXPERTS * HID, D), D ** -0.5, 0.125, ((0, 2), (1, 8), (2, 2)))
    up_weight = bell_draw(arg_keys[8], (N_PIPE, EXPERTS * HID, D), D ** -0.5, 0.125, ((0, 2), (1, 8), (2, 2)))
    down_weight = bell_draw(arg_keys[9], (N_PIPE, EXPERTS * HID, D), HID ** -0.5, 0.21875, ((0, 2), (1, 8), (2, 2)))
    return {"saved_inputs": saved_inputs, "output_grads": output_grads, "entry_grads": entry_grads, "norm_gain": norm_gain, "expert_ids": expert_ids, "keep_flags": keep_flags, "combine_weights": combine_weights, "gate_weight": gate_weight, "up_weight": up_weight, "down_weight": down_weight}


EPSILON = 1e-06
EXACT_PRODUCT = lax.Precision.HIGHEST

def silu_parts(gate_value):
    sigmoid_value = jax.nn.sigmoid(gate_value)
    return (gate_value * sigmoid_value, sigmoid_value * (1.0 + gate_value * (1.0 - sigmoid_value)))

def rounded(amount):
    return lax.optimization_barrier(amount.astype(jnp.bfloat16)).astype(jnp.float32)

def section_step(saved, incoming, gain_values, chosen_ids, keeper, weights, gate_mat, up_mat, down_mat):
    blocks = TOKENS // ROWS
    filled = blocks * CAP
    inputs = saved.astype(jnp.float32)
    scales = lax.rsqrt(lax.optimization_barrier(jnp.mean(inputs * inputs, axis=1, keepdims=True)) + EPSILON)
    normed = (inputs * scales * gain_values[None, :]).astype(jnp.bfloat16)
    chosen = chosen_ids.reshape(blocks, ROWS * TOP)
    onehot = (chosen[:, :, None] == jnp.arange(EXPERTS, dtype=jnp.int32)[None, None, :]).astype(jnp.int32)
    rank_values = lax.optimization_barrier(jnp.sum((jnp.cumsum(onehot, axis=1) - 1) * onehot, axis=2))
    places = (jnp.arange(blocks, dtype=jnp.int32)[:, None] * CAP + rank_values).reshape(-1)
    experts_flat = chosen.reshape(-1)
    picks_all = jnp.arange(TOKENS * TOP, dtype=jnp.int32)
    slot_table = jnp.full((EXPERTS, filled), TOKENS * TOP, dtype=jnp.int32).at[experts_flat, places].set(picks_all)
    token_of = slot_table // TOP
    blank_row = jnp.zeros((1, D), jnp.bfloat16)
    normed_slots = jnp.concatenate([normed, blank_row], axis=0)[token_of].astype(jnp.float32)
    grads_slots = jnp.concatenate([incoming, blank_row], axis=0)[token_of].astype(jnp.float32)
    scaled = (weights * keeper.astype(jnp.bfloat16)).reshape(-1)
    scale_slots = jnp.concatenate([scaled, jnp.zeros((1,), jnp.bfloat16)])[slot_table].astype(jnp.float32)[:, None, :, None]
    gate_split = gate_mat.reshape(EXPERTS, HSPLIT, HID_DEV, D).astype(jnp.float32)
    up_split = up_mat.reshape(EXPERTS, HSPLIT, HID_DEV, D).astype(jnp.float32)
    down_split = down_mat.reshape(EXPERTS, HSPLIT, HID_DEV, D).astype(jnp.float32)
    gate_value = jnp.einsum('erd,ejhd->ejrh', normed_slots, gate_split, precision=EXACT_PRODUCT)
    upward = jnp.einsum('erd,ejhd->ejrh', normed_slots, up_split, precision=EXACT_PRODUCT)
    backward = jnp.einsum('erd,ejhd->ejrh', grads_slots, down_split, precision=EXACT_PRODUCT)
    active, derivative = silu_parts(gate_value)
    hidden = active * upward
    part_weight = rounded(lax.optimization_barrier(jnp.sum(hidden * backward, axis=3)))
    grad_up = rounded(scale_slots * backward * active)
    grad_gate = rounded(scale_slots * backward * upward * derivative)
    part_rows = rounded(jnp.einsum('ejrh,ejhd->ejrd', grad_gate, gate_split, precision=EXACT_PRODUCT) + jnp.einsum('ejrh,ejhd->ejrd', grad_up, up_split, precision=EXACT_PRODUCT))
    rows_total = lax.optimization_barrier(jnp.sum(part_rows, axis=1)).reshape(EXPERTS * filled, D)
    weight_total = lax.optimization_barrier(jnp.sum(part_weight, axis=1)).reshape(EXPERTS * filled)
    flat_index = experts_flat * filled + places
    expert_rows = lax.optimization_barrier(jnp.sum(rows_total[flat_index].reshape(TOKENS, TOP, D), axis=1))
    combine_grad = (weight_total[flat_index] * keeper.reshape(-1).astype(jnp.float32)).reshape(TOKENS, TOP)
    gained = gain_values[None, :] * expert_rows
    mixed_mean = lax.optimization_barrier(jnp.mean(inputs * gained, axis=1, keepdims=True))
    leaving = (incoming.astype(jnp.float32) + scales * gained - inputs * (scales * scales * scales) * mixed_mean).astype(jnp.bfloat16)
    hidden_scaled = rounded(hidden * scale_slots)
    group_shape = (EXPERTS, HSPLIT, N_EXPERT, N_DP, CAP, HID_DEV)
    row_shape = (EXPERTS, N_EXPERT, N_DP, CAP, D)
    gate_part = jnp.einsum('ejigch,eigcd->gejhd', grad_gate.reshape(group_shape), normed_slots.reshape(row_shape), precision=EXACT_PRODUCT)
    up_part = jnp.einsum('ejigch,eigcd->gejhd', grad_up.reshape(group_shape), normed_slots.reshape(row_shape), precision=EXACT_PRODUCT)
    down_part = jnp.einsum('ejigch,eigcd->gejhd', hidden_scaled.reshape(group_shape), grads_slots.reshape(row_shape), precision=EXACT_PRODUCT)
    return (leaving, combine_grad, (gate_part, up_part, down_part))

def settle(accumulated):
    return lax.optimization_barrier(jnp.sum(rounded(accumulated), axis=0)).astype(jnp.bfloat16).reshape(EXPERTS * HID, D)

def reference(saved_inputs, output_grads, entry_grads, norm_gain, expert_ids, keep_flags, combine_weights, gate_weight, up_weight, down_weight):
    previous = [None] * N_PIPE
    leaving_all = [[] for section_index in range(N_PIPE)]
    combine_all = [[] for section_index in range(N_PIPE)]
    totals = [None] * N_PIPE
    for moment in range(MICRO):
        current = [None] * N_PIPE
        for section_index in range(N_PIPE):
            if section_index == N_PIPE - 1:
                incoming = output_grads[moment]
            elif moment == 0:
                incoming = entry_grads[section_index]
            else:
                incoming = previous[section_index + 1]
            leaving, combine_grad, parts = section_step(saved_inputs[section_index, moment], incoming, norm_gain[section_index], expert_ids[section_index, moment], keep_flags[section_index, moment], combine_weights[section_index, moment], gate_weight[section_index], up_weight[section_index], down_weight[section_index])
            current[section_index] = leaving
            leaving_all[section_index].append(leaving)
            combine_all[section_index].append(combine_grad)
            if totals[section_index] is None:
                totals[section_index] = parts
            else:
                totals[section_index] = jax.tree.map(jnp.add, totals[section_index], parts)
        previous = current
    input_grads = jnp.stack([jnp.stack(leaving_all[section_index]) for section_index in range(N_PIPE)])
    combine_grads = jnp.stack([jnp.stack(combine_all[section_index]) for section_index in range(N_PIPE)])
    gate_grads = jnp.stack([settle(totals[section_index][0]) for section_index in range(N_PIPE)])
    up_grads = jnp.stack([settle(totals[section_index][1]) for section_index in range(N_PIPE)])
    down_grads = jnp.stack([settle(totals[section_index][2]) for section_index in range(N_PIPE)])
    return (input_grads, combine_grads, gate_grads, up_grads, down_grads)
```

```python
import jax
import jax.numpy as jnp
from jax import lax
from jax.sharding import Mesh, PartitionSpec as P

HSPLIT = 4


EPSILON = 1e-06


def shifted(block, axis, distance):
    devices = range(lax.axis_size(axis))
    route = [(i - distance, i) for i in devices if i - distance in devices]
    return lax.ppermute(block, axis, route)


def rotated(block, axis, distance):
    size = lax.axis_size(axis)
    route = [(i, (i + distance) % size) for i in range(size)]
    return lax.ppermute(block, axis, route)


def silu_parts(gate_value):
    sigmoid_value = jax.nn.sigmoid(gate_value)
    return (gate_value * sigmoid_value, sigmoid_value * (1.0 + gate_value * (1.0 - sigmoid_value)))


def contract_last(first_operand, second_operand):
    return lax.dot_general(
        first_operand, second_operand, (((1,), (1,)), ((), ())), preferred_element_type=jnp.float32
    )


def contract_first(first_operand, second_operand):
    return lax.dot_general(
        first_operand, second_operand, (((0,), (0,)), ((), ())), preferred_element_type=jnp.float32
    )


def to_experts(blocks):
    groups = blocks.shape[0]
    moved = [blocks[0]] + [rotated(blocks[s], "eg", s) for s in range(1, groups)]
    return jnp.stack(moved)


def to_owners(blocks):
    groups = blocks.shape[0]
    moved = [blocks[0]] + [rotated(blocks[s], "eg", -s) for s in range(1, groups)]
    return jnp.stack(moved)


def local(
    saved_inputs,
    output_grads,
    entry_grads,
    norm_gain,
    expert_ids,
    keep_flags,
    combine_weights,
    gate_weight,
    up_weight,
    down_weight,
):
    sections = lax.axis_size("pipe")
    is_last = lax.axis_index("pipe") == sections - 1
    groups = lax.axis_size("eg")
    me = lax.axis_index("eg")
    micro_count = saved_inputs.shape[1]
    token_rows = saved_inputs.shape[2]
    feature_count = saved_inputs.shape[3]
    pick_count = expert_ids.shape[3]
    capacity = max(2, 3 * token_rows * pick_count // (2 * groups))
    slot_count = groups * capacity
    gate_full, up_full, down_full = (
        lax.all_gather(gate_weight[0], "dp", axis=1, tiled=True),
        lax.all_gather(up_weight[0], "dp", axis=1, tiled=True),
        lax.all_gather(down_weight[0], "dp", axis=1, tiled=True),
    )
    hidden_count = gate_full.shape[0]
    paired_weights = jnp.concatenate([gate_full, up_full], axis=0)
    gain_row = norm_gain[0][None, :]
    slot_ids = jnp.arange(slot_count, dtype=jnp.int32)
    expert_range = jnp.arange(groups, dtype=jnp.int32)

    def prepare(moment):
        inputs = saved_inputs[0, moment].astype(jnp.float32)
        scales = lax.rsqrt(jnp.mean(inputs * inputs, axis=1, keepdims=True) + EPSILON)
        normed = (inputs * scales * gain_row).astype(jnp.bfloat16)
        chosen = expert_ids[0, moment].reshape(-1)
        onehot = (chosen[:, None] == expert_range[None, :]).astype(jnp.int32)
        rank_values = jnp.sum((jnp.cumsum(onehot, axis=0) - 1) * onehot, axis=1)
        places = ((chosen - me) % groups) * capacity + rank_values
        placing = places[:, None] == slot_ids[None, :]
        token_map = jnp.any(placing.reshape(token_rows, pick_count, slot_count), axis=1)
        selector = token_map.T.astype(jnp.bfloat16)
        keeping = keep_flags[0, moment].reshape(-1)
        scaled = (combine_weights[0, moment].reshape(-1) * keeping.astype(jnp.bfloat16)).astype(
            jnp.float32
        )
        weight_slots = jnp.sum(jnp.where(placing, scaled[:, None], 0.0), axis=0).astype(
            jnp.bfloat16
        )
        return (inputs, scales, normed, places, selector, keeping, weight_slots)

    def dispatch_rows(selector, source_rows):
        picked = jnp.dot(selector, source_rows, preferred_element_type=jnp.float32)
        return picked.astype(jnp.bfloat16).reshape(groups, capacity, feature_count)

    def gather_quad(blocks):
        return lax.all_gather(to_experts(blocks), "ej", axis=0, tiled=True)

    prepared = [prepare(moment) for moment in range(micro_count)]
    rows_gathered = [
        gather_quad(dispatch_rows(current[4], current[2])) for current in prepared
    ]
    weights_gathered = [
        gather_quad(current[6].reshape(groups, capacity)) for current in prepared
    ]
    leaving_list = []
    combine_list = []
    kept_list = []
    previous = entry_grads[0]
    for moment in range(micro_count):
        current = prepared[moment]
        if moment == 0:
            arriving = entry_grads[0]
        else:
            arriving = shifted(previous, "pipe", -1)
        incoming = jnp.where(is_last, output_grads[moment], arriving)
        grads_in = gather_quad(dispatch_rows(current[4], incoming))
        flat_rows = rows_gathered[moment].reshape(-1, feature_count)
        flat_grads = grads_in.reshape(-1, feature_count)
        scale_column = weights_gathered[moment].reshape(-1, 1).astype(jnp.float32)
        gate_value = contract_last(flat_rows, gate_full)
        upward = contract_last(flat_rows, up_full)
        backward = contract_last(flat_grads, down_full)
        active, derivative = silu_parts(gate_value)
        hidden = active * upward
        part_weight = jnp.sum(hidden * backward, axis=1).astype(jnp.bfloat16)
        grad_up = (scale_column * backward * active).astype(jnp.bfloat16)
        grad_gate = (scale_column * backward * upward * derivative).astype(jnp.bfloat16)
        grad_pair = jnp.concatenate([grad_gate, grad_up], axis=1)
        part_rows = jnp.dot(grad_pair, paired_weights, preferred_element_type=jnp.float32).astype(
            jnp.bfloat16
        )
        hidden_scaled = (hidden * scale_column).astype(jnp.bfloat16)
        kept_list.append((grad_pair, hidden_scaled, flat_rows, flat_grads))
        rows_back = to_owners(
            lax.psum_scatter(
                part_rows.reshape(-1, capacity, feature_count), "ej", scatter_dimension=0, tiled=True
            )
        )
        weights_back = to_owners(
            lax.psum_scatter(
                part_weight.astype(jnp.float32).reshape(-1, capacity),
                "ej",
                scatter_dimension=0,
                tiled=True,
            )
        )
        (
            finish_inputs,
            finish_scales,
            finish_normed,
            finish_places,
            finish_selector,
            finish_keeping,
            finish_weight_slots,
        ) = current
        summed = rows_back.astype(jnp.float32).reshape(slot_count, feature_count)
        weight_sums = weights_back.reshape(slot_count)
        expert_rows = jnp.sum(
            jnp.take(summed, finish_places, axis=0).reshape(token_rows, pick_count, feature_count),
            axis=1,
        )
        combine_grad = (
            jnp.take(weight_sums, finish_places) * finish_keeping.astype(jnp.float32)
        ).reshape(token_rows, pick_count)
        gained = gain_row * expert_rows
        mixed_mean = jnp.mean(finish_inputs * gained, axis=1, keepdims=True)
        leaving = (
            incoming.astype(jnp.float32)
            + finish_scales * gained
            - finish_inputs * (finish_scales * finish_scales * finish_scales) * mixed_mean
        ).astype(jnp.bfloat16)
        previous = leaving
        leaving_list.append(leaving)
        combine_list.append(combine_grad)
    pair_all = jnp.concatenate([kept[0] for kept in kept_list], axis=0)
    scaled_all = jnp.concatenate([kept[1] for kept in kept_list], axis=0)
    rows_all = jnp.concatenate([kept[2] for kept in kept_list], axis=0)
    grads_all = jnp.concatenate([kept[3] for kept in kept_list], axis=0)
    pair_total = contract_first(pair_all, rows_all).reshape(2, hidden_count, feature_count)
    down_total = contract_first(scaled_all, grads_all)[None]
    pair_reduced, down_reduced = (
        lax.psum_scatter(
            pair_total.astype(jnp.bfloat16), "dp", scatter_dimension=2, tiled=True
        ).astype(jnp.float32),
        lax.psum_scatter(
            down_total.astype(jnp.bfloat16), "dp", scatter_dimension=2, tiled=True
        ).astype(jnp.float32),
    )
    return (
        jnp.stack(leaving_list)[None],
        jnp.stack(combine_list)[None],
        pair_reduced[0:1].astype(jnp.bfloat16),
        pair_reduced[1:2].astype(jnp.bfloat16),
        down_reduced.astype(jnp.bfloat16),
    )


def solution(mesh):
    sizes = dict(zip(mesh.axis_names, mesh.devices.shape))
    members = sizes["expert"]
    grid = mesh.devices.reshape(sizes["pipe"], members // HSPLIT, HSPLIT, sizes["dp"])
    fine = Mesh(grid, ("pipe", "eg", "ej", "dp"))
    tokens = ("eg", "ej", "dp")
    rows = ("eg", "ej")
    in_specs = (
        P("pipe", None, tokens, None),
        P(None, tokens, None),
        P("pipe", tokens, None),
        P("pipe", None),
        P("pipe", None, tokens, None),
        P("pipe", None, tokens, None),
        P("pipe", None, tokens, None),
        P("pipe", rows, "dp"),
        P("pipe", rows, "dp"),
        P("pipe", rows, "dp"),
    )
    out_specs = (
        P("pipe", None, tokens, None),
        P("pipe", None, tokens, None),
        P("pipe", rows, "dp"),
        P("pipe", rows, "dp"),
        P("pipe", rows, "dp"),
    )
    return jax.shard_map(local, mesh=fine, in_specs=in_specs, out_specs=out_specs, check_vma=False)
```

```python
import jax
import jax.numpy as jnp
from jax import lax
from jax.sharding import Mesh, PartitionSpec as P

HSPLIT = 4


EPSILON = 1e-06


def shifted(block, axis, distance):
    devices = range(lax.axis_size(axis))
    route = [(i - distance, i) for i in devices if i - distance in devices]
    return lax.ppermute(block, axis, route)


def rotated(block, axis, distance):
    size = lax.axis_size(axis)
    route = [(i, (i + distance) % size) for i in range(size)]
    return lax.ppermute(block, axis, route)


def flipped(block, axis, mask):
    size = lax.axis_size(axis)
    route = [(i, i ^ mask) for i in range(size)]
    return lax.ppermute(block, axis, route)


def silu_parts(gate_value):
    sigmoid_value = jax.nn.sigmoid(gate_value)
    return (gate_value * sigmoid_value, sigmoid_value * (1.0 + gate_value * (1.0 - sigmoid_value)))


def contract_last(first_operand, second_operand):
    return lax.dot_general(
        first_operand, second_operand, (((1,), (1,)), ((), ())), preferred_element_type=jnp.float32
    )


def contract_first(first_operand, second_operand):
    return lax.dot_general(
        first_operand, second_operand, (((0,), (0,)), ((), ())), preferred_element_type=jnp.float32
    )


def to_experts(blocks):
    groups = blocks.shape[0]
    moved = [blocks[0]] + [rotated(blocks[s], "eg", s) for s in range(1, groups)]
    return jnp.stack(moved)


def to_owners(blocks):
    groups = blocks.shape[0]
    moved = [blocks[0]] + [
        rotated(blocks[s].astype(jnp.bfloat16), "eg", -s).astype(jnp.float32)
        for s in range(1, groups)
    ]
    return jnp.stack(moved)


def weights_to_owners(blocks):
    groups = blocks.shape[0]
    moved = [blocks[0]] + [rotated(blocks[s], "eg", -s) for s in range(1, groups)]
    return jnp.stack(moved)


def gather_quad(blocks):
    staged = to_experts(blocks)
    quad = lax.axis_size("ej")
    return jnp.stack([staged] + [flipped(staged, "ej", t) for t in range(1, quad)])


def reduce_quad(parts):
    quad = parts.shape[0]
    total = parts[0].astype(jnp.float32)
    for t in range(1, quad):
        total = total + flipped(parts[t], "ej", t).astype(jnp.float32)
    return total


def local(
    saved_inputs,
    output_grads,
    entry_grads,
    norm_gain,
    expert_ids,
    keep_flags,
    combine_weights,
    gate_weight,
    up_weight,
    down_weight,
):
    sections = lax.axis_size("pipe")
    is_last = lax.axis_index("pipe") == sections - 1
    groups = lax.axis_size("eg")
    me = lax.axis_index("eg")
    micro_count = saved_inputs.shape[1]
    token_rows = saved_inputs.shape[2]
    feature_count = saved_inputs.shape[3]
    pick_count = expert_ids.shape[3]
    capacity = max(2, 3 * token_rows * pick_count // (2 * groups))
    slot_count = groups * capacity
    gate_full, up_full, down_full = (
        lax.all_gather(gate_weight[0], "dp", axis=1, tiled=True),
        lax.all_gather(up_weight[0], "dp", axis=1, tiled=True),
        lax.all_gather(down_weight[0], "dp", axis=1, tiled=True),
    )
    hidden_count = gate_full.shape[0]
    paired_weights = jnp.concatenate([gate_full, up_full], axis=0)
    gain_row = norm_gain[0][None, :]
    slot_ids = jnp.arange(slot_count, dtype=jnp.int32)
    expert_range = jnp.arange(groups, dtype=jnp.int32)

    def prepare(moment):
        inputs = saved_inputs[0, moment].astype(jnp.float32)
        scales = lax.rsqrt(jnp.mean(inputs * inputs, axis=1, keepdims=True) + EPSILON)
        normed = (inputs * scales * gain_row).astype(jnp.bfloat16)
        chosen = expert_ids[0, moment].reshape(-1)
        onehot = (chosen[:, None] == expert_range[None, :]).astype(jnp.int32)
        rank_values = jnp.sum((jnp.cumsum(onehot, axis=0) - 1) * onehot, axis=1)
        places = ((chosen - me) % groups) * capacity + rank_values
        placing = places[:, None] == slot_ids[None, :]
        token_map = jnp.any(placing.reshape(token_rows, pick_count, slot_count), axis=1)
        selector = token_map.T.astype(jnp.bfloat16)
        keeping = keep_flags[0, moment].reshape(-1)
        scaled = (combine_weights[0, moment].reshape(-1) * keeping.astype(jnp.bfloat16)).astype(
            jnp.float32
        )
        weight_slots = jnp.sum(jnp.where(placing, scaled[:, None], 0.0), axis=0).astype(
            jnp.bfloat16
        )
        return (inputs, scales, normed, places, selector, keeping, weight_slots)

    def dispatch_rows(selector, source_rows):
        picked = jnp.dot(selector, source_rows, preferred_element_type=jnp.float32)
        return picked.astype(jnp.bfloat16).reshape(groups, capacity, feature_count)

    prepared = [prepare(moment) for moment in range(micro_count)]
    rows_gathered = [
        gather_quad(dispatch_rows(current[4], current[2])) for current in prepared
    ]
    weights_gathered = [
        gather_quad(current[6].reshape(groups, capacity)) for current in prepared
    ]
    leaving_list = []
    combine_list = []
    kept_list = []
    previous = entry_grads[0]
    for moment in range(micro_count):
        current = prepared[moment]
        if moment == 0:
            arriving = entry_grads[0]
        else:
            arriving = shifted(previous, "pipe", -1)
        incoming = jnp.where(is_last, output_grads[moment], arriving)
        grads_in = gather_quad(dispatch_rows(current[4], incoming))
        flat_rows = rows_gathered[moment].reshape(-1, feature_count)
        flat_grads = grads_in.reshape(-1, feature_count)
        scale_column = weights_gathered[moment].reshape(-1, 1).astype(jnp.float32)
        gate_value = contract_last(flat_rows, gate_full)
        upward = contract_last(flat_rows, up_full)
        backward = contract_last(flat_grads, down_full)
        active, derivative = silu_parts(gate_value)
        hidden = active * upward
        part_weight = jnp.sum(hidden * backward, axis=1).astype(jnp.bfloat16)
        grad_up = (scale_column * backward * active).astype(jnp.bfloat16)
        grad_gate = (scale_column * backward * upward * derivative).astype(jnp.bfloat16)
        grad_pair = jnp.concatenate([grad_gate, grad_up], axis=1)
        part_rows = jnp.dot(grad_pair, paired_weights, preferred_element_type=jnp.float32).astype(
            jnp.bfloat16
        )
        hidden_scaled = (hidden * scale_column).astype(jnp.bfloat16)
        kept_list.append((grad_pair, hidden_scaled, flat_rows, flat_grads))
        rows_back = to_owners(
            reduce_quad(part_rows.reshape(-1, groups, capacity, feature_count))
        )
        weights_back = weights_to_owners(
            reduce_quad(part_weight.reshape(-1, groups, capacity))
        )
        (
            finish_inputs,
            finish_scales,
            finish_normed,
            finish_places,
            finish_selector,
            finish_keeping,
            finish_weight_slots,
        ) = current
        summed = rows_back.reshape(slot_count, feature_count)
        weight_sums = weights_back.reshape(slot_count)
        expert_rows = jnp.sum(
            jnp.take(summed, finish_places, axis=0).reshape(token_rows, pick_count, feature_count),
            axis=1,
        )
        combine_grad = (
            jnp.take(weight_sums, finish_places) * finish_keeping.astype(jnp.float32)
        ).reshape(token_rows, pick_count)
        gained = gain_row * expert_rows
        mixed_mean = jnp.mean(finish_inputs * gained, axis=1, keepdims=True)
        leaving = (
            incoming.astype(jnp.float32)
            + finish_scales * gained
            - finish_inputs * (finish_scales * finish_scales * finish_scales) * mixed_mean
        ).astype(jnp.bfloat16)
        previous = leaving
        leaving_list.append(leaving)
        combine_list.append(combine_grad)
    pair_all = jnp.concatenate([kept[0] for kept in kept_list], axis=0)
    scaled_all = jnp.concatenate([kept[1] for kept in kept_list], axis=0)
    rows_all = jnp.concatenate([kept[2] for kept in kept_list], axis=0)
    grads_all = jnp.concatenate([kept[3] for kept in kept_list], axis=0)
    pair_total = contract_first(pair_all, rows_all).reshape(2, hidden_count, feature_count)
    down_total = contract_first(scaled_all, grads_all)[None]
    pair_reduced, down_reduced = (
        lax.psum_scatter(
            pair_total.astype(jnp.bfloat16), "dp", scatter_dimension=2, tiled=True
        ).astype(jnp.float32),
        lax.psum_scatter(
            down_total.astype(jnp.bfloat16), "dp", scatter_dimension=2, tiled=True
        ).astype(jnp.float32),
    )
    return (
        jnp.stack(leaving_list)[None],
        jnp.stack(combine_list)[None],
        pair_reduced[0:1].astype(jnp.bfloat16),
        pair_reduced[1:2].astype(jnp.bfloat16),
        down_reduced.astype(jnp.bfloat16),
    )


def solution(mesh):
    sizes = dict(zip(mesh.axis_names, mesh.devices.shape))
    members = sizes["expert"]
    grid = mesh.devices.reshape(sizes["pipe"], members // HSPLIT, HSPLIT, sizes["dp"])
    fine = Mesh(grid, ("pipe", "eg", "ej", "dp"))
    tokens = ("eg", "ej", "dp")
    rows = ("eg", "ej")
    in_specs = (
        P("pipe", None, tokens, None),
        P(None, tokens, None),
        P("pipe", tokens, None),
        P("pipe", None),
        P("pipe", None, tokens, None),
        P("pipe", None, tokens, None),
        P("pipe", None, tokens, None),
        P("pipe", rows, "dp"),
        P("pipe", rows, "dp"),
        P("pipe", rows, "dp"),
    )
    out_specs = (
        P("pipe", None, tokens, None),
        P("pipe", None, tokens, None),
        P("pipe", rows, "dp"),
        P("pipe", rows, "dp"),
        P("pipe", rows, "dp"),
    )
    return jax.shard_map(local, mesh=fine, in_specs=in_specs, out_specs=out_specs, check_vma=False)
```

```python
import jax
import jax.numpy as jnp
from jax import lax
from jax.sharding import Mesh, PartitionSpec as P

HSPLIT = 4


EPSILON = 1e-06


def shifted(block, axis, distance):
    devices = range(lax.axis_size(axis))
    route = [(i - distance, i) for i in devices if i - distance in devices]
    return lax.ppermute(block, axis, route)


def rotated(block, axis, distance):
    size = lax.axis_size(axis)
    route = [(i, (i + distance) % size) for i in range(size)]
    return lax.ppermute(block, axis, route)


def flipped(block, axis, mask):
    size = lax.axis_size(axis)
    route = [(i, i ^ mask) for i in range(size)]
    return lax.ppermute(block, axis, route)


def silu_parts(gate_value):
    sigmoid_value = jax.nn.sigmoid(gate_value)
    return (gate_value * sigmoid_value, sigmoid_value * (1.0 + gate_value * (1.0 - sigmoid_value)))


def contract_last(first_operand, second_operand):
    return lax.dot_general(
        first_operand, second_operand, (((1,), (1,)), ((), ())), preferred_element_type=jnp.float32
    )


def contract_first(first_operand, second_operand):
    return lax.dot_general(
        first_operand, second_operand, (((0,), (0,)), ((), ())), preferred_element_type=jnp.float32
    )


def to_experts(blocks):
    groups = blocks.shape[0]
    moved = [blocks[0]] + [rotated(blocks[s], "eg", s) for s in range(1, groups)]
    return jnp.stack(moved)


def gather_quad(blocks):
    staged = to_experts(blocks)
    quad = lax.axis_size("ej")
    return jnp.stack([staged] + [flipped(staged, "ej", t) for t in range(1, quad)])


def reduce_quad(parts):
    quad = parts.shape[0]
    total = parts[0].astype(jnp.float32)
    for t in range(1, quad):
        total = total + flipped(parts[t], "ej", t).astype(jnp.float32)
    return total


def local(
    saved_inputs,
    output_grads,
    entry_grads,
    norm_gain,
    expert_ids,
    keep_flags,
    combine_weights,
    gate_weight,
    up_weight,
    down_weight,
):
    sections = lax.axis_size("pipe")
    is_last = lax.axis_index("pipe") == sections - 1
    groups = lax.axis_size("eg")
    me = lax.axis_index("eg")
    micro_count = saved_inputs.shape[1]
    token_rows = saved_inputs.shape[2]
    feature_count = saved_inputs.shape[3]
    pick_count = expert_ids.shape[3]
    capacity = max(2, 3 * token_rows * pick_count // (2 * groups))
    slot_count = groups * capacity
    gate_full, up_full, down_full = (
        lax.all_gather(gate_weight[0], "dp", axis=1, tiled=True),
        lax.all_gather(up_weight[0], "dp", axis=1, tiled=True),
        lax.all_gather(down_weight[0], "dp", axis=1, tiled=True),
    )
    hidden_count = gate_full.shape[0]
    paired_weights = jnp.concatenate([gate_full, up_full], axis=0)
    gain_row = norm_gain[0][None, :]
    slot_ids = jnp.arange(slot_count, dtype=jnp.int32)
    expert_range = jnp.arange(groups, dtype=jnp.int32)

    def prepare(moment):
        inputs = saved_inputs[0, moment].astype(jnp.float32)
        scales = lax.rsqrt(jnp.mean(inputs * inputs, axis=1, keepdims=True) + EPSILON)
        normed = (inputs * scales * gain_row).astype(jnp.bfloat16)
        chosen = expert_ids[0, moment].reshape(-1)
        onehot = (chosen[:, None] == expert_range[None, :]).astype(jnp.int32)
        rank_values = jnp.sum((jnp.cumsum(onehot, axis=0) - 1) * onehot, axis=1)
        places = ((chosen - me) % groups) * capacity + rank_values
        placing = places[:, None] == slot_ids[None, :]
        token_map = jnp.any(placing.reshape(token_rows, pick_count, slot_count), axis=1)
        selector = token_map.T.astype(jnp.bfloat16)
        keeping = keep_flags[0, moment].reshape(-1)
        scaled = (combine_weights[0, moment].reshape(-1) * keeping.astype(jnp.bfloat16)).astype(
            jnp.float32
        )
        weight_slots = jnp.sum(jnp.where(placing, scaled[:, None], 0.0), axis=0).astype(
            jnp.bfloat16
        )
        return (inputs, scales, normed, places, selector, keeping, weight_slots)

    def dispatch_rows(selector, source_rows):
        picked = jnp.dot(selector, source_rows, preferred_element_type=jnp.float32)
        return picked.astype(jnp.bfloat16).reshape(groups, capacity, feature_count)

    def weight_row(weight_slots):
        shaped = weight_slots.reshape(groups, 1, capacity)
        return jnp.pad(shaped, ((0, 0), (0, 0), (0, feature_count - capacity)))

    def send_back(part_rows, part_weight):
        quad_rows = part_rows.reshape(-1, groups, capacity, feature_count)
        quad_weight = jnp.pad(
            part_weight.reshape(-1, groups, 1, capacity),
            ((0, 0), (0, 0), (0, 0), (0, feature_count - capacity)),
        )
        total = reduce_quad(jnp.concatenate([quad_rows, quad_weight], axis=2))
        back_rows = [total[0, :capacity]]
        back_weight = [total[0, capacity, :capacity]]
        for s in range(1, groups):
            high = total[s, capacity:].astype(jnp.bfloat16)
            low = (total[s, capacity:] - high.astype(jnp.float32)).astype(jnp.bfloat16)
            block = jnp.concatenate([total[s, :capacity].astype(jnp.bfloat16), high, low], axis=0)
            got = rotated(block, "eg", -s).astype(jnp.float32)
            back_rows.append(got[:capacity])
            back_weight.append(got[capacity, :capacity] + got[capacity + 1, :capacity])
        return (
            jnp.stack(back_rows).reshape(slot_count, feature_count),
            jnp.stack(back_weight).reshape(slot_count),
        )

    prepared = [prepare(moment) for moment in range(micro_count)]
    first_incoming = jnp.where(is_last, output_grads[0], entry_grads[0])
    payload = jnp.concatenate(
        [dispatch_rows(current[4], current[2]) for current in prepared]
        + [dispatch_rows(prepared[0][4], first_incoming)]
        + [weight_row(current[6]) for current in prepared],
        axis=1,
    )
    gathered = gather_quad(payload)
    rows_gathered = [
        gathered[:, :, moment * capacity : (moment + 1) * capacity].reshape(-1, feature_count)
        for moment in range(micro_count)
    ]
    first_grads = gathered[:, :, micro_count * capacity : (micro_count + 1) * capacity]
    weights_gathered = [
        gathered[:, :, (micro_count + 1) * capacity + moment, :capacity].reshape(-1, 1)
        for moment in range(micro_count)
    ]
    leaving_list = []
    combine_list = []
    kept_list = []
    previous = entry_grads[0]
    for moment in range(micro_count):
        current = prepared[moment]
        if moment == 0:
            incoming = first_incoming
            grads_in = first_grads
        else:
            arriving = shifted(previous, "pipe", -1)
            incoming = jnp.where(is_last, output_grads[moment], arriving)
            grads_in = gather_quad(dispatch_rows(current[4], incoming))
        flat_rows = rows_gathered[moment]
        flat_grads = grads_in.reshape(-1, feature_count)
        scale_column = weights_gathered[moment].astype(jnp.float32)
        gate_value = contract_last(flat_rows, gate_full)
        upward = contract_last(flat_rows, up_full)
        backward = contract_last(flat_grads, down_full)
        active, derivative = silu_parts(gate_value)
        hidden = active * upward
        part_weight = jnp.sum(hidden * backward, axis=1).astype(jnp.bfloat16)
        grad_up = (scale_column * backward * active).astype(jnp.bfloat16)
        grad_gate = (scale_column * backward * upward * derivative).astype(jnp.bfloat16)
        grad_pair = jnp.concatenate([grad_gate, grad_up], axis=1)
        part_rows = jnp.dot(grad_pair, paired_weights, preferred_element_type=jnp.float32).astype(
            jnp.bfloat16
        )
        hidden_scaled = (hidden * scale_column).astype(jnp.bfloat16)
        kept_list.append((grad_pair, hidden_scaled, flat_rows, flat_grads))
        summed, weight_sums = send_back(part_rows, part_weight)
        (
            finish_inputs,
            finish_scales,
            finish_normed,
            finish_places,
            finish_selector,
            finish_keeping,
            finish_weight_slots,
        ) = current
        expert_rows = jnp.sum(
            jnp.take(summed, finish_places, axis=0).reshape(token_rows, pick_count, feature_count),
            axis=1,
        )
        combine_grad = (
            jnp.take(weight_sums, finish_places) * finish_keeping.astype(jnp.float32)
        ).reshape(token_rows, pick_count)
        gained = gain_row * expert_rows
        mixed_mean = jnp.mean(finish_inputs * gained, axis=1, keepdims=True)
        leaving = (
            incoming.astype(jnp.float32)
            + finish_scales * gained
            - finish_inputs * (finish_scales * finish_scales * finish_scales) * mixed_mean
        ).astype(jnp.bfloat16)
        previous = leaving
        leaving_list.append(leaving)
        combine_list.append(combine_grad)
    pair_all = jnp.concatenate([kept[0] for kept in kept_list], axis=0)
    scaled_all = jnp.concatenate([kept[1] for kept in kept_list], axis=0)
    rows_all = jnp.concatenate([kept[2] for kept in kept_list], axis=0)
    grads_all = jnp.concatenate([kept[3] for kept in kept_list], axis=0)
    pair_total = contract_first(pair_all, rows_all).reshape(2, hidden_count, feature_count)
    down_total = contract_first(scaled_all, grads_all)[None]
    pair_reduced, down_reduced = (
        lax.psum_scatter(
            pair_total.astype(jnp.bfloat16), "dp", scatter_dimension=2, tiled=True
        ).astype(jnp.float32),
        lax.psum_scatter(
            down_total.astype(jnp.bfloat16), "dp", scatter_dimension=2, tiled=True
        ).astype(jnp.float32),
    )
    return (
        jnp.stack(leaving_list)[None],
        jnp.stack(combine_list)[None],
        pair_reduced[0:1].astype(jnp.bfloat16),
        pair_reduced[1:2].astype(jnp.bfloat16),
        down_reduced.astype(jnp.bfloat16),
    )


def solution(mesh):
    sizes = dict(zip(mesh.axis_names, mesh.devices.shape))
    members = sizes["expert"]
    grid = mesh.devices.reshape(sizes["pipe"], members // HSPLIT, HSPLIT, sizes["dp"])
    fine = Mesh(grid, ("pipe", "eg", "ej", "dp"))
    tokens = ("eg", "ej", "dp")
    rows = ("eg", "ej")
    in_specs = (
        P("pipe", None, tokens, None),
        P(None, tokens, None),
        P("pipe", tokens, None),
        P("pipe", None),
        P("pipe", None, tokens, None),
        P("pipe", None, tokens, None),
        P("pipe", None, tokens, None),
        P("pipe", rows, "dp"),
        P("pipe", rows, "dp"),
        P("pipe", rows, "dp"),
    )
    out_specs = (
        P("pipe", None, tokens, None),
        P("pipe", None, tokens, None),
        P("pipe", rows, "dp"),
        P("pipe", rows, "dp"),
        P("pipe", rows, "dp"),
    )
    return jax.shard_map(local, mesh=fine, in_specs=in_specs, out_specs=out_specs, check_vma=False)
```

```python
import jax
import jax.numpy as jnp
from jax import lax
from jax.sharding import Mesh, PartitionSpec as P

HSPLIT = 4


EPSILON = 1e-06


def shifted(block, axis, distance):
    devices = range(lax.axis_size(axis))
    route = [(i - distance, i) for i in devices if i - distance in devices]
    return lax.ppermute(block, axis, route)


def rotated(block, axis, distance):
    size = lax.axis_size(axis)
    route = [(i, (i + distance) % size) for i in range(size)]
    return lax.ppermute(block, axis, route)


def flipped(block, axis, mask):
    size = lax.axis_size(axis)
    route = [(i, i ^ mask) for i in range(size)]
    return lax.ppermute(block, axis, route)


def silu_parts(gate_value):
    sigmoid_value = jax.nn.sigmoid(gate_value)
    return (gate_value * sigmoid_value, sigmoid_value * (1.0 + gate_value * (1.0 - sigmoid_value)))


def contract_last(first_operand, second_operand):
    return lax.dot_general(
        first_operand, second_operand, (((1,), (1,)), ((), ())), preferred_element_type=jnp.float32
    )


def contract_first(first_operand, second_operand):
    return lax.dot_general(
        first_operand, second_operand, (((0,), (0,)), ((), ())), preferred_element_type=jnp.float32
    )


def local(
    saved_inputs,
    output_grads,
    entry_grads,
    norm_gain,
    expert_ids,
    keep_flags,
    combine_weights,
    gate_weight,
    up_weight,
    down_weight,
):
    sections = lax.axis_size("pipe")
    is_last = lax.axis_index("pipe") == sections - 1
    groups = lax.axis_size("eg")
    me = lax.axis_index("eg")
    micro_count = saved_inputs.shape[1]
    token_rows = saved_inputs.shape[2]
    feature_count = saved_inputs.shape[3]
    pick_count = expert_ids.shape[3]
    capacity = max(2, 3 * token_rows * pick_count // (2 * groups))
    slot_count = groups * capacity
    gate_full, up_full, down_full = (
        lax.all_gather(gate_weight[0], "dp", axis=1, tiled=True),
        lax.all_gather(up_weight[0], "dp", axis=1, tiled=True),
        lax.all_gather(down_weight[0], "dp", axis=1, tiled=True),
    )
    hidden_count = gate_full.shape[0]
    paired_weights = jnp.concatenate([gate_full, up_full], axis=0)
    gain_row = norm_gain[0][None, :]
    slot_ids = jnp.arange(slot_count, dtype=jnp.int32)
    expert_range = jnp.arange(groups, dtype=jnp.int32)

    def prepare(moment):
        inputs = saved_inputs[0, moment].astype(jnp.float32)
        scales = lax.rsqrt(jnp.mean(inputs * inputs, axis=1, keepdims=True) + EPSILON)
        normed = (inputs * scales * gain_row).astype(jnp.bfloat16)
        chosen = expert_ids[0, moment].reshape(-1)
        onehot = (chosen[:, None] == expert_range[None, :]).astype(jnp.int32)
        rank_values = jnp.sum((jnp.cumsum(onehot, axis=0) - 1) * onehot, axis=1)
        places = ((chosen - me) % groups) * capacity + rank_values
        placing = places[:, None] == slot_ids[None, :]
        token_map = jnp.any(placing.reshape(token_rows, pick_count, slot_count), axis=1)
        selector = token_map.T.astype(jnp.bfloat16)
        keeping = keep_flags[0, moment].reshape(-1)
        scaled = (combine_weights[0, moment].reshape(-1) * keeping.astype(jnp.bfloat16)).astype(
            jnp.float32
        )
        weight_slots = jnp.sum(jnp.where(placing, scaled[:, None], 0.0), axis=0).astype(
            jnp.bfloat16
        )
        return (inputs, scales, normed, places, selector, keeping, weight_slots)

    def dispatch_rows(selector, source_rows):
        picked = jnp.dot(selector, source_rows, preferred_element_type=jnp.float32)
        return picked.astype(jnp.bfloat16).reshape(groups, capacity, feature_count)

    quad = lax.axis_size("ej")

    def weight_row(weight_slots):
        shaped = weight_slots.reshape(groups, 1, capacity)
        return jnp.pad(shaped, ((0, 0), (0, 0), (0, feature_count - capacity)))

    def across(block, s):
        return block if s == 0 else rotated(block, "eg", s)

    def around(block):
        return jnp.stack([block] + [flipped(block, "ej", t) for t in range(1, quad)])

    def run_block(rows_block, grads_block, weight_block):
        flat_rows = rows_block.reshape(-1, feature_count)
        flat_grads = grads_block.reshape(-1, feature_count)
        scale_column = weight_block.reshape(-1, 1).astype(jnp.float32)
        gate_value = contract_last(flat_rows, gate_full)
        upward = contract_last(flat_rows, up_full)
        backward = contract_last(flat_grads, down_full)
        active, derivative = silu_parts(gate_value)
        hidden = active * upward
        part_weight = jnp.sum(hidden * backward, axis=1).astype(jnp.bfloat16)
        grad_up = (scale_column * backward * active).astype(jnp.bfloat16)
        grad_gate = (scale_column * backward * upward * derivative).astype(jnp.bfloat16)
        grad_pair = jnp.concatenate([grad_gate, grad_up], axis=1)
        part_rows = jnp.dot(grad_pair, paired_weights, preferred_element_type=jnp.float32).astype(
            jnp.bfloat16
        )
        hidden_scaled = (hidden * scale_column).astype(jnp.bfloat16)
        return (grad_pair, hidden_scaled, flat_rows, flat_grads), part_rows, part_weight

    def send_back(part_rows, part_weight, s):
        quad_rows = part_rows.reshape(quad, capacity, feature_count)
        quad_weight = jnp.pad(
            part_weight.reshape(quad, 1, capacity), ((0, 0), (0, 0), (0, feature_count - capacity))
        )
        stacked = jnp.concatenate([quad_rows, quad_weight], axis=1)
        total = stacked[0].astype(jnp.float32)
        for t in range(1, quad):
            total = total + flipped(stacked[t], "ej", t).astype(jnp.float32)
        if s == 0:
            return total[:capacity], total[capacity, :capacity]
        high = total[capacity:].astype(jnp.bfloat16)
        low = (total[capacity:] - high.astype(jnp.float32)).astype(jnp.bfloat16)
        block = jnp.concatenate([total[:capacity].astype(jnp.bfloat16), high, low], axis=0)
        got = rotated(block, "eg", -s).astype(jnp.float32)
        return got[:capacity], got[capacity, :capacity] + got[capacity + 1, :capacity]

    prepared = [prepare(moment) for moment in range(micro_count)]
    first_incoming = jnp.where(is_last, output_grads[0], entry_grads[0])
    staged_rows = []
    for moment, current in enumerate(prepared):
        normed_slots = dispatch_rows(current[4], current[2])
        weight_rows = weight_row(current[6])
        pieces = [normed_slots]
        if moment == 0:
            pieces.append(dispatch_rows(current[4], first_incoming))
        pieces.append(weight_rows)
        payload = jnp.concatenate(pieces, axis=1)
        staged_rows.append([around(across(payload[s], s)) for s in range(groups)])
    leaving_list = []
    combine_list = []
    kept_list = []
    previous = entry_grads[0]
    for moment in range(micro_count):
        current = prepared[moment]
        if moment == 0:
            incoming = first_incoming
            grads_blocks = [staged[:, capacity : 2 * capacity] for staged in staged_rows[0]]
            weight_at = 2 * capacity
        else:
            arriving = shifted(previous, "pipe", -1)
            incoming = jnp.where(is_last, output_grads[moment], arriving)
            grads_slots = dispatch_rows(current[4], incoming)
            grads_blocks = [around(across(grads_slots[s], s)) for s in range(groups)]
            weight_at = capacity
        rows_parts = []
        weight_parts = []
        for s in range(groups):
            staged = staged_rows[moment][s]
            kept, part_rows, part_weight = run_block(
                staged[:, :capacity], grads_blocks[s], staged[:, weight_at, :capacity]
            )
            kept_list.append(kept)
            back_rows, back_weight = send_back(part_rows, part_weight, s)
            rows_parts.append(back_rows)
            weight_parts.append(back_weight)
        summed = jnp.stack(rows_parts).reshape(slot_count, feature_count)
        weight_sums = jnp.stack(weight_parts).reshape(slot_count)
        (
            finish_inputs,
            finish_scales,
            finish_normed,
            finish_places,
            finish_selector,
            finish_keeping,
            finish_weight_slots,
        ) = current
        expert_rows = jnp.sum(
            jnp.take(summed, finish_places, axis=0).reshape(token_rows, pick_count, feature_count),
            axis=1,
        )
        combine_grad = (
            jnp.take(weight_sums, finish_places) * finish_keeping.astype(jnp.float32)
        ).reshape(token_rows, pick_count)
        gained = gain_row * expert_rows
        mixed_mean = jnp.mean(finish_inputs * gained, axis=1, keepdims=True)
        leaving = (
            incoming.astype(jnp.float32)
            + finish_scales * gained
            - finish_inputs * (finish_scales * finish_scales * finish_scales) * mixed_mean
        ).astype(jnp.bfloat16)
        previous = leaving
        leaving_list.append(leaving)
        combine_list.append(combine_grad)
    pair_all = jnp.concatenate([kept[0] for kept in kept_list], axis=0)
    scaled_all = jnp.concatenate([kept[1] for kept in kept_list], axis=0)
    rows_all = jnp.concatenate([kept[2] for kept in kept_list], axis=0)
    grads_all = jnp.concatenate([kept[3] for kept in kept_list], axis=0)
    pair_total = contract_first(pair_all, rows_all).reshape(2, hidden_count, feature_count)
    down_total = contract_first(scaled_all, grads_all)[None]
    pair_reduced, down_reduced = (
        lax.psum_scatter(
            pair_total.astype(jnp.bfloat16), "dp", scatter_dimension=2, tiled=True
        ).astype(jnp.float32),
        lax.psum_scatter(
            down_total.astype(jnp.bfloat16), "dp", scatter_dimension=2, tiled=True
        ).astype(jnp.float32),
    )
    return (
        jnp.stack(leaving_list)[None],
        jnp.stack(combine_list)[None],
        pair_reduced[0:1].astype(jnp.bfloat16),
        pair_reduced[1:2].astype(jnp.bfloat16),
        down_reduced.astype(jnp.bfloat16),
    )


def solution(mesh):
    sizes = dict(zip(mesh.axis_names, mesh.devices.shape))
    members = sizes["expert"]
    grid = mesh.devices.reshape(sizes["pipe"], members // HSPLIT, HSPLIT, sizes["dp"])
    fine = Mesh(grid, ("pipe", "eg", "ej", "dp"))
    tokens = ("eg", "ej", "dp")
    rows = ("eg", "ej")
    in_specs = (
        P("pipe", None, tokens, None),
        P(None, tokens, None),
        P("pipe", tokens, None),
        P("pipe", None),
        P("pipe", None, tokens, None),
        P("pipe", None, tokens, None),
        P("pipe", None, tokens, None),
        P("pipe", rows, "dp"),
        P("pipe", rows, "dp"),
        P("pipe", rows, "dp"),
    )
    out_specs = (
        P("pipe", None, tokens, None),
        P("pipe", None, tokens, None),
        P("pipe", rows, "dp"),
        P("pipe", rows, "dp"),
        P("pipe", rows, "dp"),
    )
    return jax.shard_map(local, mesh=fine, in_specs=in_specs, out_specs=out_specs, check_vma=False)
```

```python
import jax
import jax.numpy as jnp
from jax import lax
from jax.sharding import Mesh, PartitionSpec as P

HSPLIT = 4


EPSILON = 1e-06


def shifted(block, axis, distance):
    devices = range(lax.axis_size(axis))
    route = [(i - distance, i) for i in devices if i - distance in devices]
    return lax.ppermute(block, axis, route)


def rotated(block, axis, distance):
    size = lax.axis_size(axis)
    route = [(i, (i + distance) % size) for i in range(size)]
    return lax.ppermute(block, axis, route)


def flipped(block, axis, mask):
    size = lax.axis_size(axis)
    route = [(i, i ^ mask) for i in range(size)]
    return lax.ppermute(block, axis, route)


def silu_parts(gate_value):
    sigmoid_value = jax.nn.sigmoid(gate_value)
    return (gate_value * sigmoid_value, sigmoid_value * (1.0 + gate_value * (1.0 - sigmoid_value)))


def contract_last(first_operand, second_operand):
    return lax.dot_general(
        first_operand, second_operand, (((1,), (1,)), ((), ())), preferred_element_type=jnp.float32
    )


def contract_first(first_operand, second_operand):
    return lax.dot_general(
        first_operand, second_operand, (((0,), (0,)), ((), ())), preferred_element_type=jnp.float32
    )


def local(
    saved_inputs,
    output_grads,
    entry_grads,
    norm_gain,
    expert_ids,
    keep_flags,
    combine_weights,
    gate_weight,
    up_weight,
    down_weight,
):
    sections = lax.axis_size("pipe")
    is_last = lax.axis_index("pipe") == sections - 1
    groups = lax.axis_size("eg")
    me = lax.axis_index("eg")
    micro_count = saved_inputs.shape[1]
    token_rows = saved_inputs.shape[2]
    feature_count = saved_inputs.shape[3]
    pick_count = expert_ids.shape[3]
    capacity = max(2, 3 * token_rows * pick_count // (2 * groups))
    slot_count = groups * capacity
    gate_full, up_full, down_full = (
        lax.all_gather(gate_weight[0], "dp", axis=1, tiled=True),
        lax.all_gather(up_weight[0], "dp", axis=1, tiled=True),
        lax.all_gather(down_weight[0], "dp", axis=1, tiled=True),
    )
    hidden_count = gate_full.shape[0]
    paired_weights = jnp.concatenate([gate_full, up_full], axis=0)
    gain_row = norm_gain[0][None, :]
    slot_ids = jnp.arange(slot_count, dtype=jnp.int32)
    expert_range = jnp.arange(groups, dtype=jnp.int32)

    def prepare(moment):
        inputs = saved_inputs[0, moment].astype(jnp.float32)
        scales = lax.rsqrt(jnp.mean(inputs * inputs, axis=1, keepdims=True) + EPSILON)
        normed = (inputs * scales * gain_row).astype(jnp.bfloat16)
        chosen = expert_ids[0, moment].reshape(-1)
        onehot = (chosen[:, None] == expert_range[None, :]).astype(jnp.int32)
        rank_values = jnp.sum((jnp.cumsum(onehot, axis=0) - 1) * onehot, axis=1)
        places = ((chosen - me) % groups) * capacity + rank_values
        placing = places[:, None] == slot_ids[None, :]
        token_map = jnp.any(placing.reshape(token_rows, pick_count, slot_count), axis=1)
        selector = token_map.T.astype(jnp.bfloat16)
        keeping = keep_flags[0, moment].reshape(-1)
        scaled = (combine_weights[0, moment].reshape(-1) * keeping.astype(jnp.bfloat16)).astype(
            jnp.float32
        )
        weight_slots = jnp.sum(jnp.where(placing, scaled[:, None], 0.0), axis=0).astype(
            jnp.bfloat16
        )
        return (inputs, scales, normed, places, selector, keeping, weight_slots)

    def dispatch_rows(selector, source_rows):
        picked = jnp.dot(selector, source_rows, preferred_element_type=jnp.float32)
        return picked.astype(jnp.bfloat16).reshape(groups, capacity, feature_count)

    quad = lax.axis_size("ej")

    def weight_row(weight_slots):
        shaped = weight_slots.reshape(groups, 1, capacity)
        return jnp.pad(shaped, ((0, 0), (0, 0), (0, feature_count - capacity)))

    def across(block, s):
        return block if s == 0 else rotated(block, "eg", s)

    def around(block):
        copies = jnp.broadcast_to(block[None], (quad,) + block.shape)
        return lax.all_to_all(copies, "ej", split_axis=0, concat_axis=0, tiled=True)

    def run_block(rows_block, grads_block, weight_block):
        flat_rows = rows_block.reshape(-1, feature_count)
        flat_grads = grads_block.reshape(-1, feature_count)
        scale_column = weight_block.reshape(-1, 1).astype(jnp.float32)
        gate_value = contract_last(flat_rows, gate_full)
        upward = contract_last(flat_rows, up_full)
        backward = contract_last(flat_grads, down_full)
        active, derivative = silu_parts(gate_value)
        hidden = active * upward
        part_weight = jnp.sum(hidden * backward, axis=1).astype(jnp.bfloat16)
        grad_up = (scale_column * backward * active).astype(jnp.bfloat16)
        grad_gate = (scale_column * backward * upward * derivative).astype(jnp.bfloat16)
        grad_pair = jnp.concatenate([grad_gate, grad_up], axis=1)
        part_rows = jnp.dot(grad_pair, paired_weights, preferred_element_type=jnp.float32).astype(
            jnp.bfloat16
        )
        hidden_scaled = (hidden * scale_column).astype(jnp.bfloat16)
        return (grad_pair, hidden_scaled, flat_rows, flat_grads), part_rows, part_weight

    def send_back(part_rows, part_weight, s):
        quad_rows = part_rows.reshape(quad, capacity, feature_count)
        quad_weight = jnp.pad(
            part_weight.reshape(quad, 1, capacity), ((0, 0), (0, 0), (0, feature_count - capacity))
        )
        stacked = jnp.concatenate([quad_rows, quad_weight], axis=1)
        returned = lax.all_to_all(stacked, "ej", split_axis=0, concat_axis=0, tiled=True)
        total = jnp.sum(returned.astype(jnp.float32), axis=0)
        if s == 0:
            return total[:capacity], total[capacity, :capacity]
        high = total[capacity:].astype(jnp.bfloat16)
        low = (total[capacity:] - high.astype(jnp.float32)).astype(jnp.bfloat16)
        block = jnp.concatenate([total[:capacity].astype(jnp.bfloat16), high, low], axis=0)
        got = rotated(block, "eg", -s).astype(jnp.float32)
        return got[:capacity], got[capacity, :capacity] + got[capacity + 1, :capacity]

    prepared = [prepare(moment) for moment in range(micro_count)]
    first_incoming = jnp.where(is_last, output_grads[0], entry_grads[0])
    staged_rows = []
    for moment, current in enumerate(prepared):
        normed_slots = dispatch_rows(current[4], current[2])
        weight_rows = weight_row(current[6])
        pieces = [normed_slots]
        if moment == 0:
            pieces.append(dispatch_rows(current[4], first_incoming))
        pieces.append(weight_rows)
        payload = jnp.concatenate(pieces, axis=1)
        staged_rows.append([around(across(payload[s], s)) for s in range(groups)])
    leaving_list = []
    combine_list = []
    kept_list = []
    previous = entry_grads[0]
    for moment in range(micro_count):
        current = prepared[moment]
        if moment == 0:
            incoming = first_incoming
            grads_blocks = [staged[:, capacity : 2 * capacity] for staged in staged_rows[0]]
            weight_at = 2 * capacity
        else:
            arriving = shifted(previous, "pipe", -1)
            incoming = jnp.where(is_last, output_grads[moment], arriving)
            grads_slots = dispatch_rows(current[4], incoming)
            grads_blocks = [around(across(grads_slots[s], s)) for s in range(groups)]
            weight_at = capacity
        rows_parts = []
        weight_parts = []
        for s in range(groups):
            staged = staged_rows[moment][s]
            kept, part_rows, part_weight = run_block(
                staged[:, :capacity], grads_blocks[s], staged[:, weight_at, :capacity]
            )
            kept_list.append(kept)
            back_rows, back_weight = send_back(part_rows, part_weight, s)
            rows_parts.append(back_rows)
            weight_parts.append(back_weight)
        summed = jnp.stack(rows_parts).reshape(slot_count, feature_count)
        weight_sums = jnp.stack(weight_parts).reshape(slot_count)
        (
            finish_inputs,
            finish_scales,
            finish_normed,
            finish_places,
            finish_selector,
            finish_keeping,
            finish_weight_slots,
        ) = current
        expert_rows = jnp.sum(
            jnp.take(summed, finish_places, axis=0).reshape(token_rows, pick_count, feature_count),
            axis=1,
        )
        combine_grad = (
            jnp.take(weight_sums, finish_places) * finish_keeping.astype(jnp.float32)
        ).reshape(token_rows, pick_count)
        gained = gain_row * expert_rows
        mixed_mean = jnp.mean(finish_inputs * gained, axis=1, keepdims=True)
        leaving = (
            incoming.astype(jnp.float32)
            + finish_scales * gained
            - finish_inputs * (finish_scales * finish_scales * finish_scales) * mixed_mean
        ).astype(jnp.bfloat16)
        previous = leaving
        leaving_list.append(leaving)
        combine_list.append(combine_grad)
    pair_all = jnp.concatenate([kept[0] for kept in kept_list], axis=0)
    scaled_all = jnp.concatenate([kept[1] for kept in kept_list], axis=0)
    rows_all = jnp.concatenate([kept[2] for kept in kept_list], axis=0)
    grads_all = jnp.concatenate([kept[3] for kept in kept_list], axis=0)
    pair_total = contract_first(pair_all, rows_all).reshape(2, hidden_count, feature_count)
    down_total = contract_first(scaled_all, grads_all)[None]
    pair_reduced, down_reduced = (
        lax.psum_scatter(
            pair_total.astype(jnp.bfloat16), "dp", scatter_dimension=2, tiled=True
        ).astype(jnp.float32),
        lax.psum_scatter(
            down_total.astype(jnp.bfloat16), "dp", scatter_dimension=2, tiled=True
        ).astype(jnp.float32),
    )
    return (
        jnp.stack(leaving_list)[None],
        jnp.stack(combine_list)[None],
        pair_reduced[0:1].astype(jnp.bfloat16),
        pair_reduced[1:2].astype(jnp.bfloat16),
        down_reduced.astype(jnp.bfloat16),
    )


def solution(mesh):
    sizes = dict(zip(mesh.axis_names, mesh.devices.shape))
    members = sizes["expert"]
    grid = mesh.devices.reshape(sizes["pipe"], members // HSPLIT, HSPLIT, sizes["dp"])
    fine = Mesh(grid, ("pipe", "eg", "ej", "dp"))
    tokens = ("eg", "ej", "dp")
    rows = ("eg", "ej")
    in_specs = (
        P("pipe", None, tokens, None),
        P(None, tokens, None),
        P("pipe", tokens, None),
        P("pipe", None),
        P("pipe", None, tokens, None),
        P("pipe", None, tokens, None),
        P("pipe", None, tokens, None),
        P("pipe", rows, "dp"),
        P("pipe", rows, "dp"),
        P("pipe", rows, "dp"),
    )
    out_specs = (
        P("pipe", None, tokens, None),
        P("pipe", None, tokens, None),
        P("pipe", rows, "dp"),
        P("pipe", rows, "dp"),
        P("pipe", rows, "dp"),
    )
    return jax.shard_map(local, mesh=fine, in_specs=in_specs, out_specs=out_specs, check_vma=False)
```

```python
import jax
import jax.numpy as jnp
from jax import lax
from jax.sharding import Mesh, PartitionSpec as P

HSPLIT = 4


EPSILON = 1e-06


def shifted(block, axis, distance):
    devices = range(lax.axis_size(axis))
    route = [(i - distance, i) for i in devices if i - distance in devices]
    return lax.ppermute(block, axis, route)


def rotated(block, axis, distance):
    size = lax.axis_size(axis)
    route = [(i, (i + distance) % size) for i in range(size)]
    return lax.ppermute(block, axis, route)


def flipped(block, axis, mask):
    size = lax.axis_size(axis)
    route = [(i, i ^ mask) for i in range(size)]
    return lax.ppermute(block, axis, route)


def silu_parts(gate_value):
    sigmoid_value = jax.nn.sigmoid(gate_value)
    return (gate_value * sigmoid_value, sigmoid_value * (1.0 + gate_value * (1.0 - sigmoid_value)))


def contract_last(first_operand, second_operand):
    return lax.dot_general(
        first_operand, second_operand, (((1,), (1,)), ((), ())), preferred_element_type=jnp.float32
    )


def contract_first(first_operand, second_operand):
    return lax.dot_general(
        first_operand, second_operand, (((0,), (0,)), ((), ())), preferred_element_type=jnp.float32
    )


def to_experts(blocks):
    groups = blocks.shape[0]
    moved = [blocks[0]] + [rotated(blocks[s], "eg", s) for s in range(1, groups)]
    return jnp.stack(moved)


def to_owners(blocks):
    groups = blocks.shape[0]
    moved = [blocks[0]] + [
        rotated(blocks[s].astype(jnp.bfloat16), "eg", -s).astype(jnp.float32)
        for s in range(1, groups)
    ]
    return jnp.stack(moved)


def weights_to_owners(blocks):
    groups = blocks.shape[0]
    moved = [blocks[0]] + [rotated(blocks[s], "eg", -s) for s in range(1, groups)]
    return jnp.stack(moved)


def relayed(block):
    width = block.shape[-1]
    return lax.axis_size("ej") == 4 and width >= 256 and width % 256 == 0


def gather_quad(blocks):
    staged = to_experts(blocks)
    quad = lax.axis_size("ej")
    if not relayed(staged):
        return jnp.stack([staged] + [flipped(staged, "ej", t) for t in range(1, quad)])
    half = staged.shape[-1] // 2
    first = flipped(staged, "ej", 1)
    second = flipped(staged, "ej", 2)
    diagonal = jnp.concatenate(
        [flipped(first[..., :half], "ej", 2), flipped(second[..., half:], "ej", 1)], axis=-1
    )
    return jnp.stack([staged, first, second, diagonal])


def reduce_quad(parts):
    quad = parts.shape[0]
    total = parts[0].astype(jnp.float32)
    if not relayed(parts):
        for t in range(1, quad):
            total = total + flipped(parts[t], "ej", t).astype(jnp.float32)
        return total
    half = parts.shape[-1] // 2
    from_first = flipped(parts[3][..., :half], "ej", 1).astype(jnp.float32)
    from_second = flipped(parts[3][..., half:], "ej", 2).astype(jnp.float32)
    toward_second = jnp.concatenate(
        [(parts[2][..., :half].astype(jnp.float32) + from_first).astype(parts.dtype), parts[2][..., half:]],
        axis=-1,
    )
    toward_first = jnp.concatenate(
        [parts[1][..., :half], (parts[1][..., half:].astype(jnp.float32) + from_second).astype(parts.dtype)],
        axis=-1,
    )
    total = total + flipped(toward_second, "ej", 2).astype(jnp.float32)
    return total + flipped(toward_first, "ej", 1).astype(jnp.float32)


def local(
    saved_inputs,
    output_grads,
    entry_grads,
    norm_gain,
    expert_ids,
    keep_flags,
    combine_weights,
    gate_weight,
    up_weight,
    down_weight,
):
    sections = lax.axis_size("pipe")
    is_last = lax.axis_index("pipe") == sections - 1
    groups = lax.axis_size("eg")
    me = lax.axis_index("eg")
    micro_count = saved_inputs.shape[1]
    token_rows = saved_inputs.shape[2]
    feature_count = saved_inputs.shape[3]
    pick_count = expert_ids.shape[3]
    capacity = max(2, 3 * token_rows * pick_count // (2 * groups))
    slot_count = groups * capacity
    low_half = lax.axis_index("dp") == 0

    def whole_rows(stored):
        if lax.axis_size("dp") != 2:
            return lax.all_gather(stored, "dp", axis=1, tiled=True)
        partner = flipped(stored, "dp", 1)
        return jnp.where(
            low_half,
            jnp.concatenate([stored, partner], axis=1),
            jnp.concatenate([partner, stored], axis=1),
        )

    gate_full, up_full, down_full = (
        whole_rows(gate_weight[0]),
        whole_rows(up_weight[0]),
        whole_rows(down_weight[0]),
    )
    hidden_count = gate_full.shape[0]
    paired_weights = jnp.concatenate([gate_full, up_full], axis=0)
    gain_row = norm_gain[0][None, :]
    slot_ids = jnp.arange(slot_count, dtype=jnp.int32)
    expert_range = jnp.arange(groups, dtype=jnp.int32)

    def prepare(moment):
        inputs = saved_inputs[0, moment].astype(jnp.float32)
        scales = lax.rsqrt(jnp.mean(inputs * inputs, axis=1, keepdims=True) + EPSILON)
        normed = (inputs * scales * gain_row).astype(jnp.bfloat16)
        chosen = expert_ids[0, moment].reshape(-1)
        onehot = (chosen[:, None] == expert_range[None, :]).astype(jnp.int32)
        rank_values = jnp.sum((jnp.cumsum(onehot, axis=0) - 1) * onehot, axis=1)
        places = ((chosen - me) % groups) * capacity + rank_values
        placing = places[:, None] == slot_ids[None, :]
        token_map = jnp.any(placing.reshape(token_rows, pick_count, slot_count), axis=1)
        selector = token_map.T.astype(jnp.bfloat16)
        keeping = keep_flags[0, moment].reshape(-1)
        scaled = (combine_weights[0, moment].reshape(-1) * keeping.astype(jnp.bfloat16)).astype(
            jnp.float32
        )
        weight_slots = jnp.sum(jnp.where(placing, scaled[:, None], 0.0), axis=0).astype(
            jnp.bfloat16
        )
        return (inputs, scales, normed, places, selector, keeping, weight_slots)

    def dispatch_rows(selector, source_rows):
        picked = jnp.dot(selector, source_rows, preferred_element_type=jnp.float32)
        return picked.astype(jnp.bfloat16).reshape(groups, capacity, feature_count)

    prepared = [prepare(moment) for moment in range(micro_count)]
    rows_gathered = [
        gather_quad(dispatch_rows(current[4], current[2])) for current in prepared
    ]
    weights_gathered = [
        gather_quad(current[6].reshape(groups, capacity)) for current in prepared
    ]
    leaving_list = []
    combine_list = []
    kept_list = []
    previous = entry_grads[0]
    for moment in range(micro_count):
        current = prepared[moment]
        if moment == 0:
            arriving = entry_grads[0]
        else:
            arriving = shifted(previous, "pipe", -1)
        incoming = jnp.where(is_last, output_grads[moment], arriving)
        grads_in = gather_quad(dispatch_rows(current[4], incoming))
        flat_rows = rows_gathered[moment].reshape(-1, feature_count)
        flat_grads = grads_in.reshape(-1, feature_count)
        scale_column = weights_gathered[moment].reshape(-1, 1).astype(jnp.float32)
        gate_value = contract_last(flat_rows, gate_full)
        upward = contract_last(flat_rows, up_full)
        backward = contract_last(flat_grads, down_full)
        active, derivative = silu_parts(gate_value)
        hidden = active * upward
        part_weight = jnp.sum(hidden * backward, axis=1).astype(jnp.bfloat16)
        grad_up = (scale_column * backward * active).astype(jnp.bfloat16)
        grad_gate = (scale_column * backward * upward * derivative).astype(jnp.bfloat16)
        grad_pair = jnp.concatenate([grad_gate, grad_up], axis=1)
        part_rows = jnp.dot(grad_pair, paired_weights, preferred_element_type=jnp.float32).astype(
            jnp.bfloat16
        )
        hidden_scaled = (hidden * scale_column).astype(jnp.bfloat16)
        kept_list.append((grad_pair, hidden_scaled, flat_rows, flat_grads))
        rows_back = to_owners(
            reduce_quad(part_rows.reshape(-1, groups, capacity, feature_count))
        )
        weights_back = weights_to_owners(
            reduce_quad(part_weight.reshape(-1, groups, capacity))
        )
        (
            finish_inputs,
            finish_scales,
            finish_normed,
            finish_places,
            finish_selector,
            finish_keeping,
            finish_weight_slots,
        ) = current
        summed = rows_back.reshape(slot_count, feature_count)
        weight_sums = weights_back.reshape(slot_count)
        expert_rows = jnp.sum(
            jnp.take(summed, finish_places, axis=0).reshape(token_rows, pick_count, feature_count),
            axis=1,
        )
        combine_grad = (
            jnp.take(weight_sums, finish_places) * finish_keeping.astype(jnp.float32)
        ).reshape(token_rows, pick_count)
        gained = gain_row * expert_rows
        mixed_mean = jnp.mean(finish_inputs * gained, axis=1, keepdims=True)
        leaving = (
            incoming.astype(jnp.float32)
            + finish_scales * gained
            - finish_inputs * (finish_scales * finish_scales * finish_scales) * mixed_mean
        ).astype(jnp.bfloat16)
        previous = leaving
        leaving_list.append(leaving)
        combine_list.append(combine_grad)
    pair_all = jnp.concatenate([kept[0] for kept in kept_list], axis=0)
    scaled_all = jnp.concatenate([kept[1] for kept in kept_list], axis=0)
    rows_all = jnp.concatenate([kept[2] for kept in kept_list], axis=0)
    grads_all = jnp.concatenate([kept[3] for kept in kept_list], axis=0)
    pair_total = contract_first(pair_all, rows_all).reshape(2, hidden_count, feature_count)
    down_total = contract_first(scaled_all, grads_all)[None]
    pair_reduced, down_reduced = (
        lax.psum_scatter(
            pair_total.astype(jnp.bfloat16), "dp", scatter_dimension=2, tiled=True
        ).astype(jnp.float32),
        lax.psum_scatter(
            down_total.astype(jnp.bfloat16), "dp", scatter_dimension=2, tiled=True
        ).astype(jnp.float32),
    )
    return (
        jnp.stack(leaving_list)[None],
        jnp.stack(combine_list)[None],
        pair_reduced[0:1].astype(jnp.bfloat16),
        pair_reduced[1:2].astype(jnp.bfloat16),
        down_reduced.astype(jnp.bfloat16),
    )


def solution(mesh):
    sizes = dict(zip(mesh.axis_names, mesh.devices.shape))
    members = sizes["expert"]
    grid = mesh.devices.reshape(sizes["pipe"], members // HSPLIT, HSPLIT, sizes["dp"])
    fine = Mesh(grid, ("pipe", "eg", "ej", "dp"))
    tokens = ("eg", "ej", "dp")
    rows = ("eg", "ej")
    in_specs = (
        P("pipe", None, tokens, None),
        P(None, tokens, None),
        P("pipe", tokens, None),
        P("pipe", None),
        P("pipe", None, tokens, None),
        P("pipe", None, tokens, None),
        P("pipe", None, tokens, None),
        P("pipe", rows, "dp"),
        P("pipe", rows, "dp"),
        P("pipe", rows, "dp"),
    )
    out_specs = (
        P("pipe", None, tokens, None),
        P("pipe", None, tokens, None),
        P("pipe", rows, "dp"),
        P("pipe", rows, "dp"),
        P("pipe", rows, "dp"),
    )
    return jax.shard_map(local, mesh=fine, in_specs=in_specs, out_specs=out_specs, check_vma=False)
```

```python
import jax
import jax.numpy as jnp
from jax import lax
from jax.sharding import Mesh, PartitionSpec as P

HSPLIT = 4


EPSILON = 1e-06


def shifted(block, axis, distance):
    devices = range(lax.axis_size(axis))
    route = [(i - distance, i) for i in devices if i - distance in devices]
    return lax.ppermute(block, axis, route)


def rotated(block, axis, distance):
    size = lax.axis_size(axis)
    route = [(i, (i + distance) % size) for i in range(size)]
    return lax.ppermute(block, axis, route)


def flipped(block, axis, mask):
    size = lax.axis_size(axis)
    route = [(i, i ^ mask) for i in range(size)]
    return lax.ppermute(block, axis, route)


def silu_parts(gate_value):
    sigmoid_value = jax.nn.sigmoid(gate_value)
    return (gate_value * sigmoid_value, sigmoid_value * (1.0 + gate_value * (1.0 - sigmoid_value)))


def contract_last(first_operand, second_operand):
    return lax.dot_general(
        first_operand, second_operand, (((1,), (1,)), ((), ())), preferred_element_type=jnp.float32
    )


def contract_first(first_operand, second_operand):
    return lax.dot_general(
        first_operand, second_operand, (((0,), (0,)), ((), ())), preferred_element_type=jnp.float32
    )


def to_experts(blocks):
    groups = blocks.shape[0]
    moved = [blocks[0]] + [rotated(blocks[s], "eg", s) for s in range(1, groups)]
    return jnp.stack(moved)


def relayed(block):
    width = block.shape[-1]
    return lax.axis_size("ej") == 4 and width >= 256 and width % 256 == 0


def gather_quad(blocks):
    staged = to_experts(blocks)
    quad = lax.axis_size("ej")
    if not relayed(staged):
        return jnp.stack([staged] + [flipped(staged, "ej", t) for t in range(1, quad)])
    half = staged.shape[-1] // 2
    first = flipped(staged, "ej", 1)
    second = flipped(staged, "ej", 2)
    diagonal = jnp.concatenate(
        [flipped(first[..., :half], "ej", 2), flipped(second[..., half:], "ej", 1)], axis=-1
    )
    return jnp.stack([staged, first, second, diagonal])


def reduce_quad(parts):
    quad = parts.shape[0]
    total = parts[0].astype(jnp.float32)
    if not relayed(parts):
        for t in range(1, quad):
            total = total + flipped(parts[t], "ej", t).astype(jnp.float32)
        return total
    half = parts.shape[-1] // 2
    from_first = flipped(parts[3][..., :half], "ej", 1).astype(jnp.float32)
    from_second = flipped(parts[3][..., half:], "ej", 2).astype(jnp.float32)
    toward_second = jnp.concatenate(
        [(parts[2][..., :half].astype(jnp.float32) + from_first).astype(parts.dtype), parts[2][..., half:]],
        axis=-1,
    )
    toward_first = jnp.concatenate(
        [parts[1][..., :half], (parts[1][..., half:].astype(jnp.float32) + from_second).astype(parts.dtype)],
        axis=-1,
    )
    total = total + flipped(toward_second, "ej", 2).astype(jnp.float32)
    return total + flipped(toward_first, "ej", 1).astype(jnp.float32)


def local(
    saved_inputs,
    output_grads,
    entry_grads,
    norm_gain,
    expert_ids,
    keep_flags,
    combine_weights,
    gate_weight,
    up_weight,
    down_weight,
):
    sections = lax.axis_size("pipe")
    is_last = lax.axis_index("pipe") == sections - 1
    groups = lax.axis_size("eg")
    me = lax.axis_index("eg")
    micro_count = saved_inputs.shape[1]
    token_rows = saved_inputs.shape[2]
    feature_count = saved_inputs.shape[3]
    pick_count = expert_ids.shape[3]
    capacity = max(2, 3 * token_rows * pick_count // (2 * groups))
    slot_count = groups * capacity
    low_half = lax.axis_index("dp") == 0

    stored = jnp.stack([gate_weight[0], up_weight[0], down_weight[0]])
    if lax.axis_size("dp") == 2:
        partner = flipped(stored, "dp", 1)
        whole = jnp.where(
            low_half,
            jnp.concatenate([stored, partner], axis=2),
            jnp.concatenate([partner, stored], axis=2),
        )
    else:
        whole = lax.all_gather(stored, "dp", axis=2, tiled=True)
    gate_full, up_full, down_full = whole[0], whole[1], whole[2]
    hidden_count = gate_full.shape[0]
    paired_weights = jnp.concatenate([gate_full, up_full], axis=0)
    gain_row = norm_gain[0][None, :]
    slot_ids = jnp.arange(slot_count, dtype=jnp.int32)
    expert_range = jnp.arange(groups, dtype=jnp.int32)

    def prepare(moment):
        inputs = saved_inputs[0, moment].astype(jnp.float32)
        scales = lax.rsqrt(jnp.mean(inputs * inputs, axis=1, keepdims=True) + EPSILON)
        normed = (inputs * scales * gain_row).astype(jnp.bfloat16)
        chosen = expert_ids[0, moment].reshape(-1)
        onehot = (chosen[:, None] == expert_range[None, :]).astype(jnp.int32)
        rank_values = jnp.sum((jnp.cumsum(onehot, axis=0) - 1) * onehot, axis=1)
        places = ((chosen - me) % groups) * capacity + rank_values
        placing = places[:, None] == slot_ids[None, :]
        token_map = jnp.any(placing.reshape(token_rows, pick_count, slot_count), axis=1)
        selector = token_map.T.astype(jnp.bfloat16)
        keeping = keep_flags[0, moment].reshape(-1)
        scaled = (combine_weights[0, moment].reshape(-1) * keeping.astype(jnp.bfloat16)).astype(
            jnp.float32
        )
        weight_slots = jnp.sum(jnp.where(placing, scaled[:, None], 0.0), axis=0).astype(
            jnp.bfloat16
        )
        return (inputs, scales, normed, places, selector, keeping, weight_slots)

    def dispatch_rows(selector, source_rows):
        picked = jnp.dot(selector, source_rows, preferred_element_type=jnp.float32)
        return picked.astype(jnp.bfloat16).reshape(groups, capacity, feature_count)

    def padded_row(values):
        shaped = values[..., None, :]
        width = [(0, 0)] * (shaped.ndim - 1) + [(0, feature_count - capacity)]
        return jnp.pad(shaped, width)

    def send_back(part_rows, part_weight):
        stacked = jnp.concatenate(
            [
                part_rows.reshape(-1, groups, capacity, feature_count),
                padded_row(part_weight.reshape(-1, groups, capacity)),
            ],
            axis=2,
        )
        total = reduce_quad(stacked)
        back_rows = [total[0, :capacity]]
        back_weight = [total[0, capacity, :capacity]]
        for s in range(1, groups):
            high = total[s, capacity:].astype(jnp.bfloat16)
            low = (total[s, capacity:] - high.astype(jnp.float32)).astype(jnp.bfloat16)
            block = jnp.concatenate([total[s, :capacity].astype(jnp.bfloat16), high, low], axis=0)
            got = rotated(block, "eg", -s).astype(jnp.float32)
            back_rows.append(got[:capacity])
            back_weight.append(got[capacity, :capacity] + got[capacity + 1, :capacity])
        return (
            jnp.stack(back_rows).reshape(slot_count, feature_count),
            jnp.stack(back_weight).reshape(slot_count),
        )

    prepared = [prepare(moment) for moment in range(micro_count)]
    packed_gathered = [
        gather_quad(
            jnp.concatenate(
                [
                    dispatch_rows(current[4], current[2]),
                    padded_row(current[6].reshape(groups, capacity)),
                ],
                axis=1,
            )
        )
        for current in prepared
    ]
    leaving_list = []
    combine_list = []
    kept_list = []
    previous = entry_grads[0]
    for moment in range(micro_count):
        current = prepared[moment]
        if moment == 0:
            arriving = entry_grads[0]
        else:
            arriving = shifted(previous, "pipe", -1)
        incoming = jnp.where(is_last, output_grads[moment], arriving)
        grads_in = gather_quad(dispatch_rows(current[4], incoming))
        packed = packed_gathered[moment]
        flat_rows = packed[:, :, :capacity].reshape(-1, feature_count)
        flat_grads = grads_in.reshape(-1, feature_count)
        scale_column = packed[:, :, capacity, :capacity].reshape(-1, 1).astype(jnp.float32)
        gate_value = contract_last(flat_rows, gate_full)
        upward = contract_last(flat_rows, up_full)
        backward = contract_last(flat_grads, down_full)
        active, derivative = silu_parts(gate_value)
        hidden = active * upward
        part_weight = jnp.sum(hidden * backward, axis=1).astype(jnp.bfloat16)
        grad_up = (scale_column * backward * active).astype(jnp.bfloat16)
        grad_gate = (scale_column * backward * upward * derivative).astype(jnp.bfloat16)
        grad_pair = jnp.concatenate([grad_gate, grad_up], axis=1)
        part_rows = jnp.dot(grad_pair, paired_weights, preferred_element_type=jnp.float32).astype(
            jnp.bfloat16
        )
        hidden_scaled = (hidden * scale_column).astype(jnp.bfloat16)
        kept_list.append((grad_pair, hidden_scaled, flat_rows, flat_grads))
        summed, weight_sums = send_back(part_rows, part_weight)
        (
            finish_inputs,
            finish_scales,
            finish_normed,
            finish_places,
            finish_selector,
            finish_keeping,
            finish_weight_slots,
        ) = current
        expert_rows = jnp.sum(
            jnp.take(summed, finish_places, axis=0).reshape(token_rows, pick_count, feature_count),
            axis=1,
        )
        combine_grad = (
            jnp.take(weight_sums, finish_places) * finish_keeping.astype(jnp.float32)
        ).reshape(token_rows, pick_count)
        gained = gain_row * expert_rows
        mixed_mean = jnp.mean(finish_inputs * gained, axis=1, keepdims=True)
        leaving = (
            incoming.astype(jnp.float32)
            + finish_scales * gained
            - finish_inputs * (finish_scales * finish_scales * finish_scales) * mixed_mean
        ).astype(jnp.bfloat16)
        previous = leaving
        leaving_list.append(leaving)
        combine_list.append(combine_grad)
    pair_all = jnp.concatenate([kept[0] for kept in kept_list], axis=0)
    scaled_all = jnp.concatenate([kept[1] for kept in kept_list], axis=0)
    rows_all = jnp.concatenate([kept[2] for kept in kept_list], axis=0)
    grads_all = jnp.concatenate([kept[3] for kept in kept_list], axis=0)
    pair_total = contract_first(pair_all, rows_all).reshape(2, hidden_count, feature_count)
    down_total = contract_first(scaled_all, grads_all)[None]
    pair_reduced, down_reduced = (
        lax.psum_scatter(
            pair_total.astype(jnp.bfloat16), "dp", scatter_dimension=2, tiled=True
        ).astype(jnp.float32),
        lax.psum_scatter(
            down_total.astype(jnp.bfloat16), "dp", scatter_dimension=2, tiled=True
        ).astype(jnp.float32),
    )
    return (
        jnp.stack(leaving_list)[None],
        jnp.stack(combine_list)[None],
        pair_reduced[0:1].astype(jnp.bfloat16),
        pair_reduced[1:2].astype(jnp.bfloat16),
        down_reduced.astype(jnp.bfloat16),
    )


def solution(mesh):
    sizes = dict(zip(mesh.axis_names, mesh.devices.shape))
    members = sizes["expert"]
    grid = mesh.devices.reshape(sizes["pipe"], members // HSPLIT, HSPLIT, sizes["dp"])
    fine = Mesh(grid, ("pipe", "eg", "ej", "dp"))
    tokens = ("eg", "ej", "dp")
    rows = ("eg", "ej")
    in_specs = (
        P("pipe", None, tokens, None),
        P(None, tokens, None),
        P("pipe", tokens, None),
        P("pipe", None),
        P("pipe", None, tokens, None),
        P("pipe", None, tokens, None),
        P("pipe", None, tokens, None),
        P("pipe", rows, "dp"),
        P("pipe", rows, "dp"),
        P("pipe", rows, "dp"),
    )
    out_specs = (
        P("pipe", None, tokens, None),
        P("pipe", None, tokens, None),
        P("pipe", rows, "dp"),
        P("pipe", rows, "dp"),
        P("pipe", rows, "dp"),
    )
    return jax.shard_map(local, mesh=fine, in_specs=in_specs, out_specs=out_specs, check_vma=False)
```

```python
import jax
import jax.numpy as jnp
from jax import lax
from jax.sharding import Mesh, PartitionSpec as P

HSPLIT = 4


EPSILON = 1e-06


def shifted(block, axis, distance):
    devices = range(lax.axis_size(axis))
    route = [(i - distance, i) for i in devices if i - distance in devices]
    return lax.ppermute(block, axis, route)


def rotated(block, axis, distance):
    size = lax.axis_size(axis)
    route = [(i, (i + distance) % size) for i in range(size)]
    return lax.ppermute(block, axis, route)


def flipped(block, axis, mask):
    size = lax.axis_size(axis)
    route = [(i, i ^ mask) for i in range(size)]
    return lax.ppermute(block, axis, route)


def silu_parts(gate_value):
    sigmoid_value = jax.nn.sigmoid(gate_value)
    return (gate_value * sigmoid_value, sigmoid_value * (1.0 + gate_value * (1.0 - sigmoid_value)))


def contract_last(first_operand, second_operand):
    return lax.dot_general(
        first_operand, second_operand, (((1,), (1,)), ((), ())), preferred_element_type=jnp.float32
    )


def contract_first(first_operand, second_operand):
    return lax.dot_general(
        first_operand, second_operand, (((0,), (0,)), ((), ())), preferred_element_type=jnp.float32
    )


def relayed(block):
    width = block.shape[-1]
    return lax.axis_size("ej") == 4 and width >= 256 and width % 256 == 0


def gather_quad(staged):
    quad = lax.axis_size("ej")
    if not relayed(staged):
        return jnp.stack([staged] + [flipped(staged, "ej", t) for t in range(1, quad)])
    half = staged.shape[-1] // 2
    first = flipped(staged, "ej", 1)
    second = flipped(staged, "ej", 2)
    diagonal = jnp.concatenate(
        [flipped(first[..., :half], "ej", 2), flipped(second[..., half:], "ej", 1)], axis=-1
    )
    return jnp.stack([staged, first, second, diagonal])


def reduce_quad(parts):
    quad = parts.shape[0]
    total = parts[0].astype(jnp.float32)
    if not relayed(parts):
        for t in range(1, quad):
            total = total + flipped(parts[t], "ej", t).astype(jnp.float32)
        return total
    half = parts.shape[-1] // 2
    from_first = flipped(parts[3][..., :half], "ej", 1).astype(jnp.float32)
    from_second = flipped(parts[3][..., half:], "ej", 2).astype(jnp.float32)
    toward_second = jnp.concatenate(
        [(parts[2][..., :half].astype(jnp.float32) + from_first).astype(parts.dtype), parts[2][..., half:]],
        axis=-1,
    )
    toward_first = jnp.concatenate(
        [parts[1][..., :half], (parts[1][..., half:].astype(jnp.float32) + from_second).astype(parts.dtype)],
        axis=-1,
    )
    total = total + flipped(toward_second, "ej", 2).astype(jnp.float32)
    return total + flipped(toward_first, "ej", 1).astype(jnp.float32)


def local(
    saved_inputs,
    output_grads,
    entry_grads,
    norm_gain,
    expert_ids,
    keep_flags,
    combine_weights,
    gate_weight,
    up_weight,
    down_weight,
):
    sections = lax.axis_size("pipe")
    is_last = lax.axis_index("pipe") == sections - 1
    groups = lax.axis_size("eg")
    me = lax.axis_index("eg")
    micro_count = saved_inputs.shape[1]
    token_rows = saved_inputs.shape[2]
    feature_count = saved_inputs.shape[3]
    pick_count = expert_ids.shape[3]
    capacity = max(2, 3 * token_rows * pick_count // (2 * groups))
    slot_count = groups * capacity
    low_half = lax.axis_index("dp") == 0

    def whole_rows(stored):
        if lax.axis_size("dp") != 2:
            return lax.all_gather(stored, "dp", axis=1, tiled=True)
        partner = flipped(stored, "dp", 1)
        return jnp.where(
            low_half,
            jnp.concatenate([stored, partner], axis=1),
            jnp.concatenate([partner, stored], axis=1),
        )

    gate_full, up_full, down_full = (
        whole_rows(gate_weight[0]),
        whole_rows(up_weight[0]),
        whole_rows(down_weight[0]),
    )
    hidden_count = gate_full.shape[0]
    paired_weights = jnp.concatenate([gate_full, up_full], axis=0)
    gain_row = norm_gain[0][None, :]
    slot_ids = jnp.arange(slot_count, dtype=jnp.int32)
    expert_range = jnp.arange(groups, dtype=jnp.int32)

    def prepare(moment):
        inputs = saved_inputs[0, moment].astype(jnp.float32)
        scales = lax.rsqrt(jnp.mean(inputs * inputs, axis=1, keepdims=True) + EPSILON)
        normed = (inputs * scales * gain_row).astype(jnp.bfloat16)
        chosen = expert_ids[0, moment].reshape(-1)
        onehot = (chosen[:, None] == expert_range[None, :]).astype(jnp.int32)
        rank_values = jnp.sum((jnp.cumsum(onehot, axis=0) - 1) * onehot, axis=1)
        places = ((chosen - me) % groups) * capacity + rank_values
        placing = places[:, None] == slot_ids[None, :]
        token_map = jnp.any(placing.reshape(token_rows, pick_count, slot_count), axis=1)
        selector = token_map.T.astype(jnp.bfloat16)
        keeping = keep_flags[0, moment].reshape(-1)
        scaled = (combine_weights[0, moment].reshape(-1) * keeping.astype(jnp.bfloat16)).astype(
            jnp.float32
        )
        weight_slots = jnp.sum(jnp.where(placing, scaled[:, None], 0.0), axis=0).astype(
            jnp.bfloat16
        )
        return (inputs, scales, normed, places, selector, keeping, weight_slots)

    def dispatch_rows(selector, source_rows):
        picked = jnp.dot(selector, source_rows, preferred_element_type=jnp.float32)
        return picked.astype(jnp.bfloat16).reshape(groups, capacity, feature_count)

    quad = lax.axis_size("ej")

    def weight_row(weight_slots):
        shaped = weight_slots.reshape(groups, 1, capacity)
        return jnp.pad(shaped, ((0, 0), (0, 0), (0, feature_count - capacity)))

    def across(block, s):
        return block if s == 0 else rotated(block, "eg", s)

    def around(block):
        return gather_quad(block)

    def run_block(rows_block, grads_block, weight_block):
        flat_rows = rows_block.reshape(-1, feature_count)
        flat_grads = grads_block.reshape(-1, feature_count)
        scale_column = weight_block.reshape(-1, 1).astype(jnp.float32)
        gate_value = contract_last(flat_rows, gate_full)
        upward = contract_last(flat_rows, up_full)
        backward = contract_last(flat_grads, down_full)
        active, derivative = silu_parts(gate_value)
        hidden = active * upward
        part_weight = jnp.sum(hidden * backward, axis=1).astype(jnp.bfloat16)
        grad_up = (scale_column * backward * active).astype(jnp.bfloat16)
        grad_gate = (scale_column * backward * upward * derivative).astype(jnp.bfloat16)
        grad_pair = jnp.concatenate([grad_gate, grad_up], axis=1)
        part_rows = jnp.dot(grad_pair, paired_weights, preferred_element_type=jnp.float32).astype(
            jnp.bfloat16
        )
        hidden_scaled = (hidden * scale_column).astype(jnp.bfloat16)
        return (grad_pair, hidden_scaled, flat_rows, flat_grads), part_rows, part_weight

    def send_back(part_rows, part_weight, s):
        quad_rows = part_rows.reshape(quad, capacity, feature_count)
        quad_weight = jnp.pad(
            part_weight.reshape(quad, 1, capacity), ((0, 0), (0, 0), (0, feature_count - capacity))
        )
        total = reduce_quad(jnp.concatenate([quad_rows, quad_weight], axis=1))
        if s == 0:
            return total[:capacity], total[capacity, :capacity]
        high = total[capacity:].astype(jnp.bfloat16)
        low = (total[capacity:] - high.astype(jnp.float32)).astype(jnp.bfloat16)
        block = jnp.concatenate([total[:capacity].astype(jnp.bfloat16), high, low], axis=0)
        got = rotated(block, "eg", -s).astype(jnp.float32)
        return got[:capacity], got[capacity, :capacity] + got[capacity + 1, :capacity]

    prepared = [prepare(moment) for moment in range(micro_count)]
    first_incoming = jnp.where(is_last, output_grads[0], entry_grads[0])
    staged_rows = []
    for moment, current in enumerate(prepared):
        normed_slots = dispatch_rows(current[4], current[2])
        weight_rows = weight_row(current[6])
        pieces = [normed_slots]
        if moment == 0:
            pieces.append(dispatch_rows(current[4], first_incoming))
        pieces.append(weight_rows)
        payload = jnp.concatenate(pieces, axis=1)
        staged_rows.append([around(across(payload[s], s)) for s in range(groups)])
    leaving_list = []
    combine_list = []
    kept_list = []
    previous = entry_grads[0]
    for moment in range(micro_count):
        current = prepared[moment]
        if moment == 0:
            incoming = first_incoming
            grads_blocks = [staged[:, capacity : 2 * capacity] for staged in staged_rows[0]]
            weight_at = 2 * capacity
        else:
            arriving = shifted(previous, "pipe", -1)
            incoming = jnp.where(is_last, output_grads[moment], arriving)
            grads_slots = dispatch_rows(current[4], incoming)
            grads_blocks = [around(across(grads_slots[s], s)) for s in range(groups)]
            weight_at = capacity
        rows_parts = []
        weight_parts = []
        for s in range(groups):
            staged = staged_rows[moment][s]
            kept, part_rows, part_weight = run_block(
                staged[:, :capacity], grads_blocks[s], staged[:, weight_at, :capacity]
            )
            kept_list.append(kept)
            back_rows, back_weight = send_back(part_rows, part_weight, s)
            rows_parts.append(back_rows)
            weight_parts.append(back_weight)
        summed = jnp.stack(rows_parts).reshape(slot_count, feature_count)
        weight_sums = jnp.stack(weight_parts).reshape(slot_count)
        (
            finish_inputs,
            finish_scales,
            finish_normed,
            finish_places,
            finish_selector,
            finish_keeping,
            finish_weight_slots,
        ) = current
        expert_rows = jnp.sum(
            jnp.take(summed, finish_places, axis=0).reshape(token_rows, pick_count, feature_count),
            axis=1,
        )
        combine_grad = (
            jnp.take(weight_sums, finish_places) * finish_keeping.astype(jnp.float32)
        ).reshape(token_rows, pick_count)
        gained = gain_row * expert_rows
        mixed_mean = jnp.mean(finish_inputs * gained, axis=1, keepdims=True)
        leaving = (
            incoming.astype(jnp.float32)
            + finish_scales * gained
            - finish_inputs * (finish_scales * finish_scales * finish_scales) * mixed_mean
        ).astype(jnp.bfloat16)
        previous = leaving
        leaving_list.append(leaving)
        combine_list.append(combine_grad)
    pair_all = jnp.concatenate([kept[0] for kept in kept_list], axis=0)
    scaled_all = jnp.concatenate([kept[1] for kept in kept_list], axis=0)
    rows_all = jnp.concatenate([kept[2] for kept in kept_list], axis=0)
    grads_all = jnp.concatenate([kept[3] for kept in kept_list], axis=0)
    pair_total = contract_first(pair_all, rows_all).reshape(2, hidden_count, feature_count)
    down_total = contract_first(scaled_all, grads_all)[None]
    pair_reduced, down_reduced = (
        lax.psum_scatter(
            pair_total.astype(jnp.bfloat16), "dp", scatter_dimension=2, tiled=True
        ).astype(jnp.float32),
        lax.psum_scatter(
            down_total.astype(jnp.bfloat16), "dp", scatter_dimension=2, tiled=True
        ).astype(jnp.float32),
    )
    return (
        jnp.stack(leaving_list)[None],
        jnp.stack(combine_list)[None],
        pair_reduced[0:1].astype(jnp.bfloat16),
        pair_reduced[1:2].astype(jnp.bfloat16),
        down_reduced.astype(jnp.bfloat16),
    )


def solution(mesh):
    sizes = dict(zip(mesh.axis_names, mesh.devices.shape))
    members = sizes["expert"]
    grid = mesh.devices.reshape(sizes["pipe"], members // HSPLIT, HSPLIT, sizes["dp"])
    fine = Mesh(grid, ("pipe", "eg", "ej", "dp"))
    tokens = ("eg", "ej", "dp")
    rows = ("eg", "ej")
    in_specs = (
        P("pipe", None, tokens, None),
        P(None, tokens, None),
        P("pipe", tokens, None),
        P("pipe", None),
        P("pipe", None, tokens, None),
        P("pipe", None, tokens, None),
        P("pipe", None, tokens, None),
        P("pipe", rows, "dp"),
        P("pipe", rows, "dp"),
        P("pipe", rows, "dp"),
    )
    out_specs = (
        P("pipe", None, tokens, None),
        P("pipe", None, tokens, None),
        P("pipe", rows, "dp"),
        P("pipe", rows, "dp"),
        P("pipe", rows, "dp"),
    )
    return jax.shard_map(local, mesh=fine, in_specs=in_specs, out_specs=out_specs, check_vma=False)
```

```python
import jax
import jax.numpy as jnp
from jax import lax
from jax.sharding import Mesh, PartitionSpec as P

HSPLIT = 4


EPSILON = 1e-06


def shifted(block, axis, distance):
    devices = range(lax.axis_size(axis))
    route = [(i - distance, i) for i in devices if i - distance in devices]
    return lax.ppermute(block, axis, route)


def rotated(block, axis, distance):
    size = lax.axis_size(axis)
    route = [(i, (i + distance) % size) for i in range(size)]
    return lax.ppermute(block, axis, route)


def flipped(block, axis, mask):
    size = lax.axis_size(axis)
    route = [(i, i ^ mask) for i in range(size)]
    return lax.ppermute(block, axis, route)


def silu_parts(gate_value):
    sigmoid_value = jax.nn.sigmoid(gate_value)
    return (gate_value * sigmoid_value, sigmoid_value * (1.0 + gate_value * (1.0 - sigmoid_value)))


def contract_last(first_operand, second_operand):
    return lax.dot_general(
        first_operand, second_operand, (((1,), (1,)), ((), ())), preferred_element_type=jnp.float32
    )


def contract_first(first_operand, second_operand):
    return lax.dot_general(
        first_operand, second_operand, (((0,), (0,)), ((), ())), preferred_element_type=jnp.float32
    )


def to_experts(blocks):
    groups = blocks.shape[0]
    moved = [blocks[0]] + [rotated(blocks[s], "eg", s) for s in range(1, groups)]
    return jnp.stack(moved)


def to_owners(blocks):
    groups = blocks.shape[0]
    moved = [blocks[0]] + [
        rotated(blocks[s].astype(jnp.bfloat16), "eg", -s).astype(jnp.float32)
        for s in range(1, groups)
    ]
    return jnp.stack(moved)


def weights_to_owners(blocks):
    groups = blocks.shape[0]
    moved = [blocks[0]] + [rotated(blocks[s], "eg", -s) for s in range(1, groups)]
    return jnp.stack(moved)


def relayed(block):
    width = block.shape[-1]
    return lax.axis_size("ej") == 4 and width >= 256 and width % 256 == 0


def gather_quad(blocks):
    staged = to_experts(blocks)
    quad = lax.axis_size("ej")
    if not relayed(staged):
        return jnp.stack([staged] + [flipped(staged, "ej", t) for t in range(1, quad)])
    half = staged.shape[-1] // 2
    first = flipped(staged, "ej", 1)
    second = flipped(staged, "ej", 2)
    diagonal = jnp.concatenate(
        [flipped(first[..., :half], "ej", 2), flipped(second[..., half:], "ej", 1)], axis=-1
    )
    return jnp.stack([staged, first, second, diagonal])


def reduce_quad(parts):
    quad = parts.shape[0]
    total = parts[0].astype(jnp.float32)
    if not relayed(parts):
        for t in range(1, quad):
            total = total + flipped(parts[t], "ej", t).astype(jnp.float32)
        return total
    half = parts.shape[-1] // 2
    from_first = flipped(parts[3][..., :half], "ej", 1).astype(jnp.float32)
    from_second = flipped(parts[3][..., half:], "ej", 2).astype(jnp.float32)
    toward_second = jnp.concatenate(
        [(parts[2][..., :half].astype(jnp.float32) + from_first).astype(parts.dtype), parts[2][..., half:]],
        axis=-1,
    )
    toward_first = jnp.concatenate(
        [parts[1][..., :half], (parts[1][..., half:].astype(jnp.float32) + from_second).astype(parts.dtype)],
        axis=-1,
    )
    total = total + flipped(toward_second, "ej", 2).astype(jnp.float32)
    return total + flipped(toward_first, "ej", 1).astype(jnp.float32)


def local(
    saved_inputs,
    output_grads,
    entry_grads,
    norm_gain,
    expert_ids,
    keep_flags,
    combine_weights,
    gate_weight,
    up_weight,
    down_weight,
):
    sections = lax.axis_size("pipe")
    is_last = lax.axis_index("pipe") == sections - 1
    groups = lax.axis_size("eg")
    me = lax.axis_index("eg")
    micro_count = saved_inputs.shape[1]
    token_rows = saved_inputs.shape[2]
    feature_count = saved_inputs.shape[3]
    pick_count = expert_ids.shape[3]
    capacity = max(2, 3 * token_rows * pick_count // (2 * groups))
    slot_count = groups * capacity

    def whole_rows(stored):
        return lax.all_gather(stored, "dp", axis=1, tiled=True)

    gate_full, up_full, down_full = (
        whole_rows(gate_weight[0]),
        whole_rows(up_weight[0]),
        whole_rows(down_weight[0]),
    )
    hidden_count = gate_full.shape[0]
    paired_weights = jnp.concatenate([gate_full, up_full], axis=0)
    gain_row = norm_gain[0][None, :]
    slot_ids = jnp.arange(slot_count, dtype=jnp.int32)
    expert_range = jnp.arange(groups, dtype=jnp.int32)

    def prepare(moment):
        inputs = saved_inputs[0, moment].astype(jnp.float32)
        scales = lax.rsqrt(jnp.mean(inputs * inputs, axis=1, keepdims=True) + EPSILON)
        normed = (inputs * scales * gain_row).astype(jnp.bfloat16)
        chosen = expert_ids[0, moment].reshape(-1)
        onehot = (chosen[:, None] == expert_range[None, :]).astype(jnp.int32)
        rank_values = jnp.sum((jnp.cumsum(onehot, axis=0) - 1) * onehot, axis=1)
        places = ((chosen - me) % groups) * capacity + rank_values
        placing = places[:, None] == slot_ids[None, :]
        token_map = jnp.any(placing.reshape(token_rows, pick_count, slot_count), axis=1)
        selector = token_map.T.astype(jnp.bfloat16)
        keeping = keep_flags[0, moment].reshape(-1)
        scaled = (combine_weights[0, moment].reshape(-1) * keeping.astype(jnp.bfloat16)).astype(
            jnp.float32
        )
        weight_slots = jnp.sum(jnp.where(placing, scaled[:, None], 0.0), axis=0).astype(
            jnp.bfloat16
        )
        return (inputs, scales, normed, places, selector, keeping, weight_slots)

    def dispatch_rows(selector, source_rows):
        picked = jnp.dot(selector, source_rows, preferred_element_type=jnp.float32)
        return picked.astype(jnp.bfloat16).reshape(groups, capacity, feature_count)

    prepared = [prepare(moment) for moment in range(micro_count)]
    rows_gathered = [
        gather_quad(dispatch_rows(current[4], current[2])) for current in prepared
    ]
    weights_gathered = [
        gather_quad(current[6].reshape(groups, capacity)) for current in prepared
    ]
    leaving_list = []
    combine_list = []
    kept_list = []
    previous = entry_grads[0]
    for moment in range(micro_count):
        current = prepared[moment]
        if moment == 0:
            arriving = entry_grads[0]
        else:
            arriving = shifted(previous, "pipe", -1)
        incoming = jnp.where(is_last, output_grads[moment], arriving)
        grads_in = gather_quad(dispatch_rows(current[4], incoming))
        flat_rows = rows_gathered[moment].reshape(-1, feature_count)
        flat_grads = grads_in.reshape(-1, feature_count)
        scale_column = weights_gathered[moment].reshape(-1, 1).astype(jnp.float32)
        gate_value = contract_last(flat_rows, gate_full)
        upward = contract_last(flat_rows, up_full)
        backward = contract_last(flat_grads, down_full)
        active, derivative = silu_parts(gate_value)
        hidden = active * upward
        part_weight = jnp.sum(hidden * backward, axis=1).astype(jnp.bfloat16)
        grad_up = (scale_column * backward * active).astype(jnp.bfloat16)
        grad_gate = (scale_column * backward * upward * derivative).astype(jnp.bfloat16)
        grad_pair = jnp.concatenate([grad_gate, grad_up], axis=1)
        part_rows = jnp.dot(grad_pair, paired_weights, preferred_element_type=jnp.float32).astype(
            jnp.bfloat16
        )
        hidden_scaled = (hidden * scale_column).astype(jnp.bfloat16)
        kept_list.append((grad_pair, hidden_scaled, flat_rows, flat_grads))
        rows_back = to_owners(
            reduce_quad(part_rows.reshape(-1, groups, capacity, feature_count))
        )
        weights_back = weights_to_owners(
            reduce_quad(part_weight.reshape(-1, groups, capacity))
        )
        (
            finish_inputs,
            finish_scales,
            finish_normed,
            finish_places,
            finish_selector,
            finish_keeping,
            finish_weight_slots,
        ) = current
        summed = rows_back.reshape(slot_count, feature_count)
        weight_sums = weights_back.reshape(slot_count)
        expert_rows = jnp.sum(
            jnp.take(summed, finish_places, axis=0).reshape(token_rows, pick_count, feature_count),
            axis=1,
        )
        combine_grad = (
            jnp.take(weight_sums, finish_places) * finish_keeping.astype(jnp.float32)
        ).reshape(token_rows, pick_count)
        gained = gain_row * expert_rows
        mixed_mean = jnp.mean(finish_inputs * gained, axis=1, keepdims=True)
        leaving = (
            incoming.astype(jnp.float32)
            + finish_scales * gained
            - finish_inputs * (finish_scales * finish_scales * finish_scales) * mixed_mean
        ).astype(jnp.bfloat16)
        previous = leaving
        leaving_list.append(leaving)
        combine_list.append(combine_grad)
    pair_all = jnp.concatenate([kept[0] for kept in kept_list], axis=0)
    scaled_all = jnp.concatenate([kept[1] for kept in kept_list], axis=0)
    rows_all = jnp.concatenate([kept[2] for kept in kept_list], axis=0)
    grads_all = jnp.concatenate([kept[3] for kept in kept_list], axis=0)
    pair_total = contract_first(pair_all, rows_all).reshape(2, hidden_count, feature_count)
    down_total = contract_first(scaled_all, grads_all)[None]
    pair_reduced, down_reduced = (
        lax.psum_scatter(
            pair_total.astype(jnp.bfloat16), "dp", scatter_dimension=2, tiled=True
        ).astype(jnp.float32),
        lax.psum_scatter(
            down_total.astype(jnp.bfloat16), "dp", scatter_dimension=2, tiled=True
        ).astype(jnp.float32),
    )
    return (
        jnp.stack(leaving_list)[None],
        jnp.stack(combine_list)[None],
        pair_reduced[0:1].astype(jnp.bfloat16),
        pair_reduced[1:2].astype(jnp.bfloat16),
        down_reduced.astype(jnp.bfloat16),
    )


def solution(mesh):
    sizes = dict(zip(mesh.axis_names, mesh.devices.shape))
    members = sizes["expert"]
    grid = mesh.devices.reshape(sizes["pipe"], members // HSPLIT, HSPLIT, sizes["dp"])
    fine = Mesh(grid, ("pipe", "eg", "ej", "dp"))
    tokens = ("eg", "ej", "dp")
    rows = ("eg", "ej")
    in_specs = (
        P("pipe", None, tokens, None),
        P(None, tokens, None),
        P("pipe", tokens, None),
        P("pipe", None),
        P("pipe", None, tokens, None),
        P("pipe", None, tokens, None),
        P("pipe", None, tokens, None),
        P("pipe", rows, "dp"),
        P("pipe", rows, "dp"),
        P("pipe", rows, "dp"),
    )
    out_specs = (
        P("pipe", None, tokens, None),
        P("pipe", None, tokens, None),
        P("pipe", rows, "dp"),
        P("pipe", rows, "dp"),
        P("pipe", rows, "dp"),
    )
    return jax.shard_map(local, mesh=fine, in_specs=in_specs, out_specs=out_specs, check_vma=False)
```

```python
import jax
import jax.numpy as jnp
from jax import lax
from jax.sharding import Mesh, PartitionSpec as P

HSPLIT = 4


EPSILON = 1e-06


def shifted(block, axis, distance):
    devices = range(lax.axis_size(axis))
    route = [(i - distance, i) for i in devices if i - distance in devices]
    return lax.ppermute(block, axis, route)


def rotated(block, axis, distance):
    size = lax.axis_size(axis)
    route = [(i, (i + distance) % size) for i in range(size)]
    return lax.ppermute(block, axis, route)


def flipped(block, axis, mask):
    size = lax.axis_size(axis)
    route = [(i, i ^ mask) for i in range(size)]
    return lax.ppermute(block, axis, route)


def silu_parts(gate_value):
    sigmoid_value = jax.nn.sigmoid(gate_value)
    return (gate_value * sigmoid_value, sigmoid_value * (1.0 + gate_value * (1.0 - sigmoid_value)))


def contract_last(first_operand, second_operand):
    return lax.dot_general(
        first_operand, second_operand, (((1,), (1,)), ((), ())), preferred_element_type=jnp.float32
    )


def contract_first(first_operand, second_operand):
    return lax.dot_general(
        first_operand, second_operand, (((0,), (0,)), ((), ())), preferred_element_type=jnp.float32
    )


def to_experts(blocks):
    groups = blocks.shape[0]
    moved = [blocks[0]] + [rotated(blocks[s], "eg", s) for s in range(1, groups)]
    return jnp.stack(moved)


def to_owners(blocks):
    groups = blocks.shape[0]
    moved = [blocks[0]] + [
        rotated(blocks[s].astype(jnp.bfloat16), "eg", -s).astype(jnp.float32)
        for s in range(1, groups)
    ]
    return jnp.stack(moved)


def weights_to_owners(blocks):
    groups = blocks.shape[0]
    moved = [blocks[0]] + [rotated(blocks[s], "eg", -s) for s in range(1, groups)]
    return jnp.stack(moved)


def relayed(block):
    width = block.shape[-1]
    return lax.axis_size("ej") == 4 and width >= 256 and width % 256 == 0


def gather_quad(blocks):
    staged = to_experts(blocks)
    quad = lax.axis_size("ej")
    if not relayed(staged):
        return jnp.stack([staged] + [flipped(staged, "ej", t) for t in range(1, quad)])
    half = staged.shape[-1] // 2
    first = flipped(staged, "ej", 1)
    second = flipped(staged, "ej", 2)
    diagonal = jnp.concatenate(
        [flipped(first[..., :half], "ej", 2), flipped(second[..., half:], "ej", 1)], axis=-1
    )
    return jnp.stack([staged, first, second, diagonal])


def reduce_quad(parts):
    quad = parts.shape[0]
    total = parts[0].astype(jnp.float32)
    if not relayed(parts):
        for t in range(1, quad):
            total = total + flipped(parts[t], "ej", t).astype(jnp.float32)
        return total
    half = parts.shape[-1] // 2
    from_first = flipped(parts[3][..., :half], "ej", 1).astype(jnp.float32)
    from_second = flipped(parts[3][..., half:], "ej", 2).astype(jnp.float32)
    toward_second = jnp.concatenate(
        [(parts[2][..., :half].astype(jnp.float32) + from_first).astype(parts.dtype), parts[2][..., half:]],
        axis=-1,
    )
    toward_first = jnp.concatenate(
        [parts[1][..., :half], (parts[1][..., half:].astype(jnp.float32) + from_second).astype(parts.dtype)],
        axis=-1,
    )
    total = total + flipped(toward_second, "ej", 2).astype(jnp.float32)
    return total + flipped(toward_first, "ej", 1).astype(jnp.float32)


def local(
    saved_inputs,
    output_grads,
    entry_grads,
    norm_gain,
    expert_ids,
    keep_flags,
    combine_weights,
    gate_weight,
    up_weight,
    down_weight,
):
    sections = lax.axis_size("pipe")
    is_last = lax.axis_index("pipe") == sections - 1
    groups = lax.axis_size("eg")
    me = lax.axis_index("eg")
    micro_count = saved_inputs.shape[1]
    token_rows = saved_inputs.shape[2]
    feature_count = saved_inputs.shape[3]
    pick_count = expert_ids.shape[3]
    capacity = max(2, 3 * token_rows * pick_count // (2 * groups))
    slot_count = groups * capacity
    low_half = lax.axis_index("dp") == 0

    def whole_rows(stored):
        if lax.axis_size("dp") != 2:
            return lax.all_gather(stored, "dp", axis=1, tiled=True)
        partner = flipped(stored, "dp", 1)
        return jnp.where(
            low_half,
            jnp.concatenate([stored, partner], axis=1),
            jnp.concatenate([partner, stored], axis=1),
        )

    gate_full, up_full, down_full = (
        whole_rows(gate_weight[0]),
        whole_rows(up_weight[0]),
        whole_rows(down_weight[0]),
    )
    hidden_count = gate_full.shape[0]
    paired_weights = jnp.concatenate([gate_full, up_full], axis=0)
    gain_row = norm_gain[0][None, :]
    slot_ids = jnp.arange(slot_count, dtype=jnp.int32)
    expert_range = jnp.arange(groups, dtype=jnp.int32)

    def prepare(moment):
        inputs = saved_inputs[0, moment].astype(jnp.float32)
        scales = lax.rsqrt(jnp.mean(inputs * inputs, axis=1, keepdims=True) + EPSILON)
        normed = (inputs * scales * gain_row).astype(jnp.bfloat16)
        chosen = expert_ids[0, moment].reshape(-1)
        onehot = (chosen[:, None] == expert_range[None, :]).astype(jnp.int32)
        rank_values = jnp.sum((jnp.cumsum(onehot, axis=0) - 1) * onehot, axis=1)
        places = ((chosen - me) % groups) * capacity + rank_values
        placing = places[:, None] == slot_ids[None, :]
        token_map = jnp.any(placing.reshape(token_rows, pick_count, slot_count), axis=1)
        selector = token_map.T.astype(jnp.bfloat16)
        keeping = keep_flags[0, moment].reshape(-1)
        scaled = (combine_weights[0, moment].reshape(-1) * keeping.astype(jnp.bfloat16)).astype(
            jnp.float32
        )
        weight_slots = jnp.sum(jnp.where(placing, scaled[:, None], 0.0), axis=0).astype(
            jnp.bfloat16
        )
        return (inputs, scales, normed, places, selector, keeping, weight_slots)

    def dispatch_rows(selector, source_rows):
        picked = jnp.dot(selector, source_rows, preferred_element_type=jnp.float32)
        return picked.astype(jnp.bfloat16).reshape(groups, capacity, feature_count)

    prepared = [prepare(moment) for moment in range(micro_count)]
    first_incoming = jnp.where(is_last, output_grads[0], entry_grads[0])
    first_grads = gather_quad(dispatch_rows(prepared[0][4], first_incoming))
    rows_gathered = [gather_quad(dispatch_rows(prepared[0][4], prepared[0][2]))]
    weights_gathered = [gather_quad(prepared[0][6].reshape(groups, capacity))]
    for current in prepared[1:]:
        later_rows, later_weights, _ = lax.optimization_barrier(
            (dispatch_rows(current[4], current[2]), current[6], first_grads)
        )
        rows_gathered.append(gather_quad(later_rows))
        weights_gathered.append(gather_quad(later_weights.reshape(groups, capacity)))
    leaving_list = []
    combine_list = []
    kept_list = []
    previous = entry_grads[0]
    for moment in range(micro_count):
        current = prepared[moment]
        if moment == 0:
            incoming = first_incoming
            grads_in = first_grads
        else:
            arriving = shifted(previous, "pipe", -1)
            incoming = jnp.where(is_last, output_grads[moment], arriving)
            grads_in = gather_quad(dispatch_rows(current[4], incoming))
        flat_rows = rows_gathered[moment].reshape(-1, feature_count)
        flat_grads = grads_in.reshape(-1, feature_count)
        scale_column = weights_gathered[moment].reshape(-1, 1).astype(jnp.float32)
        gate_value = contract_last(flat_rows, gate_full)
        upward = contract_last(flat_rows, up_full)
        backward = contract_last(flat_grads, down_full)
        active, derivative = silu_parts(gate_value)
        hidden = active * upward
        part_weight = jnp.sum(hidden * backward, axis=1).astype(jnp.bfloat16)
        grad_up = (scale_column * backward * active).astype(jnp.bfloat16)
        grad_gate = (scale_column * backward * upward * derivative).astype(jnp.bfloat16)
        grad_pair = jnp.concatenate([grad_gate, grad_up], axis=1)
        part_rows = jnp.dot(grad_pair, paired_weights, preferred_element_type=jnp.float32).astype(
            jnp.bfloat16
        )
        hidden_scaled = (hidden * scale_column).astype(jnp.bfloat16)
        kept_list.append((grad_pair, hidden_scaled, flat_rows, flat_grads))
        rows_back = to_owners(
            reduce_quad(part_rows.reshape(-1, groups, capacity, feature_count))
        )
        weights_back = weights_to_owners(
            reduce_quad(part_weight.reshape(-1, groups, capacity))
        )
        (
            finish_inputs,
            finish_scales,
            finish_normed,
            finish_places,
            finish_selector,
            finish_keeping,
            finish_weight_slots,
        ) = current
        summed = rows_back.reshape(slot_count, feature_count)
        weight_sums = weights_back.reshape(slot_count)
        expert_rows = jnp.sum(
            jnp.take(summed, finish_places, axis=0).reshape(token_rows, pick_count, feature_count),
            axis=1,
        )
        combine_grad = (
            jnp.take(weight_sums, finish_places) * finish_keeping.astype(jnp.float32)
        ).reshape(token_rows, pick_count)
        gained = gain_row * expert_rows
        mixed_mean = jnp.mean(finish_inputs * gained, axis=1, keepdims=True)
        leaving = (
            incoming.astype(jnp.float32)
            + finish_scales * gained
            - finish_inputs * (finish_scales * finish_scales * finish_scales) * mixed_mean
        ).astype(jnp.bfloat16)
        previous = leaving
        leaving_list.append(leaving)
        combine_list.append(combine_grad)
    pair_all = jnp.concatenate([kept[0] for kept in kept_list], axis=0)
    scaled_all = jnp.concatenate([kept[1] for kept in kept_list], axis=0)
    rows_all = jnp.concatenate([kept[2] for kept in kept_list], axis=0)
    grads_all = jnp.concatenate([kept[3] for kept in kept_list], axis=0)
    pair_total = contract_first(pair_all, rows_all).reshape(2, hidden_count, feature_count)
    down_total = contract_first(scaled_all, grads_all)[None]
    pair_reduced, down_reduced = (
        lax.psum_scatter(
            pair_total.astype(jnp.bfloat16), "dp", scatter_dimension=2, tiled=True
        ).astype(jnp.float32),
        lax.psum_scatter(
            down_total.astype(jnp.bfloat16), "dp", scatter_dimension=2, tiled=True
        ).astype(jnp.float32),
    )
    return (
        jnp.stack(leaving_list)[None],
        jnp.stack(combine_list)[None],
        pair_reduced[0:1].astype(jnp.bfloat16),
        pair_reduced[1:2].astype(jnp.bfloat16),
        down_reduced.astype(jnp.bfloat16),
    )


def solution(mesh):
    sizes = dict(zip(mesh.axis_names, mesh.devices.shape))
    members = sizes["expert"]
    grid = mesh.devices.reshape(sizes["pipe"], members // HSPLIT, HSPLIT, sizes["dp"])
    fine = Mesh(grid, ("pipe", "eg", "ej", "dp"))
    tokens = ("eg", "ej", "dp")
    rows = ("eg", "ej")
    in_specs = (
        P("pipe", None, tokens, None),
        P(None, tokens, None),
        P("pipe", tokens, None),
        P("pipe", None),
        P("pipe", None, tokens, None),
        P("pipe", None, tokens, None),
        P("pipe", None, tokens, None),
        P("pipe", rows, "dp"),
        P("pipe", rows, "dp"),
        P("pipe", rows, "dp"),
    )
    out_specs = (
        P("pipe", None, tokens, None),
        P("pipe", None, tokens, None),
        P("pipe", rows, "dp"),
        P("pipe", rows, "dp"),
        P("pipe", rows, "dp"),
    )
    return jax.shard_map(local, mesh=fine, in_specs=in_specs, out_specs=out_specs, check_vma=False)
```

```python
import jax
import jax.numpy as jnp
from jax import lax
from jax.sharding import Mesh, PartitionSpec as P

HSPLIT = 4


EPSILON = 1e-06


def shifted(block, axis, distance):
    devices = range(lax.axis_size(axis))
    route = [(i - distance, i) for i in devices if i - distance in devices]
    return lax.ppermute(block, axis, route)


def rotated(block, axis, distance):
    size = lax.axis_size(axis)
    route = [(i, (i + distance) % size) for i in range(size)]
    return lax.ppermute(block, axis, route)


def flipped(block, axis, mask):
    size = lax.axis_size(axis)
    route = [(i, i ^ mask) for i in range(size)]
    return lax.ppermute(block, axis, route)


def silu_parts(gate_value):
    sigmoid_value = jax.nn.sigmoid(gate_value)
    return (gate_value * sigmoid_value, sigmoid_value * (1.0 + gate_value * (1.0 - sigmoid_value)))


def contract_last(first_operand, second_operand):
    return lax.dot_general(
        first_operand, second_operand, (((1,), (1,)), ((), ())), preferred_element_type=jnp.float32
    )


def contract_first(first_operand, second_operand):
    return lax.dot_general(
        first_operand, second_operand, (((0,), (0,)), ((), ())), preferred_element_type=jnp.float32
    )


def to_experts(blocks):
    groups = blocks.shape[0]
    moved = [blocks[0]] + [rotated(blocks[s], "eg", s) for s in range(1, groups)]
    return jnp.stack(moved)


def to_owners(blocks):
    groups = blocks.shape[0]
    moved = [blocks[0]] + [
        rotated(blocks[s].astype(jnp.bfloat16), "eg", -s).astype(jnp.float32)
        for s in range(1, groups)
    ]
    return jnp.stack(moved)


def weights_to_owners(blocks):
    groups = blocks.shape[0]
    moved = [blocks[0]] + [rotated(blocks[s], "eg", -s) for s in range(1, groups)]
    return jnp.stack(moved)


def relayed(block):
    width = block.shape[-1]
    return lax.axis_size("ej") == 4 and width >= 256 and width % 256 == 0


def gather_quad(blocks):
    staged = to_experts(blocks)
    quad = lax.axis_size("ej")
    if not relayed(staged):
        return jnp.stack([staged] + [flipped(staged, "ej", t) for t in range(1, quad)])
    half = staged.shape[-1] // 2
    first = flipped(staged, "ej", 1)
    second = flipped(staged, "ej", 2)
    diagonal = jnp.concatenate(
        [flipped(first[..., :half], "ej", 2), flipped(second[..., half:], "ej", 1)], axis=-1
    )
    return jnp.stack([staged, first, second, diagonal])


def reduce_quad(parts):
    quad = parts.shape[0]
    total = parts[0].astype(jnp.float32)
    if not relayed(parts):
        for t in range(1, quad):
            total = total + flipped(parts[t], "ej", t).astype(jnp.float32)
        return total
    half = parts.shape[-1] // 2
    from_first = flipped(parts[3][..., :half], "ej", 1).astype(jnp.float32)
    from_second = flipped(parts[3][..., half:], "ej", 2).astype(jnp.float32)
    toward_second = jnp.concatenate(
        [(parts[2][..., :half].astype(jnp.float32) + from_first).astype(parts.dtype), parts[2][..., half:]],
        axis=-1,
    )
    toward_first = jnp.concatenate(
        [parts[1][..., :half], (parts[1][..., half:].astype(jnp.float32) + from_second).astype(parts.dtype)],
        axis=-1,
    )
    total = total + flipped(toward_second, "ej", 2).astype(jnp.float32)
    return total + flipped(toward_first, "ej", 1).astype(jnp.float32)


def local(
    saved_inputs,
    output_grads,
    entry_grads,
    norm_gain,
    expert_ids,
    keep_flags,
    combine_weights,
    gate_weight,
    up_weight,
    down_weight,
):
    sections = lax.axis_size("pipe")
    is_last = lax.axis_index("pipe") == sections - 1
    groups = lax.axis_size("eg")
    me = lax.axis_index("eg")
    micro_count = saved_inputs.shape[1]
    token_rows = saved_inputs.shape[2]
    feature_count = saved_inputs.shape[3]
    pick_count = expert_ids.shape[3]
    capacity = max(2, 3 * token_rows * pick_count // (2 * groups))
    slot_count = groups * capacity
    low_half = lax.axis_index("dp") == 0

    def whole_rows(stored):
        if lax.axis_size("dp") != 2:
            return lax.all_gather(stored, "dp", axis=1, tiled=True)
        partner = flipped(stored, "dp", 1)
        return jnp.where(
            low_half,
            jnp.concatenate([stored, partner], axis=1),
            jnp.concatenate([partner, stored], axis=1),
        )

    gate_full, up_full, down_full = (
        whole_rows(gate_weight[0]),
        whole_rows(up_weight[0]),
        whole_rows(down_weight[0]),
    )
    hidden_count = gate_full.shape[0]
    paired_weights = jnp.concatenate([gate_full, up_full], axis=0)
    gain_row = norm_gain[0][None, :]
    slot_ids = jnp.arange(slot_count, dtype=jnp.int32)
    expert_range = jnp.arange(groups, dtype=jnp.int32)

    def prepare(moment):
        inputs = saved_inputs[0, moment].astype(jnp.float32)
        scales = lax.rsqrt(jnp.mean(inputs * inputs, axis=1, keepdims=True) + EPSILON)
        normed = (inputs * scales * gain_row).astype(jnp.bfloat16)
        chosen = expert_ids[0, moment].reshape(-1)
        onehot = (chosen[:, None] == expert_range[None, :]).astype(jnp.int32)
        rank_values = jnp.sum((jnp.cumsum(onehot, axis=0) - 1) * onehot, axis=1)
        places = ((chosen - me) % groups) * capacity + rank_values
        placing = places[:, None] == slot_ids[None, :]
        token_map = jnp.any(placing.reshape(token_rows, pick_count, slot_count), axis=1)
        selector = token_map.T.astype(jnp.bfloat16)
        keeping = keep_flags[0, moment].reshape(-1)
        scaled = (combine_weights[0, moment].reshape(-1) * keeping.astype(jnp.bfloat16)).astype(
            jnp.float32
        )
        weight_slots = jnp.sum(jnp.where(placing, scaled[:, None], 0.0), axis=0).astype(
            jnp.bfloat16
        )
        return (inputs, scales, normed, places, selector, keeping, weight_slots)

    def dispatch_rows(selector, source_rows):
        picked = jnp.dot(selector, source_rows, preferred_element_type=jnp.float32)
        return picked.astype(jnp.bfloat16).reshape(groups, capacity, feature_count)

    prepared = [prepare(moment) for moment in range(micro_count)]
    first_incoming = jnp.where(is_last, output_grads[0], entry_grads[0])
    first_both = gather_quad(
        jnp.concatenate(
            [
                dispatch_rows(prepared[0][4], prepared[0][2]),
                dispatch_rows(prepared[0][4], first_incoming),
            ],
            axis=1,
        )
    )
    first_grads = first_both[:, :, capacity:]
    rows_gathered = [first_both[:, :, :capacity]]
    weights_gathered = [gather_quad(prepared[0][6].reshape(groups, capacity))]
    for current in prepared[1:]:
        later_rows, later_weights, _ = lax.optimization_barrier(
            (dispatch_rows(current[4], current[2]), current[6], first_grads)
        )
        rows_gathered.append(gather_quad(later_rows))
        weights_gathered.append(gather_quad(later_weights.reshape(groups, capacity)))
    leaving_list = []
    combine_list = []
    kept_list = []
    previous = entry_grads[0]
    for moment in range(micro_count):
        current = prepared[moment]
        if moment == 0:
            incoming = first_incoming
            grads_in = first_grads
        else:
            arriving = shifted(previous, "pipe", -1)
            incoming = jnp.where(is_last, output_grads[moment], arriving)
            grads_in = gather_quad(dispatch_rows(current[4], incoming))
        flat_rows = rows_gathered[moment].reshape(-1, feature_count)
        flat_grads = grads_in.reshape(-1, feature_count)
        scale_column = weights_gathered[moment].reshape(-1, 1).astype(jnp.float32)
        gate_value = contract_last(flat_rows, gate_full)
        upward = contract_last(flat_rows, up_full)
        backward = contract_last(flat_grads, down_full)
        active, derivative = silu_parts(gate_value)
        hidden = active * upward
        part_weight = jnp.sum(hidden * backward, axis=1).astype(jnp.bfloat16)
        grad_up = (scale_column * backward * active).astype(jnp.bfloat16)
        grad_gate = (scale_column * backward * upward * derivative).astype(jnp.bfloat16)
        grad_pair = jnp.concatenate([grad_gate, grad_up], axis=1)
        part_rows = jnp.dot(grad_pair, paired_weights, preferred_element_type=jnp.float32).astype(
            jnp.bfloat16
        )
        hidden_scaled = (hidden * scale_column).astype(jnp.bfloat16)
        kept_list.append((grad_pair, hidden_scaled, flat_rows, flat_grads))
        rows_back = to_owners(
            reduce_quad(part_rows.reshape(-1, groups, capacity, feature_count))
        )
        weights_back = weights_to_owners(
            reduce_quad(part_weight.reshape(-1, groups, capacity))
        )
        (
            finish_inputs,
            finish_scales,
            finish_normed,
            finish_places,
            finish_selector,
            finish_keeping,
            finish_weight_slots,
        ) = current
        summed = rows_back.reshape(slot_count, feature_count)
        weight_sums = weights_back.reshape(slot_count)
        expert_rows = jnp.sum(
            jnp.take(summed, finish_places, axis=0).reshape(token_rows, pick_count, feature_count),
            axis=1,
        )
        combine_grad = (
            jnp.take(weight_sums, finish_places) * finish_keeping.astype(jnp.float32)
        ).reshape(token_rows, pick_count)
        gained = gain_row * expert_rows
        mixed_mean = jnp.mean(finish_inputs * gained, axis=1, keepdims=True)
        leaving = (
            incoming.astype(jnp.float32)
            + finish_scales * gained
            - finish_inputs * (finish_scales * finish_scales * finish_scales) * mixed_mean
        ).astype(jnp.bfloat16)
        previous = leaving
        leaving_list.append(leaving)
        combine_list.append(combine_grad)
    pair_all = jnp.concatenate([kept[0] for kept in kept_list], axis=0)
    scaled_all = jnp.concatenate([kept[1] for kept in kept_list], axis=0)
    rows_all = jnp.concatenate([kept[2] for kept in kept_list], axis=0)
    grads_all = jnp.concatenate([kept[3] for kept in kept_list], axis=0)
    pair_total = contract_first(pair_all, rows_all).reshape(2, hidden_count, feature_count)
    down_total = contract_first(scaled_all, grads_all)[None]
    pair_reduced, down_reduced = (
        lax.psum_scatter(
            pair_total.astype(jnp.bfloat16), "dp", scatter_dimension=2, tiled=True
        ).astype(jnp.float32),
        lax.psum_scatter(
            down_total.astype(jnp.bfloat16), "dp", scatter_dimension=2, tiled=True
        ).astype(jnp.float32),
    )
    return (
        jnp.stack(leaving_list)[None],
        jnp.stack(combine_list)[None],
        pair_reduced[0:1].astype(jnp.bfloat16),
        pair_reduced[1:2].astype(jnp.bfloat16),
        down_reduced.astype(jnp.bfloat16),
    )


def solution(mesh):
    sizes = dict(zip(mesh.axis_names, mesh.devices.shape))
    members = sizes["expert"]
    grid = mesh.devices.reshape(sizes["pipe"], members // HSPLIT, HSPLIT, sizes["dp"])
    fine = Mesh(grid, ("pipe", "eg", "ej", "dp"))
    tokens = ("eg", "ej", "dp")
    rows = ("eg", "ej")
    in_specs = (
        P("pipe", None, tokens, None),
        P(None, tokens, None),
        P("pipe", tokens, None),
        P("pipe", None),
        P("pipe", None, tokens, None),
        P("pipe", None, tokens, None),
        P("pipe", None, tokens, None),
        P("pipe", rows, "dp"),
        P("pipe", rows, "dp"),
        P("pipe", rows, "dp"),
    )
    out_specs = (
        P("pipe", None, tokens, None),
        P("pipe", None, tokens, None),
        P("pipe", rows, "dp"),
        P("pipe", rows, "dp"),
        P("pipe", rows, "dp"),
    )
    return jax.shard_map(local, mesh=fine, in_specs=in_specs, out_specs=out_specs, check_vma=False)
```

```python
import jax
import jax.numpy as jnp
from jax import lax
from jax.sharding import Mesh, PartitionSpec as P

HSPLIT = 4


EPSILON = 1e-06


def shifted(block, axis, distance):
    devices = range(lax.axis_size(axis))
    route = [(i - distance, i) for i in devices if i - distance in devices]
    return lax.ppermute(block, axis, route)


def in_streams(block, axis, route):
    width = block.shape[-1]
    if width < 2048 or width % 256:
        return lax.ppermute(block, axis, route)
    half = width // 2
    return jnp.concatenate(
        [lax.ppermute(block[..., :half], axis, route), lax.ppermute(block[..., half:], axis, route)],
        axis=-1,
    )


def rotated(block, axis, distance):
    size = lax.axis_size(axis)
    route = [(i, (i + distance) % size) for i in range(size)]
    return in_streams(block, axis, route)


def flipped(block, axis, mask):
    size = lax.axis_size(axis)
    route = [(i, i ^ mask) for i in range(size)]
    return in_streams(block, axis, route)


def silu_parts(gate_value):
    sigmoid_value = jax.nn.sigmoid(gate_value)
    return (gate_value * sigmoid_value, sigmoid_value * (1.0 + gate_value * (1.0 - sigmoid_value)))


def contract_last(first_operand, second_operand):
    return lax.dot_general(
        first_operand, second_operand, (((1,), (1,)), ((), ())), preferred_element_type=jnp.float32
    )


def contract_first(first_operand, second_operand):
    return lax.dot_general(
        first_operand, second_operand, (((0,), (0,)), ((), ())), preferred_element_type=jnp.float32
    )


def to_experts(blocks):
    groups = blocks.shape[0]
    moved = [blocks[0]] + [rotated(blocks[s], "eg", s) for s in range(1, groups)]
    return jnp.stack(moved)


def to_owners(blocks):
    groups = blocks.shape[0]
    moved = [blocks[0]] + [
        rotated(blocks[s].astype(jnp.bfloat16), "eg", -s).astype(jnp.float32)
        for s in range(1, groups)
    ]
    return jnp.stack(moved)


def weights_to_owners(blocks):
    groups = blocks.shape[0]
    moved = [blocks[0]] + [rotated(blocks[s], "eg", -s) for s in range(1, groups)]
    return jnp.stack(moved)


def relayed(block):
    width = block.shape[-1]
    return lax.axis_size("ej") == 4 and width >= 256 and width % 256 == 0


def gather_quad(blocks):
    staged = to_experts(blocks)
    quad = lax.axis_size("ej")
    if not relayed(staged):
        return jnp.stack([staged] + [flipped(staged, "ej", t) for t in range(1, quad)])
    half = staged.shape[-1] // 2
    first = flipped(staged, "ej", 1)
    second = flipped(staged, "ej", 2)
    diagonal = jnp.concatenate(
        [flipped(first[..., :half], "ej", 2), flipped(second[..., half:], "ej", 1)], axis=-1
    )
    return jnp.stack([staged, first, second, diagonal])


def reduce_quad(parts):
    quad = parts.shape[0]
    total = parts[0].astype(jnp.float32)
    if not relayed(parts):
        for t in range(1, quad):
            total = total + flipped(parts[t], "ej", t).astype(jnp.float32)
        return total
    half = parts.shape[-1] // 2
    from_first = flipped(parts[3][..., :half], "ej", 1).astype(jnp.float32)
    from_second = flipped(parts[3][..., half:], "ej", 2).astype(jnp.float32)
    toward_second = jnp.concatenate(
        [(parts[2][..., :half].astype(jnp.float32) + from_first).astype(parts.dtype), parts[2][..., half:]],
        axis=-1,
    )
    toward_first = jnp.concatenate(
        [parts[1][..., :half], (parts[1][..., half:].astype(jnp.float32) + from_second).astype(parts.dtype)],
        axis=-1,
    )
    total = total + flipped(toward_second, "ej", 2).astype(jnp.float32)
    return total + flipped(toward_first, "ej", 1).astype(jnp.float32)


def local(
    saved_inputs,
    output_grads,
    entry_grads,
    norm_gain,
    expert_ids,
    keep_flags,
    combine_weights,
    gate_weight,
    up_weight,
    down_weight,
):
    sections = lax.axis_size("pipe")
    is_last = lax.axis_index("pipe") == sections - 1
    groups = lax.axis_size("eg")
    me = lax.axis_index("eg")
    micro_count = saved_inputs.shape[1]
    token_rows = saved_inputs.shape[2]
    feature_count = saved_inputs.shape[3]
    pick_count = expert_ids.shape[3]
    capacity = max(2, 3 * token_rows * pick_count // (2 * groups))
    slot_count = groups * capacity
    low_half = lax.axis_index("dp") == 0

    def whole_rows(stored):
        if lax.axis_size("dp") != 2:
            return lax.all_gather(stored, "dp", axis=1, tiled=True)
        partner = flipped(stored, "dp", 1)
        return jnp.where(
            low_half,
            jnp.concatenate([stored, partner], axis=1),
            jnp.concatenate([partner, stored], axis=1),
        )

    gate_full, up_full, down_full = (
        whole_rows(gate_weight[0]),
        whole_rows(up_weight[0]),
        whole_rows(down_weight[0]),
    )
    hidden_count = gate_full.shape[0]
    paired_weights = jnp.concatenate([gate_full, up_full], axis=0)
    gain_row = norm_gain[0][None, :]
    slot_ids = jnp.arange(slot_count, dtype=jnp.int32)
    expert_range = jnp.arange(groups, dtype=jnp.int32)

    def prepare(moment):
        inputs = saved_inputs[0, moment].astype(jnp.float32)
        scales = lax.rsqrt(jnp.mean(inputs * inputs, axis=1, keepdims=True) + EPSILON)
        normed = (inputs * scales * gain_row).astype(jnp.bfloat16)
        chosen = expert_ids[0, moment].reshape(-1)
        onehot = (chosen[:, None] == expert_range[None, :]).astype(jnp.int32)
        rank_values = jnp.sum((jnp.cumsum(onehot, axis=0) - 1) * onehot, axis=1)
        places = ((chosen - me) % groups) * capacity + rank_values
        placing = places[:, None] == slot_ids[None, :]
        token_map = jnp.any(placing.reshape(token_rows, pick_count, slot_count), axis=1)
        selector = token_map.T.astype(jnp.bfloat16)
        keeping = keep_flags[0, moment].reshape(-1)
        scaled = (combine_weights[0, moment].reshape(-1) * keeping.astype(jnp.bfloat16)).astype(
            jnp.float32
        )
        weight_slots = jnp.sum(jnp.where(placing, scaled[:, None], 0.0), axis=0).astype(
            jnp.bfloat16
        )
        return (inputs, scales, normed, places, selector, keeping, weight_slots)

    def dispatch_rows(selector, source_rows):
        picked = jnp.dot(selector, source_rows, preferred_element_type=jnp.float32)
        return picked.astype(jnp.bfloat16).reshape(groups, capacity, feature_count)

    prepared = [prepare(moment) for moment in range(micro_count)]
    first_incoming = jnp.where(is_last, output_grads[0], entry_grads[0])
    first_grads = gather_quad(dispatch_rows(prepared[0][4], first_incoming))
    rows_gathered = [gather_quad(dispatch_rows(prepared[0][4], prepared[0][2]))]
    weights_gathered = [gather_quad(prepared[0][6].reshape(groups, capacity))]
    for current in prepared[1:]:
        later_rows, later_weights, _ = lax.optimization_barrier(
            (dispatch_rows(current[4], current[2]), current[6], first_grads)
        )
        rows_gathered.append(gather_quad(later_rows))
        weights_gathered.append(gather_quad(later_weights.reshape(groups, capacity)))
    leaving_list = []
    combine_list = []
    kept_list = []
    previous = entry_grads[0]
    for moment in range(micro_count):
        current = prepared[moment]
        if moment == 0:
            incoming = first_incoming
            grads_in = first_grads
        else:
            arriving = shifted(previous, "pipe", -1)
            incoming = jnp.where(is_last, output_grads[moment], arriving)
            grads_in = gather_quad(dispatch_rows(current[4], incoming))
        flat_rows = rows_gathered[moment].reshape(-1, feature_count)
        flat_grads = grads_in.reshape(-1, feature_count)
        scale_column = weights_gathered[moment].reshape(-1, 1).astype(jnp.float32)
        gate_value = contract_last(flat_rows, gate_full)
        upward = contract_last(flat_rows, up_full)
        backward = contract_last(flat_grads, down_full)
        active, derivative = silu_parts(gate_value)
        hidden = active * upward
        part_weight = jnp.sum(hidden * backward, axis=1).astype(jnp.bfloat16)
        grad_up = (scale_column * backward * active).astype(jnp.bfloat16)
        grad_gate = (scale_column * backward * upward * derivative).astype(jnp.bfloat16)
        grad_pair = jnp.concatenate([grad_gate, grad_up], axis=1)
        part_rows = jnp.dot(grad_pair, paired_weights, preferred_element_type=jnp.float32).astype(
            jnp.bfloat16
        )
        hidden_scaled = (hidden * scale_column).astype(jnp.bfloat16)
        kept_list.append((grad_pair, hidden_scaled, flat_rows, flat_grads))
        rows_back = to_owners(
            reduce_quad(part_rows.reshape(-1, groups, capacity, feature_count))
        )
        weights_back = weights_to_owners(
            reduce_quad(part_weight.reshape(-1, groups, capacity))
        )
        (
            finish_inputs,
            finish_scales,
            finish_normed,
            finish_places,
            finish_selector,
            finish_keeping,
            finish_weight_slots,
        ) = current
        summed = rows_back.reshape(slot_count, feature_count)
        weight_sums = weights_back.reshape(slot_count)
        expert_rows = jnp.sum(
            jnp.take(summed, finish_places, axis=0).reshape(token_rows, pick_count, feature_count),
            axis=1,
        )
        combine_grad = (
            jnp.take(weight_sums, finish_places) * finish_keeping.astype(jnp.float32)
        ).reshape(token_rows, pick_count)
        gained = gain_row * expert_rows
        mixed_mean = jnp.mean(finish_inputs * gained, axis=1, keepdims=True)
        leaving = (
            incoming.astype(jnp.float32)
            + finish_scales * gained
            - finish_inputs * (finish_scales * finish_scales * finish_scales) * mixed_mean
        ).astype(jnp.bfloat16)
        previous = leaving
        leaving_list.append(leaving)
        combine_list.append(combine_grad)
    pair_all = jnp.concatenate([kept[0] for kept in kept_list], axis=0)
    scaled_all = jnp.concatenate([kept[1] for kept in kept_list], axis=0)
    rows_all = jnp.concatenate([kept[2] for kept in kept_list], axis=0)
    grads_all = jnp.concatenate([kept[3] for kept in kept_list], axis=0)
    pair_total = contract_first(pair_all, rows_all).reshape(2, hidden_count, feature_count)
    down_total = contract_first(scaled_all, grads_all)[None]
    pair_reduced, down_reduced = (
        lax.psum_scatter(
            pair_total.astype(jnp.bfloat16), "dp", scatter_dimension=2, tiled=True
        ).astype(jnp.float32),
        lax.psum_scatter(
            down_total.astype(jnp.bfloat16), "dp", scatter_dimension=2, tiled=True
        ).astype(jnp.float32),
    )
    return (
        jnp.stack(leaving_list)[None],
        jnp.stack(combine_list)[None],
        pair_reduced[0:1].astype(jnp.bfloat16),
        pair_reduced[1:2].astype(jnp.bfloat16),
        down_reduced.astype(jnp.bfloat16),
    )


def solution(mesh):
    sizes = dict(zip(mesh.axis_names, mesh.devices.shape))
    members = sizes["expert"]
    grid = mesh.devices.reshape(sizes["pipe"], members // HSPLIT, HSPLIT, sizes["dp"])
    fine = Mesh(grid, ("pipe", "eg", "ej", "dp"))
    tokens = ("eg", "ej", "dp")
    rows = ("eg", "ej")
    in_specs = (
        P("pipe", None, tokens, None),
        P(None, tokens, None),
        P("pipe", tokens, None),
        P("pipe", None),
        P("pipe", None, tokens, None),
        P("pipe", None, tokens, None),
        P("pipe", None, tokens, None),
        P("pipe", rows, "dp"),
        P("pipe", rows, "dp"),
        P("pipe", rows, "dp"),
    )
    out_specs = (
        P("pipe", None, tokens, None),
        P("pipe", None, tokens, None),
        P("pipe", rows, "dp"),
        P("pipe", rows, "dp"),
        P("pipe", rows, "dp"),
    )
    return jax.shard_map(local, mesh=fine, in_specs=in_specs, out_specs=out_specs, check_vma=False)
```

```python
import jax
import jax.numpy as jnp
from jax import lax
from jax.sharding import Mesh, PartitionSpec as P

HSPLIT = 4


EPSILON = 1e-06


def shifted(block, axis, distance):
    devices = range(lax.axis_size(axis))
    route = [(i - distance, i) for i in devices if i - distance in devices]
    return lax.ppermute(block, axis, route)


def rotated(block, axis, distance):
    size = lax.axis_size(axis)
    route = [(i, (i + distance) % size) for i in range(size)]
    return lax.ppermute(block, axis, route)


def flipped(block, axis, mask):
    size = lax.axis_size(axis)
    route = [(i, i ^ mask) for i in range(size)]
    return lax.ppermute(block, axis, route)


def silu_parts(gate_value):
    sigmoid_value = jax.nn.sigmoid(gate_value)
    return (gate_value * sigmoid_value, sigmoid_value * (1.0 + gate_value * (1.0 - sigmoid_value)))


def contract_last(first_operand, second_operand):
    return lax.dot_general(
        first_operand, second_operand, (((1,), (1,)), ((), ())), preferred_element_type=jnp.float32
    )


def contract_first(first_operand, second_operand):
    return lax.dot_general(
        first_operand, second_operand, (((0,), (0,)), ((), ())), preferred_element_type=jnp.float32
    )


def to_experts(blocks):
    groups = blocks.shape[0]
    moved = [blocks[0]] + [rotated(blocks[s], "eg", s) for s in range(1, groups)]
    return jnp.stack(moved)


def to_owners(blocks):
    groups = blocks.shape[0]
    moved = [blocks[0]] + [
        rotated(blocks[s].astype(jnp.bfloat16), "eg", -s).astype(jnp.float32)
        for s in range(1, groups)
    ]
    return jnp.stack(moved)


def weights_to_owners(blocks):
    groups = blocks.shape[0]
    moved = [blocks[0]] + [rotated(blocks[s], "eg", -s) for s in range(1, groups)]
    return jnp.stack(moved)


def relayed(block):
    width = block.shape[-1]
    return lax.axis_size("ej") == 4 and width >= 256 and width % 256 == 0


def gather_quad(blocks):
    return quad_of(to_experts(blocks))


def quad_of(staged):
    quad = lax.axis_size("ej")
    if not relayed(staged):
        return jnp.stack([staged] + [flipped(staged, "ej", t) for t in range(1, quad)])
    half = staged.shape[-1] // 2
    first = flipped(staged, "ej", 1)
    second = flipped(staged, "ej", 2)
    diagonal = jnp.concatenate(
        [flipped(first[..., :half], "ej", 2), flipped(second[..., half:], "ej", 1)], axis=-1
    )
    return jnp.stack([staged, first, second, diagonal])


def reduce_quad(parts):
    quad = parts.shape[0]
    total = parts[0].astype(jnp.float32)
    if not relayed(parts):
        for t in range(1, quad):
            total = total + flipped(parts[t], "ej", t).astype(jnp.float32)
        return total
    half = parts.shape[-1] // 2
    from_first = flipped(parts[3][..., :half], "ej", 1).astype(jnp.float32)
    from_second = flipped(parts[3][..., half:], "ej", 2).astype(jnp.float32)
    toward_second = jnp.concatenate(
        [(parts[2][..., :half].astype(jnp.float32) + from_first).astype(parts.dtype), parts[2][..., half:]],
        axis=-1,
    )
    toward_first = jnp.concatenate(
        [parts[1][..., :half], (parts[1][..., half:].astype(jnp.float32) + from_second).astype(parts.dtype)],
        axis=-1,
    )
    total = total + flipped(toward_second, "ej", 2).astype(jnp.float32)
    return total + flipped(toward_first, "ej", 1).astype(jnp.float32)


def local(
    saved_inputs,
    output_grads,
    entry_grads,
    norm_gain,
    expert_ids,
    keep_flags,
    combine_weights,
    gate_weight,
    up_weight,
    down_weight,
):
    sections = lax.axis_size("pipe")
    is_last = lax.axis_index("pipe") == sections - 1
    groups = lax.axis_size("eg")
    me = lax.axis_index("eg")
    micro_count = saved_inputs.shape[1]
    token_rows = saved_inputs.shape[2]
    feature_count = saved_inputs.shape[3]
    pick_count = expert_ids.shape[3]
    capacity = max(2, 3 * token_rows * pick_count // (2 * groups))
    slot_count = groups * capacity
    low_half = lax.axis_index("dp") == 0

    def whole_rows(stored):
        if lax.axis_size("dp") != 2:
            return lax.all_gather(stored, "dp", axis=1, tiled=True)
        partner = flipped(stored, "dp", 1)
        return jnp.where(
            low_half,
            jnp.concatenate([stored, partner], axis=1),
            jnp.concatenate([partner, stored], axis=1),
        )

    gate_full, up_full, down_full = (
        whole_rows(gate_weight[0]),
        whole_rows(up_weight[0]),
        whole_rows(down_weight[0]),
    )
    hidden_count = gate_full.shape[0]
    paired_weights = jnp.concatenate([gate_full, up_full], axis=0)
    gain_row = norm_gain[0][None, :]
    slot_ids = jnp.arange(slot_count, dtype=jnp.int32)
    expert_range = jnp.arange(groups, dtype=jnp.int32)

    def selector_of(chosen):
        onehot = (chosen[:, None] == expert_range[None, :]).astype(jnp.int32)
        rank_values = jnp.sum((jnp.cumsum(onehot, axis=0) - 1) * onehot, axis=1)
        places = ((chosen - me) % groups) * capacity + rank_values
        placing = places[:, None] == slot_ids[None, :]
        token_map = jnp.any(placing.reshape(token_rows, pick_count, slot_count), axis=1)
        return token_map.T.astype(jnp.bfloat16)

    def prepare(moment):
        inputs = saved_inputs[0, moment].astype(jnp.float32)
        scales = lax.rsqrt(jnp.mean(inputs * inputs, axis=1, keepdims=True) + EPSILON)
        normed = (inputs * scales * gain_row).astype(jnp.bfloat16)
        chosen = expert_ids[0, moment].reshape(-1)
        onehot = (chosen[:, None] == expert_range[None, :]).astype(jnp.int32)
        rank_values = jnp.sum((jnp.cumsum(onehot, axis=0) - 1) * onehot, axis=1)
        places = ((chosen - me) % groups) * capacity + rank_values
        placing = places[:, None] == slot_ids[None, :]
        token_map = jnp.any(placing.reshape(token_rows, pick_count, slot_count), axis=1)
        selector = token_map.T.astype(jnp.bfloat16)
        keeping = keep_flags[0, moment].reshape(-1)
        scaled = (combine_weights[0, moment].reshape(-1) * keeping.astype(jnp.bfloat16)).astype(
            jnp.float32
        )
        weight_slots = jnp.sum(jnp.where(placing, scaled[:, None], 0.0), axis=0).astype(
            jnp.bfloat16
        )
        return (inputs, scales, normed, places, selector, keeping, weight_slots)

    def dispatch_rows(selector, source_rows):
        picked = jnp.dot(selector, source_rows, preferred_element_type=jnp.float32)
        return picked.astype(jnp.bfloat16).reshape(groups, capacity, feature_count)

    prepared = [prepare(moment) for moment in range(micro_count)]
    first_incoming = jnp.where(is_last, output_grads[0], entry_grads[0])
    first_grads = gather_quad(dispatch_rows(prepared[0][4], first_incoming))
    rows_gathered = [gather_quad(dispatch_rows(prepared[0][4], prepared[0][2]))]
    weights_gathered = [gather_quad(prepared[0][6].reshape(groups, capacity))]
    for current in prepared[1:]:
        later_rows, later_weights, _ = lax.optimization_barrier(
            (dispatch_rows(current[4], current[2]), current[6], first_grads)
        )
        rows_gathered.append(gather_quad(later_rows))
        weights_gathered.append(gather_quad(later_weights.reshape(groups, capacity)))
    below_selectors = [
        selector_of(shifted(expert_ids[0, moment].reshape(-1), "pipe", 1))
        for moment in range(micro_count)
    ]
    last_staged = []
    for moment in range(micro_count):
        own_blocks = dispatch_rows(prepared[moment][4], output_grads[moment])
        moved = [own_blocks[0]]
        for s in range(1, groups):
            pairs = [
                ((sections - 1) * groups + g, (sections - 1) * groups + (g + s) % groups)
                for g in range(groups)
            ]
            moved.append(lax.ppermute(own_blocks[s], ("pipe", "eg"), pairs))
        last_staged.append(jnp.stack(moved))

    def relayed_down(leaving_rows, moment):
        blocks = dispatch_rows(below_selectors[moment], leaving_rows)
        moved = []
        for s in range(groups):
            pairs = [
                ((p + 1) * groups + g, p * groups + (g + s) % groups)
                for p in range(sections - 1)
                for g in range(groups)
            ]
            moved.append(lax.ppermute(blocks[s], ("pipe", "eg"), pairs))
        return jnp.stack(moved)

    leaving_list = []
    combine_list = []
    kept_list = []
    previous = entry_grads[0]
    for moment in range(micro_count):
        current = prepared[moment]
        if moment == 0:
            incoming = first_incoming
            grads_in = first_grads
        else:
            arriving = shifted(previous, "pipe", -1)
            incoming = jnp.where(is_last, output_grads[moment], arriving)
            staged = jnp.where(is_last, last_staged[moment], relayed_down(previous, moment))
            grads_in = quad_of(staged)
        flat_rows = rows_gathered[moment].reshape(-1, feature_count)
        flat_grads = grads_in.reshape(-1, feature_count)
        scale_column = weights_gathered[moment].reshape(-1, 1).astype(jnp.float32)
        gate_value = contract_last(flat_rows, gate_full)
        upward = contract_last(flat_rows, up_full)
        backward = contract_last(flat_grads, down_full)
        active, derivative = silu_parts(gate_value)
        hidden = active * upward
        part_weight = jnp.sum(hidden * backward, axis=1).astype(jnp.bfloat16)
        grad_up = (scale_column * backward * active).astype(jnp.bfloat16)
        grad_gate = (scale_column * backward * upward * derivative).astype(jnp.bfloat16)
        grad_pair = jnp.concatenate([grad_gate, grad_up], axis=1)
        part_rows = jnp.dot(grad_pair, paired_weights, preferred_element_type=jnp.float32).astype(
            jnp.bfloat16
        )
        hidden_scaled = (hidden * scale_column).astype(jnp.bfloat16)
        kept_list.append((grad_pair, hidden_scaled, flat_rows, flat_grads))
        rows_back = to_owners(
            reduce_quad(part_rows.reshape(-1, groups, capacity, feature_count))
        )
        weights_back = weights_to_owners(
            reduce_quad(part_weight.reshape(-1, groups, capacity))
        )
        (
            finish_inputs,
            finish_scales,
            finish_normed,
            finish_places,
            finish_selector,
            finish_keeping,
            finish_weight_slots,
        ) = current
        summed = rows_back.reshape(slot_count, feature_count)
        weight_sums = weights_back.reshape(slot_count)
        expert_rows = jnp.sum(
            jnp.take(summed, finish_places, axis=0).reshape(token_rows, pick_count, feature_count),
            axis=1,
        )
        combine_grad = (
            jnp.take(weight_sums, finish_places) * finish_keeping.astype(jnp.float32)
        ).reshape(token_rows, pick_count)
        gained = gain_row * expert_rows
        mixed_mean = jnp.mean(finish_inputs * gained, axis=1, keepdims=True)
        leaving = (
            incoming.astype(jnp.float32)
            + finish_scales * gained
            - finish_inputs * (finish_scales * finish_scales * finish_scales) * mixed_mean
        ).astype(jnp.bfloat16)
        previous = leaving
        leaving_list.append(leaving)
        combine_list.append(combine_grad)
    pair_all = jnp.concatenate([kept[0] for kept in kept_list], axis=0)
    scaled_all = jnp.concatenate([kept[1] for kept in kept_list], axis=0)
    rows_all = jnp.concatenate([kept[2] for kept in kept_list], axis=0)
    grads_all = jnp.concatenate([kept[3] for kept in kept_list], axis=0)
    pair_total = contract_first(pair_all, rows_all).reshape(2, hidden_count, feature_count)
    down_total = contract_first(scaled_all, grads_all)[None]
    pair_reduced, down_reduced = (
        lax.psum_scatter(
            pair_total.astype(jnp.bfloat16), "dp", scatter_dimension=2, tiled=True
        ).astype(jnp.float32),
        lax.psum_scatter(
            down_total.astype(jnp.bfloat16), "dp", scatter_dimension=2, tiled=True
        ).astype(jnp.float32),
    )
    return (
        jnp.stack(leaving_list)[None],
        jnp.stack(combine_list)[None],
        pair_reduced[0:1].astype(jnp.bfloat16),
        pair_reduced[1:2].astype(jnp.bfloat16),
        down_reduced.astype(jnp.bfloat16),
    )


def solution(mesh):
    sizes = dict(zip(mesh.axis_names, mesh.devices.shape))
    members = sizes["expert"]
    grid = mesh.devices.reshape(sizes["pipe"], members // HSPLIT, HSPLIT, sizes["dp"])
    fine = Mesh(grid, ("pipe", "eg", "ej", "dp"))
    tokens = ("eg", "ej", "dp")
    rows = ("eg", "ej")
    in_specs = (
        P("pipe", None, tokens, None),
        P(None, tokens, None),
        P("pipe", tokens, None),
        P("pipe", None),
        P("pipe", None, tokens, None),
        P("pipe", None, tokens, None),
        P("pipe", None, tokens, None),
        P("pipe", rows, "dp"),
        P("pipe", rows, "dp"),
        P("pipe", rows, "dp"),
    )
    out_specs = (
        P("pipe", None, tokens, None),
        P("pipe", None, tokens, None),
        P("pipe", rows, "dp"),
        P("pipe", rows, "dp"),
        P("pipe", rows, "dp"),
    )
    return jax.shard_map(local, mesh=fine, in_specs=in_specs, out_specs=out_specs, check_vma=False)
```

```python
import jax
import jax.numpy as jnp
from jax import lax
from jax.sharding import Mesh, PartitionSpec as P

HSPLIT = 4


EPSILON = 1e-06


def shifted(block, axis, distance):
    devices = range(lax.axis_size(axis))
    route = [(i - distance, i) for i in devices if i - distance in devices]
    return lax.ppermute(block, axis, route)


def rotated(block, axis, distance):
    size = lax.axis_size(axis)
    route = [(i, (i + distance) % size) for i in range(size)]
    return lax.ppermute(block, axis, route)


def flipped(block, axis, mask):
    size = lax.axis_size(axis)
    route = [(i, i ^ mask) for i in range(size)]
    return lax.ppermute(block, axis, route)


def silu_parts(gate_value):
    sigmoid_value = jax.nn.sigmoid(gate_value)
    return (gate_value * sigmoid_value, sigmoid_value * (1.0 + gate_value * (1.0 - sigmoid_value)))


def contract_last(first_operand, second_operand):
    return lax.dot_general(
        first_operand, second_operand, (((1,), (1,)), ((), ())), preferred_element_type=jnp.float32
    )


def contract_first(first_operand, second_operand):
    return lax.dot_general(
        first_operand, second_operand, (((0,), (0,)), ((), ())), preferred_element_type=jnp.float32
    )


def to_experts(blocks):
    groups = blocks.shape[0]
    moved = [blocks[0]] + [rotated(blocks[s], "eg", s) for s in range(1, groups)]
    return jnp.stack(moved)


def to_owners(blocks, weights):
    groups, capacity, width = blocks.shape
    rows = [blocks[0]]
    sums = [weights[0]]
    for s in range(1, groups):
        high = weights[s].astype(jnp.bfloat16)
        low = (weights[s] - high.astype(jnp.float32)).astype(jnp.bfloat16)
        packed = jnp.pad(jnp.stack([high, low]), ((0, 0), (0, width - capacity)))
        block = jnp.concatenate([blocks[s].astype(jnp.bfloat16), packed], axis=0)
        got = rotated(block, "eg", -s).astype(jnp.float32)
        rows.append(got[:capacity])
        sums.append(got[capacity, :capacity] + got[capacity + 1, :capacity])
    return jnp.stack(rows), jnp.stack(sums)


def relayed(block):
    width = block.shape[-1]
    return lax.axis_size("ej") == 4 and width >= 256 and width % 256 == 0


def gather_quad(blocks):
    staged = to_experts(blocks)
    quad = lax.axis_size("ej")
    if not relayed(staged):
        return jnp.stack([staged] + [flipped(staged, "ej", t) for t in range(1, quad)])
    half = staged.shape[-1] // 2
    first = flipped(staged, "ej", 1)
    second = flipped(staged, "ej", 2)
    diagonal = jnp.concatenate(
        [flipped(first[..., :half], "ej", 2), flipped(second[..., half:], "ej", 1)], axis=-1
    )
    return jnp.stack([staged, first, second, diagonal])


def reduce_quad(parts):
    quad = parts.shape[0]
    total = parts[0].astype(jnp.float32)
    if not relayed(parts):
        for t in range(1, quad):
            total = total + flipped(parts[t], "ej", t).astype(jnp.float32)
        return total
    half = parts.shape[-1] // 2
    from_first = flipped(parts[3][..., :half], "ej", 1).astype(jnp.float32)
    from_second = flipped(parts[3][..., half:], "ej", 2).astype(jnp.float32)
    toward_second = jnp.concatenate(
        [(parts[2][..., :half].astype(jnp.float32) + from_first).astype(parts.dtype), parts[2][..., half:]],
        axis=-1,
    )
    toward_first = jnp.concatenate(
        [parts[1][..., :half], (parts[1][..., half:].astype(jnp.float32) + from_second).astype(parts.dtype)],
        axis=-1,
    )
    total = total + flipped(toward_second, "ej", 2).astype(jnp.float32)
    return total + flipped(toward_first, "ej", 1).astype(jnp.float32)


def local(
    saved_inputs,
    output_grads,
    entry_grads,
    norm_gain,
    expert_ids,
    keep_flags,
    combine_weights,
    gate_weight,
    up_weight,
    down_weight,
):
    sections = lax.axis_size("pipe")
    is_last = lax.axis_index("pipe") == sections - 1
    groups = lax.axis_size("eg")
    me = lax.axis_index("eg")
    micro_count = saved_inputs.shape[1]
    token_rows = saved_inputs.shape[2]
    feature_count = saved_inputs.shape[3]
    pick_count = expert_ids.shape[3]
    capacity = max(2, 3 * token_rows * pick_count // (2 * groups))
    slot_count = groups * capacity
    low_half = lax.axis_index("dp") == 0

    def whole_rows(stored):
        if lax.axis_size("dp") != 2:
            return lax.all_gather(stored, "dp", axis=1, tiled=True)
        partner = flipped(stored, "dp", 1)
        return jnp.where(
            low_half,
            jnp.concatenate([stored, partner], axis=1),
            jnp.concatenate([partner, stored], axis=1),
        )

    gate_full, up_full, down_full = (
        whole_rows(gate_weight[0]),
        whole_rows(up_weight[0]),
        whole_rows(down_weight[0]),
    )
    hidden_count = gate_full.shape[0]
    paired_weights = jnp.concatenate([gate_full, up_full], axis=0)
    gain_row = norm_gain[0][None, :]
    slot_ids = jnp.arange(slot_count, dtype=jnp.int32)
    expert_range = jnp.arange(groups, dtype=jnp.int32)

    def prepare(moment):
        inputs = saved_inputs[0, moment].astype(jnp.float32)
        scales = lax.rsqrt(jnp.mean(inputs * inputs, axis=1, keepdims=True) + EPSILON)
        normed = (inputs * scales * gain_row).astype(jnp.bfloat16)
        chosen = expert_ids[0, moment].reshape(-1)
        onehot = (chosen[:, None] == expert_range[None, :]).astype(jnp.int32)
        rank_values = jnp.sum((jnp.cumsum(onehot, axis=0) - 1) * onehot, axis=1)
        places = ((chosen - me) % groups) * capacity + rank_values
        placing = places[:, None] == slot_ids[None, :]
        token_map = jnp.any(placing.reshape(token_rows, pick_count, slot_count), axis=1)
        selector = token_map.T.astype(jnp.bfloat16)
        keeping = keep_flags[0, moment].reshape(-1)
        scaled = (combine_weights[0, moment].reshape(-1) * keeping.astype(jnp.bfloat16)).astype(
            jnp.float32
        )
        weight_slots = jnp.sum(jnp.where(placing, scaled[:, None], 0.0), axis=0).astype(
            jnp.bfloat16
        )
        return (inputs, scales, normed, places, selector, keeping, weight_slots)

    def dispatch_rows(selector, source_rows):
        picked = jnp.dot(selector, source_rows, preferred_element_type=jnp.float32)
        return picked.astype(jnp.bfloat16).reshape(groups, capacity, feature_count)

    prepared = [prepare(moment) for moment in range(micro_count)]
    first_incoming = jnp.where(is_last, output_grads[0], entry_grads[0])
    first_grads = gather_quad(dispatch_rows(prepared[0][4], first_incoming))
    rows_gathered = [gather_quad(dispatch_rows(prepared[0][4], prepared[0][2]))]
    weights_gathered = [gather_quad(prepared[0][6].reshape(groups, capacity))]
    for current in prepared[1:]:
        later_rows, later_weights, _ = lax.optimization_barrier(
            (dispatch_rows(current[4], current[2]), current[6], first_grads)
        )
        rows_gathered.append(gather_quad(later_rows))
        weights_gathered.append(gather_quad(later_weights.reshape(groups, capacity)))
    leaving_list = []
    combine_list = []
    kept_list = []
    previous = entry_grads[0]
    for moment in range(micro_count):
        current = prepared[moment]
        if moment == 0:
            incoming = first_incoming
            grads_in = first_grads
        else:
            arriving = shifted(previous, "pipe", -1)
            incoming = jnp.where(is_last, output_grads[moment], arriving)
            grads_in = gather_quad(dispatch_rows(current[4], incoming))
        flat_rows = rows_gathered[moment].reshape(-1, feature_count)
        flat_grads = grads_in.reshape(-1, feature_count)
        scale_column = weights_gathered[moment].reshape(-1, 1).astype(jnp.float32)
        gate_value = contract_last(flat_rows, gate_full)
        upward = contract_last(flat_rows, up_full)
        backward = contract_last(flat_grads, down_full)
        active, derivative = silu_parts(gate_value)
        hidden = active * upward
        part_weight = jnp.sum(hidden * backward, axis=1).astype(jnp.bfloat16)
        grad_up = (scale_column * backward * active).astype(jnp.bfloat16)
        grad_gate = (scale_column * backward * upward * derivative).astype(jnp.bfloat16)
        grad_pair = jnp.concatenate([grad_gate, grad_up], axis=1)
        part_rows = jnp.dot(grad_pair, paired_weights, preferred_element_type=jnp.float32).astype(
            jnp.bfloat16
        )
        hidden_scaled = (hidden * scale_column).astype(jnp.bfloat16)
        kept_list.append((grad_pair, hidden_scaled, flat_rows, flat_grads))
        rows_back, weights_back = to_owners(
            reduce_quad(part_rows.reshape(-1, groups, capacity, feature_count)),
            reduce_quad(part_weight.reshape(-1, groups, capacity)),
        )
        (
            finish_inputs,
            finish_scales,
            finish_normed,
            finish_places,
            finish_selector,
            finish_keeping,
            finish_weight_slots,
        ) = current
        summed = rows_back.reshape(slot_count, feature_count)
        weight_sums = weights_back.reshape(slot_count)
        expert_rows = jnp.sum(
            jnp.take(summed, finish_places, axis=0).reshape(token_rows, pick_count, feature_count),
            axis=1,
        )
        combine_grad = (
            jnp.take(weight_sums, finish_places) * finish_keeping.astype(jnp.float32)
        ).reshape(token_rows, pick_count)
        gained = gain_row * expert_rows
        mixed_mean = jnp.mean(finish_inputs * gained, axis=1, keepdims=True)
        leaving = (
            incoming.astype(jnp.float32)
            + finish_scales * gained
            - finish_inputs * (finish_scales * finish_scales * finish_scales) * mixed_mean
        ).astype(jnp.bfloat16)
        previous = leaving
        leaving_list.append(leaving)
        combine_list.append(combine_grad)
    pair_all = jnp.concatenate([kept[0] for kept in kept_list], axis=0)
    scaled_all = jnp.concatenate([kept[1] for kept in kept_list], axis=0)
    rows_all = jnp.concatenate([kept[2] for kept in kept_list], axis=0)
    grads_all = jnp.concatenate([kept[3] for kept in kept_list], axis=0)
    pair_total = contract_first(pair_all, rows_all).reshape(2, hidden_count, feature_count)
    down_total = contract_first(scaled_all, grads_all)[None]
    pair_reduced, down_reduced = (
        lax.psum_scatter(
            pair_total.astype(jnp.bfloat16), "dp", scatter_dimension=2, tiled=True
        ).astype(jnp.float32),
        lax.psum_scatter(
            down_total.astype(jnp.bfloat16), "dp", scatter_dimension=2, tiled=True
        ).astype(jnp.float32),
    )
    return (
        jnp.stack(leaving_list)[None],
        jnp.stack(combine_list)[None],
        pair_reduced[0:1].astype(jnp.bfloat16),
        pair_reduced[1:2].astype(jnp.bfloat16),
        down_reduced.astype(jnp.bfloat16),
    )


def solution(mesh):
    sizes = dict(zip(mesh.axis_names, mesh.devices.shape))
    members = sizes["expert"]
    grid = mesh.devices.reshape(sizes["pipe"], members // HSPLIT, HSPLIT, sizes["dp"])
    fine = Mesh(grid, ("pipe", "eg", "ej", "dp"))
    tokens = ("eg", "ej", "dp")
    rows = ("eg", "ej")
    in_specs = (
        P("pipe", None, tokens, None),
        P(None, tokens, None),
        P("pipe", tokens, None),
        P("pipe", None),
        P("pipe", None, tokens, None),
        P("pipe", None, tokens, None),
        P("pipe", None, tokens, None),
        P("pipe", rows, "dp"),
        P("pipe", rows, "dp"),
        P("pipe", rows, "dp"),
    )
    out_specs = (
        P("pipe", None, tokens, None),
        P("pipe", None, tokens, None),
        P("pipe", rows, "dp"),
        P("pipe", rows, "dp"),
        P("pipe", rows, "dp"),
    )
    return jax.shard_map(local, mesh=fine, in_specs=in_specs, out_specs=out_specs, check_vma=False)
```

```python
import jax
import jax.numpy as jnp
from jax import lax
from jax.sharding import Mesh, PartitionSpec as P

HSPLIT = 4


EPSILON = 1e-06


def shifted(block, axis, distance):
    devices = range(lax.axis_size(axis))
    route = [(i - distance, i) for i in devices if i - distance in devices]
    return lax.ppermute(block, axis, route)


def rotated(block, axis, distance):
    size = lax.axis_size(axis)
    route = [(i, (i + distance) % size) for i in range(size)]
    return lax.ppermute(block, axis, route)


def flipped(block, axis, mask):
    size = lax.axis_size(axis)
    route = [(i, i ^ mask) for i in range(size)]
    return lax.ppermute(block, axis, route)


def silu_parts(gate_value):
    sigmoid_value = jax.nn.sigmoid(gate_value)
    return (gate_value * sigmoid_value, sigmoid_value * (1.0 + gate_value * (1.0 - sigmoid_value)))


def contract_last(first_operand, second_operand):
    return lax.dot_general(
        first_operand, second_operand, (((1,), (1,)), ((), ())), preferred_element_type=jnp.float32
    )


def contract_first(first_operand, second_operand):
    return lax.dot_general(
        first_operand, second_operand, (((0,), (0,)), ((), ())), preferred_element_type=jnp.float32
    )


def rows_and_weights(blocks, weights):
    groups, capacity, width = blocks.shape
    rows = [blocks[0]]
    kept = [weights[0]]
    for s in range(1, groups):
        extra = jnp.pad(weights[s][None, :], ((0, 0), (0, width - capacity)))
        got = rotated(jnp.concatenate([blocks[s], extra], axis=0), "eg", s)
        rows.append(got[:capacity])
        kept.append(got[capacity, :capacity])
    return quad_of(jnp.stack(rows)), quad_of(jnp.stack(kept))


def to_experts(blocks):
    groups = blocks.shape[0]
    moved = [blocks[0]] + [rotated(blocks[s], "eg", s) for s in range(1, groups)]
    return jnp.stack(moved)


def to_owners(blocks, weights):
    groups, capacity, width = blocks.shape
    rows = [blocks[0]]
    sums = [weights[0]]
    for s in range(1, groups):
        high = weights[s].astype(jnp.bfloat16)
        low = (weights[s] - high.astype(jnp.float32)).astype(jnp.bfloat16)
        packed = jnp.pad(jnp.stack([high, low]), ((0, 0), (0, width - capacity)))
        block = jnp.concatenate([blocks[s].astype(jnp.bfloat16), packed], axis=0)
        got = rotated(block, "eg", -s).astype(jnp.float32)
        rows.append(got[:capacity])
        sums.append(got[capacity, :capacity] + got[capacity + 1, :capacity])
    return jnp.stack(rows), jnp.stack(sums)


def relayed(block):
    width = block.shape[-1]
    return lax.axis_size("ej") == 4 and width >= 256 and width % 256 == 0


def gather_quad(blocks):
    return quad_of(to_experts(blocks))


def quad_of(staged):
    quad = lax.axis_size("ej")
    if not relayed(staged):
        return jnp.stack([staged] + [flipped(staged, "ej", t) for t in range(1, quad)])
    half = staged.shape[-1] // 2
    first = flipped(staged, "ej", 1)
    second = flipped(staged, "ej", 2)
    diagonal = jnp.concatenate(
        [flipped(first[..., :half], "ej", 2), flipped(second[..., half:], "ej", 1)], axis=-1
    )
    return jnp.stack([staged, first, second, diagonal])


def reduce_quad(parts):
    quad = parts.shape[0]
    total = parts[0].astype(jnp.float32)
    if not relayed(parts):
        for t in range(1, quad):
            total = total + flipped(parts[t], "ej", t).astype(jnp.float32)
        return total
    half = parts.shape[-1] // 2
    from_first = flipped(parts[3][..., :half], "ej", 1).astype(jnp.float32)
    from_second = flipped(parts[3][..., half:], "ej", 2).astype(jnp.float32)
    toward_second = jnp.concatenate(
        [(parts[2][..., :half].astype(jnp.float32) + from_first).astype(parts.dtype), parts[2][..., half:]],
        axis=-1,
    )
    toward_first = jnp.concatenate(
        [parts[1][..., :half], (parts[1][..., half:].astype(jnp.float32) + from_second).astype(parts.dtype)],
        axis=-1,
    )
    total = total + flipped(toward_second, "ej", 2).astype(jnp.float32)
    return total + flipped(toward_first, "ej", 1).astype(jnp.float32)


def local(
    saved_inputs,
    output_grads,
    entry_grads,
    norm_gain,
    expert_ids,
    keep_flags,
    combine_weights,
    gate_weight,
    up_weight,
    down_weight,
):
    sections = lax.axis_size("pipe")
    is_last = lax.axis_index("pipe") == sections - 1
    groups = lax.axis_size("eg")
    me = lax.axis_index("eg")
    micro_count = saved_inputs.shape[1]
    token_rows = saved_inputs.shape[2]
    feature_count = saved_inputs.shape[3]
    pick_count = expert_ids.shape[3]
    capacity = max(2, 3 * token_rows * pick_count // (2 * groups))
    slot_count = groups * capacity
    low_half = lax.axis_index("dp") == 0

    def whole_rows(stored):
        if lax.axis_size("dp") != 2:
            return lax.all_gather(stored, "dp", axis=1, tiled=True)
        partner = flipped(stored, "dp", 1)
        return jnp.where(
            low_half,
            jnp.concatenate([stored, partner], axis=1),
            jnp.concatenate([partner, stored], axis=1),
        )

    gate_full, up_full, down_full = (
        whole_rows(gate_weight[0]),
        whole_rows(up_weight[0]),
        whole_rows(down_weight[0]),
    )
    hidden_count = gate_full.shape[0]
    paired_weights = jnp.concatenate([gate_full, up_full], axis=0)
    gain_row = norm_gain[0][None, :]
    slot_ids = jnp.arange(slot_count, dtype=jnp.int32)
    expert_range = jnp.arange(groups, dtype=jnp.int32)

    def prepare(moment):
        inputs = saved_inputs[0, moment].astype(jnp.float32)
        scales = lax.rsqrt(jnp.mean(inputs * inputs, axis=1, keepdims=True) + EPSILON)
        normed = (inputs * scales * gain_row).astype(jnp.bfloat16)
        chosen = expert_ids[0, moment].reshape(-1)
        onehot = (chosen[:, None] == expert_range[None, :]).astype(jnp.int32)
        rank_values = jnp.sum((jnp.cumsum(onehot, axis=0) - 1) * onehot, axis=1)
        places = ((chosen - me) % groups) * capacity + rank_values
        placing = places[:, None] == slot_ids[None, :]
        token_map = jnp.any(placing.reshape(token_rows, pick_count, slot_count), axis=1)
        selector = token_map.T.astype(jnp.bfloat16)
        keeping = keep_flags[0, moment].reshape(-1)
        scaled = (combine_weights[0, moment].reshape(-1) * keeping.astype(jnp.bfloat16)).astype(
            jnp.float32
        )
        weight_slots = jnp.sum(jnp.where(placing, scaled[:, None], 0.0), axis=0).astype(
            jnp.bfloat16
        )
        return (inputs, scales, normed, places, selector, keeping, weight_slots)

    def dispatch_rows(selector, source_rows):
        picked = jnp.dot(selector, source_rows, preferred_element_type=jnp.float32)
        return picked.astype(jnp.bfloat16).reshape(groups, capacity, feature_count)

    prepared = [prepare(moment) for moment in range(micro_count)]
    first_incoming = jnp.where(is_last, output_grads[0], entry_grads[0])
    first_grads = gather_quad(dispatch_rows(prepared[0][4], first_incoming))
    first_rows, first_weights = rows_and_weights(
        dispatch_rows(prepared[0][4], prepared[0][2]), prepared[0][6].reshape(groups, capacity)
    )
    rows_gathered = [first_rows]
    weights_gathered = [first_weights]
    for current in prepared[1:]:
        later_rows, later_weights, _ = lax.optimization_barrier(
            (dispatch_rows(current[4], current[2]), current[6], first_grads)
        )
        later_gathered = rows_and_weights(later_rows, later_weights.reshape(groups, capacity))
        rows_gathered.append(later_gathered[0])
        weights_gathered.append(later_gathered[1])
    leaving_list = []
    combine_list = []
    kept_list = []
    previous = entry_grads[0]
    for moment in range(micro_count):
        current = prepared[moment]
        if moment == 0:
            incoming = first_incoming
            grads_in = first_grads
        else:
            arriving = shifted(previous, "pipe", -1)
            incoming = jnp.where(is_last, output_grads[moment], arriving)
            grads_in = gather_quad(dispatch_rows(current[4], incoming))
        flat_rows = rows_gathered[moment].reshape(-1, feature_count)
        flat_grads = grads_in.reshape(-1, feature_count)
        scale_column = weights_gathered[moment].reshape(-1, 1).astype(jnp.float32)
        gate_value = contract_last(flat_rows, gate_full)
        upward = contract_last(flat_rows, up_full)
        backward = contract_last(flat_grads, down_full)
        active, derivative = silu_parts(gate_value)
        hidden = active * upward
        part_weight = jnp.sum(hidden * backward, axis=1).astype(jnp.bfloat16)
        grad_up = (scale_column * backward * active).astype(jnp.bfloat16)
        grad_gate = (scale_column * backward * upward * derivative).astype(jnp.bfloat16)
        grad_pair = jnp.concatenate([grad_gate, grad_up], axis=1)
        part_rows = jnp.dot(grad_pair, paired_weights, preferred_element_type=jnp.float32).astype(
            jnp.bfloat16
        )
        hidden_scaled = (hidden * scale_column).astype(jnp.bfloat16)
        kept_list.append((grad_pair, hidden_scaled, flat_rows, flat_grads))
        rows_back, weights_back = to_owners(
            reduce_quad(part_rows.reshape(-1, groups, capacity, feature_count)),
            reduce_quad(part_weight.reshape(-1, groups, capacity)),
        )
        (
            finish_inputs,
            finish_scales,
            finish_normed,
            finish_places,
            finish_selector,
            finish_keeping,
            finish_weight_slots,
        ) = current
        summed = rows_back.reshape(slot_count, feature_count)
        weight_sums = weights_back.reshape(slot_count)
        expert_rows = jnp.sum(
            jnp.take(summed, finish_places, axis=0).reshape(token_rows, pick_count, feature_count),
            axis=1,
        )
        combine_grad = (
            jnp.take(weight_sums, finish_places) * finish_keeping.astype(jnp.float32)
        ).reshape(token_rows, pick_count)
        gained = gain_row * expert_rows
        mixed_mean = jnp.mean(finish_inputs * gained, axis=1, keepdims=True)
        leaving = (
            incoming.astype(jnp.float32)
            + finish_scales * gained
            - finish_inputs * (finish_scales * finish_scales * finish_scales) * mixed_mean
        ).astype(jnp.bfloat16)
        previous = leaving
        leaving_list.append(leaving)
        combine_list.append(combine_grad)
    pair_all = jnp.concatenate([kept[0] for kept in kept_list], axis=0)
    scaled_all = jnp.concatenate([kept[1] for kept in kept_list], axis=0)
    rows_all = jnp.concatenate([kept[2] for kept in kept_list], axis=0)
    grads_all = jnp.concatenate([kept[3] for kept in kept_list], axis=0)
    pair_total = contract_first(pair_all, rows_all).reshape(2, hidden_count, feature_count)
    down_total = contract_first(scaled_all, grads_all)[None]
    pair_reduced, down_reduced = (
        lax.psum_scatter(
            pair_total.astype(jnp.bfloat16), "dp", scatter_dimension=2, tiled=True
        ).astype(jnp.float32),
        lax.psum_scatter(
            down_total.astype(jnp.bfloat16), "dp", scatter_dimension=2, tiled=True
        ).astype(jnp.float32),
    )
    return (
        jnp.stack(leaving_list)[None],
        jnp.stack(combine_list)[None],
        pair_reduced[0:1].astype(jnp.bfloat16),
        pair_reduced[1:2].astype(jnp.bfloat16),
        down_reduced.astype(jnp.bfloat16),
    )


def solution(mesh):
    sizes = dict(zip(mesh.axis_names, mesh.devices.shape))
    members = sizes["expert"]
    grid = mesh.devices.reshape(sizes["pipe"], members // HSPLIT, HSPLIT, sizes["dp"])
    fine = Mesh(grid, ("pipe", "eg", "ej", "dp"))
    tokens = ("eg", "ej", "dp")
    rows = ("eg", "ej")
    in_specs = (
        P("pipe", None, tokens, None),
        P(None, tokens, None),
        P("pipe", tokens, None),
        P("pipe", None),
        P("pipe", None, tokens, None),
        P("pipe", None, tokens, None),
        P("pipe", None, tokens, None),
        P("pipe", rows, "dp"),
        P("pipe", rows, "dp"),
        P("pipe", rows, "dp"),
    )
    out_specs = (
        P("pipe", None, tokens, None),
        P("pipe", None, tokens, None),
        P("pipe", rows, "dp"),
        P("pipe", rows, "dp"),
        P("pipe", rows, "dp"),
    )
    return jax.shard_map(local, mesh=fine, in_specs=in_specs, out_specs=out_specs, check_vma=False)
```

```python
import jax
import jax.numpy as jnp
from jax import lax
from jax.sharding import Mesh, PartitionSpec as P

HSPLIT = 4


EPSILON = 1e-06


def shifted(block, axis, distance):
    devices = range(lax.axis_size(axis))
    route = [(i - distance, i) for i in devices if i - distance in devices]
    return lax.ppermute(block, axis, route)


def rotated(block, axis, distance):
    size = lax.axis_size(axis)
    route = [(i, (i + distance) % size) for i in range(size)]
    return lax.ppermute(block, axis, route)


def flipped(block, axis, mask):
    size = lax.axis_size(axis)
    route = [(i, i ^ mask) for i in range(size)]
    return lax.ppermute(block, axis, route)


def silu_parts(gate_value):
    sigmoid_value = jax.nn.sigmoid(gate_value)
    return (gate_value * sigmoid_value, sigmoid_value * (1.0 + gate_value * (1.0 - sigmoid_value)))


def contract_last(first_operand, second_operand):
    return lax.dot_general(
        first_operand, second_operand, (((1,), (1,)), ((), ())), preferred_element_type=jnp.float32
    )


def contract_first(first_operand, second_operand):
    return lax.dot_general(
        first_operand, second_operand, (((0,), (0,)), ((), ())), preferred_element_type=jnp.float32
    )


def to_experts(blocks):
    groups = blocks.shape[0]
    moved = [blocks[0]] + [rotated(blocks[s], "eg", s) for s in range(1, groups)]
    return jnp.stack(moved)


def to_owners(blocks, weights):
    groups, capacity, width = blocks.shape
    rows = [blocks[0]]
    sums = [weights[0]]
    for s in range(1, groups):
        high = weights[s].astype(jnp.bfloat16)
        low = (weights[s] - high.astype(jnp.float32)).astype(jnp.bfloat16)
        packed = jnp.pad(jnp.stack([high, low]), ((0, 0), (0, width - capacity)))
        block = jnp.concatenate([blocks[s].astype(jnp.bfloat16), packed], axis=0)
        got = rotated(block, "eg", -s).astype(jnp.float32)
        rows.append(got[:capacity])
        sums.append(got[capacity, :capacity] + got[capacity + 1, :capacity])
    return jnp.stack(rows), jnp.stack(sums)


def relayed(block):
    width = block.shape[-1]
    return lax.axis_size("ej") == 4 and width >= 256 and width % 256 == 0


def gather_quad(blocks):
    staged = to_experts(blocks)
    quad = lax.axis_size("ej")
    if not relayed(staged):
        return jnp.stack([staged] + [flipped(staged, "ej", t) for t in range(1, quad)])
    half = staged.shape[-1] // 2
    first = flipped(staged, "ej", 1)
    second = flipped(staged, "ej", 2)
    diagonal = jnp.concatenate(
        [flipped(first[..., :half], "ej", 2), flipped(second[..., half:], "ej", 1)], axis=-1
    )
    return jnp.stack([staged, first, second, diagonal])


def reduce_quad(parts):
    quad = parts.shape[0]
    total = parts[0].astype(jnp.float32)
    if not relayed(parts):
        for t in range(1, quad):
            total = total + flipped(parts[t], "ej", t).astype(jnp.float32)
        return total
    half = parts.shape[-1] // 2
    from_first = flipped(parts[3][..., :half], "ej", 1).astype(jnp.float32)
    from_second = flipped(parts[3][..., half:], "ej", 2).astype(jnp.float32)
    toward_second = jnp.concatenate(
        [(parts[2][..., :half].astype(jnp.float32) + from_first).astype(parts.dtype), parts[2][..., half:]],
        axis=-1,
    )
    toward_first = jnp.concatenate(
        [parts[1][..., :half], (parts[1][..., half:].astype(jnp.float32) + from_second).astype(parts.dtype)],
        axis=-1,
    )
    total = total + flipped(toward_second, "ej", 2).astype(jnp.float32)
    return total + flipped(toward_first, "ej", 1).astype(jnp.float32)


def local(
    saved_inputs,
    output_grads,
    entry_grads,
    norm_gain,
    expert_ids,
    keep_flags,
    combine_weights,
    gate_weight,
    up_weight,
    down_weight,
):
    sections = lax.axis_size("pipe")
    is_last = lax.axis_index("pipe") == sections - 1
    groups = lax.axis_size("eg")
    me = lax.axis_index("eg")
    micro_count = saved_inputs.shape[1]
    token_rows = saved_inputs.shape[2]
    feature_count = saved_inputs.shape[3]
    pick_count = expert_ids.shape[3]
    capacity = max(2, 3 * token_rows * pick_count // (2 * groups))
    slot_count = groups * capacity
    low_half = lax.axis_index("dp") == 0

    def whole_rows(stored):
        if lax.axis_size("dp") != 2:
            return lax.all_gather(stored, "dp", axis=1, tiled=True)
        partner = flipped(stored, "dp", 1)
        return jnp.where(
            low_half,
            jnp.concatenate([stored, partner], axis=1),
            jnp.concatenate([partner, stored], axis=1),
        )

    gate_full, up_full, down_full = (
        whole_rows(gate_weight[0]),
        whole_rows(up_weight[0]),
        whole_rows(down_weight[0]),
    )
    hidden_count = gate_full.shape[0]
    paired_weights = jnp.concatenate([gate_full, up_full], axis=0)
    gain_row = norm_gain[0][None, :]
    slot_ids = jnp.arange(slot_count, dtype=jnp.int32)
    expert_range = jnp.arange(groups, dtype=jnp.int32)

    def prepare(moment):
        inputs = saved_inputs[0, moment].astype(jnp.float32)
        scales = lax.rsqrt(jnp.mean(inputs * inputs, axis=1, keepdims=True) + EPSILON)
        normed = (inputs * scales * gain_row).astype(jnp.bfloat16)
        chosen = expert_ids[0, moment].reshape(-1)
        onehot = (chosen[:, None] == expert_range[None, :]).astype(jnp.int32)
        rank_values = jnp.sum((jnp.cumsum(onehot, axis=0) - 1) * onehot, axis=1)
        places = ((chosen - me) % groups) * capacity + rank_values
        placing = places[:, None] == slot_ids[None, :]
        token_map = jnp.any(placing.reshape(token_rows, pick_count, slot_count), axis=1)
        selector = token_map.T.astype(jnp.bfloat16)
        keeping = keep_flags[0, moment].reshape(-1)
        scaled = (combine_weights[0, moment].reshape(-1) * keeping.astype(jnp.bfloat16)).astype(
            jnp.float32
        )
        weight_slots = jnp.sum(jnp.where(placing, scaled[:, None], 0.0), axis=0).astype(
            jnp.bfloat16
        )
        return (inputs, scales, normed, places, selector, keeping, weight_slots)

    def dispatch_rows(selector, source_rows):
        picked = jnp.dot(selector, source_rows, preferred_element_type=jnp.float32)
        return picked.astype(jnp.bfloat16).reshape(groups, capacity, feature_count)

    prepared = [prepare(moment) for moment in range(micro_count)]
    first_incoming = jnp.where(is_last, output_grads[0], entry_grads[0])
    first_grads = gather_quad(dispatch_rows(prepared[0][4], first_incoming))
    rows_gathered = [gather_quad(dispatch_rows(prepared[0][4], prepared[0][2]))]
    weights_gathered = [gather_quad(prepared[0][6].reshape(groups, capacity))]
    for current in prepared[1:]:
        later_rows, later_weights, _ = lax.optimization_barrier(
            (dispatch_rows(current[4], current[2]), current[6], first_grads)
        )
        rows_gathered.append(gather_quad(later_rows))
        weights_gathered.append(gather_quad(later_weights.reshape(groups, capacity)))
    leaving_list = []
    combine_list = []
    kept_list = []
    previous = entry_grads[0]
    for moment in range(micro_count):
        current = prepared[moment]
        if moment == 0:
            incoming = first_incoming
            grads_in = first_grads
        else:
            arriving = shifted(previous, "pipe", -1)
            incoming = jnp.where(is_last, output_grads[moment], arriving)
            grads_in = gather_quad(dispatch_rows(current[4], incoming))
        flat_rows = rows_gathered[moment].reshape(-1, feature_count)
        flat_grads = grads_in.reshape(-1, feature_count)
        scale_column = weights_gathered[moment].reshape(-1, 1).astype(jnp.float32)
        gate_value = contract_last(flat_rows, gate_full)
        upward = contract_last(flat_rows, up_full)
        backward = contract_last(flat_grads, down_full)
        active, derivative = silu_parts(gate_value)
        hidden = active * upward
        part_weight = jnp.sum(hidden * backward, axis=1).astype(jnp.bfloat16)
        grad_up = (scale_column * backward * active).astype(jnp.bfloat16)
        grad_gate = (scale_column * backward * upward * derivative).astype(jnp.bfloat16)
        grad_pair = jnp.concatenate([grad_gate, grad_up], axis=1)
        part_rows = jnp.dot(grad_pair, paired_weights, preferred_element_type=jnp.float32).astype(
            jnp.bfloat16
        )
        hidden_scaled = (hidden * scale_column).astype(jnp.bfloat16)
        kept_list.append((grad_pair, hidden_scaled, flat_rows, flat_grads))
        weight_rows = jnp.pad(
            part_weight.reshape(-1, groups, 1, capacity),
            ((0, 0), (0, 0), (0, 0), (0, feature_count - capacity)),
        )
        quad_total = reduce_quad(
            jnp.concatenate(
                [part_rows.reshape(-1, groups, capacity, feature_count), weight_rows], axis=2
            )
        )
        rows_back, weights_back = to_owners(
            quad_total[:, :capacity], quad_total[:, capacity, :capacity]
        )
        (
            finish_inputs,
            finish_scales,
            finish_normed,
            finish_places,
            finish_selector,
            finish_keeping,
            finish_weight_slots,
        ) = current
        summed = rows_back.reshape(slot_count, feature_count)
        weight_sums = weights_back.reshape(slot_count)
        expert_rows = jnp.sum(
            jnp.take(summed, finish_places, axis=0).reshape(token_rows, pick_count, feature_count),
            axis=1,
        )
        combine_grad = (
            jnp.take(weight_sums, finish_places) * finish_keeping.astype(jnp.float32)
        ).reshape(token_rows, pick_count)
        gained = gain_row * expert_rows
        mixed_mean = jnp.mean(finish_inputs * gained, axis=1, keepdims=True)
        leaving = (
            incoming.astype(jnp.float32)
            + finish_scales * gained
            - finish_inputs * (finish_scales * finish_scales * finish_scales) * mixed_mean
        ).astype(jnp.bfloat16)
        previous = leaving
        leaving_list.append(leaving)
        combine_list.append(combine_grad)
    pair_all = jnp.concatenate([kept[0] for kept in kept_list], axis=0)
    scaled_all = jnp.concatenate([kept[1] for kept in kept_list], axis=0)
    rows_all = jnp.concatenate([kept[2] for kept in kept_list], axis=0)
    grads_all = jnp.concatenate([kept[3] for kept in kept_list], axis=0)
    pair_total = contract_first(pair_all, rows_all).reshape(2, hidden_count, feature_count)
    down_total = contract_first(scaled_all, grads_all)[None]
    pair_reduced, down_reduced = (
        lax.psum_scatter(
            pair_total.astype(jnp.bfloat16), "dp", scatter_dimension=2, tiled=True
        ).astype(jnp.float32),
        lax.psum_scatter(
            down_total.astype(jnp.bfloat16), "dp", scatter_dimension=2, tiled=True
        ).astype(jnp.float32),
    )
    return (
        jnp.stack(leaving_list)[None],
        jnp.stack(combine_list)[None],
        pair_reduced[0:1].astype(jnp.bfloat16),
        pair_reduced[1:2].astype(jnp.bfloat16),
        down_reduced.astype(jnp.bfloat16),
    )


def solution(mesh):
    sizes = dict(zip(mesh.axis_names, mesh.devices.shape))
    members = sizes["expert"]
    grid = mesh.devices.reshape(sizes["pipe"], members // HSPLIT, HSPLIT, sizes["dp"])
    fine = Mesh(grid, ("pipe", "eg", "ej", "dp"))
    tokens = ("eg", "ej", "dp")
    rows = ("eg", "ej")
    in_specs = (
        P("pipe", None, tokens, None),
        P(None, tokens, None),
        P("pipe", tokens, None),
        P("pipe", None),
        P("pipe", None, tokens, None),
        P("pipe", None, tokens, None),
        P("pipe", None, tokens, None),
        P("pipe", rows, "dp"),
        P("pipe", rows, "dp"),
        P("pipe", rows, "dp"),
    )
    out_specs = (
        P("pipe", None, tokens, None),
        P("pipe", None, tokens, None),
        P("pipe", rows, "dp"),
        P("pipe", rows, "dp"),
        P("pipe", rows, "dp"),
    )
    return jax.shard_map(local, mesh=fine, in_specs=in_specs, out_specs=out_specs, check_vma=False)
```

```python
import jax
import jax.numpy as jnp
from jax import lax
from jax.sharding import Mesh, PartitionSpec as P

HSPLIT = 4


EPSILON = 1e-06


def shifted(block, axis, distance):
    devices = range(lax.axis_size(axis))
    route = [(i - distance, i) for i in devices if i - distance in devices]
    return lax.ppermute(block, axis, route)


def rotated(block, axis, distance):
    size = lax.axis_size(axis)
    route = [(i, (i + distance) % size) for i in range(size)]
    return lax.ppermute(block, axis, route)


def flipped(block, axis, mask):
    size = lax.axis_size(axis)
    route = [(i, i ^ mask) for i in range(size)]
    return lax.ppermute(block, axis, route)


def silu_parts(gate_value):
    sigmoid_value = jax.nn.sigmoid(gate_value)
    return (gate_value * sigmoid_value, sigmoid_value * (1.0 + gate_value * (1.0 - sigmoid_value)))


def contract_last(first_operand, second_operand):
    return lax.dot_general(
        first_operand, second_operand, (((1,), (1,)), ((), ())), preferred_element_type=jnp.float32
    )


def contract_first(first_operand, second_operand):
    return lax.dot_general(
        first_operand, second_operand, (((0,), (0,)), ((), ())), preferred_element_type=jnp.float32
    )


def to_experts(blocks):
    groups = blocks.shape[0]
    moved = [blocks[0]] + [rotated(blocks[s], "eg", s) for s in range(1, groups)]
    return jnp.stack(moved)


def to_owners(blocks, weights):
    groups, capacity, width = blocks.shape
    rows = [blocks[0]]
    sums = [weights[0]]
    for s in range(1, groups):
        high = weights[s].astype(jnp.bfloat16)
        low = (weights[s] - high.astype(jnp.float32)).astype(jnp.bfloat16)
        packed = jnp.pad(jnp.stack([high, low]), ((0, 0), (0, width - capacity)))
        block = jnp.concatenate([blocks[s].astype(jnp.bfloat16), packed], axis=0)
        got = rotated(block, "eg", -s).astype(jnp.float32)
        rows.append(got[:capacity])
        sums.append(got[capacity, :capacity] + got[capacity + 1, :capacity])
    return jnp.stack(rows), jnp.stack(sums)


def relayed(block):
    width = block.shape[-1]
    return lax.axis_size("ej") == 4 and width >= 256 and width % 256 == 0


def gather_quad(blocks):
    staged = to_experts(blocks)
    quad = lax.axis_size("ej")
    if not relayed(staged):
        return jnp.stack([staged] + [flipped(staged, "ej", t) for t in range(1, quad)])
    half = staged.shape[-1] // 2
    first = flipped(staged, "ej", 1)
    second = flipped(staged, "ej", 2)
    diagonal = jnp.concatenate(
        [flipped(first[..., :half], "ej", 2), flipped(second[..., half:], "ej", 1)], axis=-1
    )
    return jnp.stack([staged, first, second, diagonal])


def reduce_quad(parts):
    quad = parts.shape[0]
    total = parts[0].astype(jnp.float32)
    if not relayed(parts):
        for t in range(1, quad):
            total = total + flipped(parts[t], "ej", t).astype(jnp.float32)
        return total
    half = parts.shape[-1] // 2
    from_first = flipped(parts[3][..., :half], "ej", 1).astype(jnp.float32)
    from_second = flipped(parts[3][..., half:], "ej", 2).astype(jnp.float32)
    toward_second = jnp.concatenate(
        [(parts[2][..., :half].astype(jnp.float32) + from_first).astype(parts.dtype), parts[2][..., half:]],
        axis=-1,
    )
    toward_first = jnp.concatenate(
        [parts[1][..., :half], (parts[1][..., half:].astype(jnp.float32) + from_second).astype(parts.dtype)],
        axis=-1,
    )
    total = total + flipped(toward_second, "ej", 2).astype(jnp.float32)
    return total + flipped(toward_first, "ej", 1).astype(jnp.float32)


def local(
    saved_inputs,
    output_grads,
    entry_grads,
    norm_gain,
    expert_ids,
    keep_flags,
    combine_weights,
    gate_weight,
    up_weight,
    down_weight,
):
    sections = lax.axis_size("pipe")
    is_last = lax.axis_index("pipe") == sections - 1
    groups = lax.axis_size("eg")
    me = lax.axis_index("eg")
    micro_count = saved_inputs.shape[1]
    token_rows = saved_inputs.shape[2]
    feature_count = saved_inputs.shape[3]
    pick_count = expert_ids.shape[3]
    capacity = max(2, 3 * token_rows * pick_count // (2 * groups))
    slot_count = groups * capacity
    low_half = lax.axis_index("dp") == 0

    stored = jnp.stack([gate_weight[0], up_weight[0], down_weight[0]])
    if lax.axis_size("dp") == 2:
        partner = flipped(stored, "dp", 1)
        whole = jnp.where(
            low_half,
            jnp.concatenate([stored, partner], axis=2),
            jnp.concatenate([partner, stored], axis=2),
        )
    else:
        whole = lax.all_gather(stored, "dp", axis=2, tiled=True)
    gate_full, up_full, down_full = whole[0], whole[1], whole[2]
    hidden_count = gate_full.shape[0]
    paired_weights = jnp.concatenate([gate_full, up_full], axis=0)
    gain_row = norm_gain[0][None, :]
    slot_ids = jnp.arange(slot_count, dtype=jnp.int32)
    expert_range = jnp.arange(groups, dtype=jnp.int32)

    def prepare(moment):
        inputs = saved_inputs[0, moment].astype(jnp.float32)
        scales = lax.rsqrt(jnp.mean(inputs * inputs, axis=1, keepdims=True) + EPSILON)
        normed = (inputs * scales * gain_row).astype(jnp.bfloat16)
        chosen = expert_ids[0, moment].reshape(-1)
        onehot = (chosen[:, None] == expert_range[None, :]).astype(jnp.int32)
        rank_values = jnp.sum((jnp.cumsum(onehot, axis=0) - 1) * onehot, axis=1)
        places = ((chosen - me) % groups) * capacity + rank_values
        placing = places[:, None] == slot_ids[None, :]
        token_map = jnp.any(placing.reshape(token_rows, pick_count, slot_count), axis=1)
        selector = token_map.T.astype(jnp.bfloat16)
        keeping = keep_flags[0, moment].reshape(-1)
        scaled = (combine_weights[0, moment].reshape(-1) * keeping.astype(jnp.bfloat16)).astype(
            jnp.float32
        )
        weight_slots = jnp.sum(jnp.where(placing, scaled[:, None], 0.0), axis=0).astype(
            jnp.bfloat16
        )
        return (inputs, scales, normed, places, selector, keeping, weight_slots)

    def dispatch_rows(selector, source_rows):
        picked = jnp.dot(selector, source_rows, preferred_element_type=jnp.float32)
        return picked.astype(jnp.bfloat16).reshape(groups, capacity, feature_count)

    prepared = [prepare(moment) for moment in range(micro_count)]
    first_incoming = jnp.where(is_last, output_grads[0], entry_grads[0])
    first_grads = gather_quad(dispatch_rows(prepared[0][4], first_incoming))
    rows_gathered = [gather_quad(dispatch_rows(prepared[0][4], prepared[0][2]))]
    weights_gathered = [gather_quad(prepared[0][6].reshape(groups, capacity))]
    for current in prepared[1:]:
        later_rows, later_weights, _ = lax.optimization_barrier(
            (dispatch_rows(current[4], current[2]), current[6], first_grads)
        )
        rows_gathered.append(gather_quad(later_rows))
        weights_gathered.append(gather_quad(later_weights.reshape(groups, capacity)))
    leaving_list = []
    combine_list = []
    kept_list = []
    previous = entry_grads[0]
    for moment in range(micro_count):
        current = prepared[moment]
        if moment == 0:
            incoming = first_incoming
            grads_in = first_grads
        else:
            arriving = shifted(previous, "pipe", -1)
            incoming = jnp.where(is_last, output_grads[moment], arriving)
            grads_in = gather_quad(dispatch_rows(current[4], incoming))
        flat_rows = rows_gathered[moment].reshape(-1, feature_count)
        flat_grads = grads_in.reshape(-1, feature_count)
        scale_column = weights_gathered[moment].reshape(-1, 1).astype(jnp.float32)
        gate_value = contract_last(flat_rows, gate_full)
        upward = contract_last(flat_rows, up_full)
        backward = contract_last(flat_grads, down_full)
        active, derivative = silu_parts(gate_value)
        hidden = active * upward
        part_weight = jnp.sum(hidden * backward, axis=1).astype(jnp.bfloat16)
        grad_up = (scale_column * backward * active).astype(jnp.bfloat16)
        grad_gate = (scale_column * backward * upward * derivative).astype(jnp.bfloat16)
        grad_pair = jnp.concatenate([grad_gate, grad_up], axis=1)
        part_rows = jnp.dot(grad_pair, paired_weights, preferred_element_type=jnp.float32).astype(
            jnp.bfloat16
        )
        hidden_scaled = (hidden * scale_column).astype(jnp.bfloat16)
        kept_list.append((grad_pair, hidden_scaled, flat_rows, flat_grads))
        rows_back, weights_back = to_owners(
            reduce_quad(part_rows.reshape(-1, groups, capacity, feature_count)),
            reduce_quad(part_weight.reshape(-1, groups, capacity)),
        )
        (
            finish_inputs,
            finish_scales,
            finish_normed,
            finish_places,
            finish_selector,
            finish_keeping,
            finish_weight_slots,
        ) = current
        summed = rows_back.reshape(slot_count, feature_count)
        weight_sums = weights_back.reshape(slot_count)
        expert_rows = jnp.sum(
            jnp.take(summed, finish_places, axis=0).reshape(token_rows, pick_count, feature_count),
            axis=1,
        )
        combine_grad = (
            jnp.take(weight_sums, finish_places) * finish_keeping.astype(jnp.float32)
        ).reshape(token_rows, pick_count)
        gained = gain_row * expert_rows
        mixed_mean = jnp.mean(finish_inputs * gained, axis=1, keepdims=True)
        leaving = (
            incoming.astype(jnp.float32)
            + finish_scales * gained
            - finish_inputs * (finish_scales * finish_scales * finish_scales) * mixed_mean
        ).astype(jnp.bfloat16)
        previous = leaving
        leaving_list.append(leaving)
        combine_list.append(combine_grad)
    pair_all = jnp.concatenate([kept[0] for kept in kept_list], axis=0)
    scaled_all = jnp.concatenate([kept[1] for kept in kept_list], axis=0)
    rows_all = jnp.concatenate([kept[2] for kept in kept_list], axis=0)
    grads_all = jnp.concatenate([kept[3] for kept in kept_list], axis=0)
    pair_total = contract_first(pair_all, rows_all).reshape(2, hidden_count, feature_count)
    down_total = contract_first(scaled_all, grads_all)[None]
    pair_reduced, down_reduced = (
        lax.psum_scatter(
            pair_total.astype(jnp.bfloat16), "dp", scatter_dimension=2, tiled=True
        ).astype(jnp.float32),
        lax.psum_scatter(
            down_total.astype(jnp.bfloat16), "dp", scatter_dimension=2, tiled=True
        ).astype(jnp.float32),
    )
    return (
        jnp.stack(leaving_list)[None],
        jnp.stack(combine_list)[None],
        pair_reduced[0:1].astype(jnp.bfloat16),
        pair_reduced[1:2].astype(jnp.bfloat16),
        down_reduced.astype(jnp.bfloat16),
    )


def solution(mesh):
    sizes = dict(zip(mesh.axis_names, mesh.devices.shape))
    members = sizes["expert"]
    grid = mesh.devices.reshape(sizes["pipe"], members // HSPLIT, HSPLIT, sizes["dp"])
    fine = Mesh(grid, ("pipe", "eg", "ej", "dp"))
    tokens = ("eg", "ej", "dp")
    rows = ("eg", "ej")
    in_specs = (
        P("pipe", None, tokens, None),
        P(None, tokens, None),
        P("pipe", tokens, None),
        P("pipe", None),
        P("pipe", None, tokens, None),
        P("pipe", None, tokens, None),
        P("pipe", None, tokens, None),
        P("pipe", rows, "dp"),
        P("pipe", rows, "dp"),
        P("pipe", rows, "dp"),
    )
    out_specs = (
        P("pipe", None, tokens, None),
        P("pipe", None, tokens, None),
        P("pipe", rows, "dp"),
        P("pipe", rows, "dp"),
        P("pipe", rows, "dp"),
    )
    return jax.shard_map(local, mesh=fine, in_specs=in_specs, out_specs=out_specs, check_vma=False)
```

```python
import jax
import jax.numpy as jnp
from jax import lax
from jax.sharding import Mesh, PartitionSpec as P

HSPLIT = 4


EPSILON = 1e-06


def shifted(block, axis, distance):
    devices = range(lax.axis_size(axis))
    route = [(i - distance, i) for i in devices if i - distance in devices]
    return lax.ppermute(block, axis, route)


def rotated(block, axis, distance):
    size = lax.axis_size(axis)
    route = [(i, (i + distance) % size) for i in range(size)]
    return lax.ppermute(block, axis, route)


def flipped(block, axis, mask):
    size = lax.axis_size(axis)
    route = [(i, i ^ mask) for i in range(size)]
    return lax.ppermute(block, axis, route)


def silu_parts(gate_value):
    sigmoid_value = jax.nn.sigmoid(gate_value)
    return (gate_value * sigmoid_value, sigmoid_value * (1.0 + gate_value * (1.0 - sigmoid_value)))


def contract_last(first_operand, second_operand):
    return lax.dot_general(
        first_operand, second_operand, (((1,), (1,)), ((), ())), preferred_element_type=jnp.float32
    )


def contract_first(first_operand, second_operand):
    return lax.dot_general(
        first_operand, second_operand, (((0,), (0,)), ((), ())), preferred_element_type=jnp.float32
    )


def to_experts(blocks):
    groups = blocks.shape[0]
    moved = [blocks[0]] + [rotated(blocks[s], "eg", s) for s in range(1, groups)]
    return jnp.stack(moved)


def to_owners(blocks, weights):
    groups, capacity, width = blocks.shape
    rows = [blocks[0]]
    sums = [weights[0]]
    for s in range(1, groups):
        high = weights[s].astype(jnp.bfloat16)
        low = (weights[s] - high.astype(jnp.float32)).astype(jnp.bfloat16)
        packed = jnp.pad(jnp.stack([high, low]), ((0, 0), (0, width - capacity)))
        block = jnp.concatenate([blocks[s].astype(jnp.bfloat16), packed], axis=0)
        got = rotated(block, "eg", -s).astype(jnp.float32)
        rows.append(got[:capacity])
        sums.append(got[capacity, :capacity] + got[capacity + 1, :capacity])
    return jnp.stack(rows), jnp.stack(sums)


def relayed(block):
    width = block.shape[-1]
    return lax.axis_size("ej") == 4 and width >= 256 and width % 256 == 0


def gather_quad(blocks):
    staged = to_experts(blocks)
    quad = lax.axis_size("ej")
    if not relayed(staged):
        return jnp.stack([staged] + [flipped(staged, "ej", t) for t in range(1, quad)])
    half = staged.shape[-1] // 2
    first = flipped(staged, "ej", 1)
    second = flipped(staged, "ej", 2)
    diagonal = jnp.concatenate(
        [flipped(first[..., :half], "ej", 2), flipped(second[..., half:], "ej", 1)], axis=-1
    )
    return jnp.stack([staged, first, second, diagonal])


def reduce_quad(parts):
    quad = parts.shape[0]
    total = parts[0].astype(jnp.float32)
    if not relayed(parts):
        for t in range(1, quad):
            total = total + flipped(parts[t], "ej", t).astype(jnp.float32)
        return total
    half = parts.shape[-1] // 2
    from_first = flipped(parts[3][..., :half], "ej", 1).astype(jnp.float32)
    from_second = flipped(parts[3][..., half:], "ej", 2).astype(jnp.float32)
    toward_second = jnp.concatenate(
        [(parts[2][..., :half].astype(jnp.float32) + from_first).astype(parts.dtype), parts[2][..., half:]],
        axis=-1,
    )
    toward_first = jnp.concatenate(
        [parts[1][..., :half], (parts[1][..., half:].astype(jnp.float32) + from_second).astype(parts.dtype)],
        axis=-1,
    )
    total = total + flipped(toward_second, "ej", 2).astype(jnp.float32)
    return total + flipped(toward_first, "ej", 1).astype(jnp.float32)


def local(
    saved_inputs,
    output_grads,
    entry_grads,
    norm_gain,
    expert_ids,
    keep_flags,
    combine_weights,
    gate_weight,
    up_weight,
    down_weight,
):
    sections = lax.axis_size("pipe")
    is_last = lax.axis_index("pipe") == sections - 1
    groups = lax.axis_size("eg")
    me = lax.axis_index("eg")
    micro_count = saved_inputs.shape[1]
    token_rows = saved_inputs.shape[2]
    feature_count = saved_inputs.shape[3]
    pick_count = expert_ids.shape[3]
    capacity = max(2, 3 * token_rows * pick_count // (2 * groups))
    slot_count = groups * capacity
    low_half = lax.axis_index("dp") == 0

    def whole_rows(stored):
        if lax.axis_size("dp") != 2:
            return lax.all_gather(stored, "dp", axis=1, tiled=True)
        partner = flipped(stored, "dp", 1)
        return jnp.where(
            low_half,
            jnp.concatenate([stored, partner], axis=1),
            jnp.concatenate([partner, stored], axis=1),
        )

    gate_full, up_full, down_full = (
        whole_rows(gate_weight[0]),
        whole_rows(up_weight[0]),
        whole_rows(down_weight[0]),
    )
    hidden_count = gate_full.shape[0]
    paired_weights = jnp.concatenate([gate_full, up_full], axis=0)
    gain_row = norm_gain[0][None, :]
    slot_ids = jnp.arange(slot_count, dtype=jnp.int32)
    expert_range = jnp.arange(groups, dtype=jnp.int32)

    def prepare(moment):
        inputs = saved_inputs[0, moment].astype(jnp.float32)
        scales = lax.rsqrt(jnp.mean(inputs * inputs, axis=1, keepdims=True) + EPSILON)
        normed = (inputs * scales * gain_row).astype(jnp.bfloat16)
        chosen = expert_ids[0, moment].reshape(-1)
        onehot = (chosen[:, None] == expert_range[None, :]).astype(jnp.int32)
        rank_values = jnp.sum((jnp.cumsum(onehot, axis=0) - 1) * onehot, axis=1)
        places = ((chosen - me) % groups) * capacity + rank_values
        placing = places[:, None] == slot_ids[None, :]
        token_map = jnp.any(placing.reshape(token_rows, pick_count, slot_count), axis=1)
        selector = token_map.T.astype(jnp.bfloat16)
        keeping = keep_flags[0, moment].reshape(-1)
        scaled = (combine_weights[0, moment].reshape(-1) * keeping.astype(jnp.bfloat16)).astype(
            jnp.float32
        )
        weight_slots = jnp.sum(jnp.where(placing, scaled[:, None], 0.0), axis=0).astype(
            jnp.bfloat16
        )
        return (inputs, scales, normed, places, selector, keeping, weight_slots)

    def dispatch_rows(selector, source_rows):
        picked = jnp.dot(selector, source_rows, preferred_element_type=jnp.float32)
        return picked.astype(jnp.bfloat16).reshape(groups, capacity, feature_count)

    prepared = [prepare(moment) for moment in range(micro_count)]
    first_incoming = jnp.where(is_last, output_grads[0], entry_grads[0])
    first_grads = gather_quad(dispatch_rows(prepared[0][4], first_incoming))
    rows_gathered = [gather_quad(dispatch_rows(prepared[0][4], prepared[0][2]))]
    weights_gathered = [gather_quad(prepared[0][6].reshape(groups, capacity))]
    for current in prepared[1:]:
        later_rows, later_weights = dispatch_rows(current[4], current[2]), current[6]
        rows_gathered.append(gather_quad(later_rows))
        weights_gathered.append(gather_quad(later_weights.reshape(groups, capacity)))
    leaving_list = []
    combine_list = []
    kept_list = []
    previous = entry_grads[0]
    for moment in range(micro_count):
        current = prepared[moment]
        if moment == 0:
            incoming = first_incoming
            grads_in = first_grads
        else:
            arriving = shifted(previous, "pipe", -1)
            incoming = jnp.where(is_last, output_grads[moment], arriving)
            grads_in = gather_quad(dispatch_rows(current[4], incoming))
        flat_rows = rows_gathered[moment].reshape(-1, feature_count)
        flat_grads = grads_in.reshape(-1, feature_count)
        scale_column = weights_gathered[moment].reshape(-1, 1).astype(jnp.float32)
        gate_value = contract_last(flat_rows, gate_full)
        upward = contract_last(flat_rows, up_full)
        backward = contract_last(flat_grads, down_full)
        active, derivative = silu_parts(gate_value)
        hidden = active * upward
        part_weight = jnp.sum(hidden * backward, axis=1).astype(jnp.bfloat16)
        grad_up = (scale_column * backward * active).astype(jnp.bfloat16)
        grad_gate = (scale_column * backward * upward * derivative).astype(jnp.bfloat16)
        grad_pair = jnp.concatenate([grad_gate, grad_up], axis=1)
        part_rows = jnp.dot(grad_pair, paired_weights, preferred_element_type=jnp.float32).astype(
            jnp.bfloat16
        )
        hidden_scaled = (hidden * scale_column).astype(jnp.bfloat16)
        kept_list.append((grad_pair, hidden_scaled, flat_rows, flat_grads))
        rows_back, weights_back = to_owners(
            reduce_quad(part_rows.reshape(-1, groups, capacity, feature_count)),
            reduce_quad(part_weight.reshape(-1, groups, capacity)),
        )
        (
            finish_inputs,
            finish_scales,
            finish_normed,
            finish_places,
            finish_selector,
            finish_keeping,
            finish_weight_slots,
        ) = current
        summed = rows_back.reshape(slot_count, feature_count)
        weight_sums = weights_back.reshape(slot_count)
        expert_rows = jnp.sum(
            jnp.take(summed, finish_places, axis=0).reshape(token_rows, pick_count, feature_count),
            axis=1,
        )
        combine_grad = (
            jnp.take(weight_sums, finish_places) * finish_keeping.astype(jnp.float32)
        ).reshape(token_rows, pick_count)
        gained = gain_row * expert_rows
        mixed_mean = jnp.mean(finish_inputs * gained, axis=1, keepdims=True)
        leaving = (
            incoming.astype(jnp.float32)
            + finish_scales * gained
            - finish_inputs * (finish_scales * finish_scales * finish_scales) * mixed_mean
        ).astype(jnp.bfloat16)
        previous = leaving
        leaving_list.append(leaving)
        combine_list.append(combine_grad)
    pair_all = jnp.concatenate([kept[0] for kept in kept_list], axis=0)
    scaled_all = jnp.concatenate([kept[1] for kept in kept_list], axis=0)
    rows_all = jnp.concatenate([kept[2] for kept in kept_list], axis=0)
    grads_all = jnp.concatenate([kept[3] for kept in kept_list], axis=0)
    pair_total = contract_first(pair_all, rows_all).reshape(2, hidden_count, feature_count)
    down_total = contract_first(scaled_all, grads_all)[None]
    pair_reduced, down_reduced = (
        lax.psum_scatter(
            pair_total.astype(jnp.bfloat16), "dp", scatter_dimension=2, tiled=True
        ).astype(jnp.float32),
        lax.psum_scatter(
            down_total.astype(jnp.bfloat16), "dp", scatter_dimension=2, tiled=True
        ).astype(jnp.float32),
    )
    return (
        jnp.stack(leaving_list)[None],
        jnp.stack(combine_list)[None],
        pair_reduced[0:1].astype(jnp.bfloat16),
        pair_reduced[1:2].astype(jnp.bfloat16),
        down_reduced.astype(jnp.bfloat16),
    )


def solution(mesh):
    sizes = dict(zip(mesh.axis_names, mesh.devices.shape))
    members = sizes["expert"]
    grid = mesh.devices.reshape(sizes["pipe"], members // HSPLIT, HSPLIT, sizes["dp"])
    fine = Mesh(grid, ("pipe", "eg", "ej", "dp"))
    tokens = ("eg", "ej", "dp")
    rows = ("eg", "ej")
    in_specs = (
        P("pipe", None, tokens, None),
        P(None, tokens, None),
        P("pipe", tokens, None),
        P("pipe", None),
        P("pipe", None, tokens, None),
        P("pipe", None, tokens, None),
        P("pipe", None, tokens, None),
        P("pipe", rows, "dp"),
        P("pipe", rows, "dp"),
        P("pipe", rows, "dp"),
    )
    out_specs = (
        P("pipe", None, tokens, None),
        P("pipe", None, tokens, None),
        P("pipe", rows, "dp"),
        P("pipe", rows, "dp"),
        P("pipe", rows, "dp"),
    )
    return jax.shard_map(local, mesh=fine, in_specs=in_specs, out_specs=out_specs, check_vma=False)
```

```python
import jax
import jax.numpy as jnp
from jax import lax
from jax.sharding import Mesh, PartitionSpec as P

HSPLIT = 4


EPSILON = 1e-06


def shifted(block, axis, distance):
    devices = range(lax.axis_size(axis))
    route = [(i - distance, i) for i in devices if i - distance in devices]
    return lax.ppermute(block, axis, route)


def rotated(block, axis, distance):
    size = lax.axis_size(axis)
    route = [(i, (i + distance) % size) for i in range(size)]
    return lax.ppermute(block, axis, route)


def flipped(block, axis, mask):
    size = lax.axis_size(axis)
    route = [(i, i ^ mask) for i in range(size)]
    return lax.ppermute(block, axis, route)


def silu_parts(gate_value):
    sigmoid_value = jax.nn.sigmoid(gate_value)
    return (gate_value * sigmoid_value, sigmoid_value * (1.0 + gate_value * (1.0 - sigmoid_value)))


def contract_last(first_operand, second_operand):
    return lax.dot_general(
        first_operand, second_operand, (((1,), (1,)), ((), ())), preferred_element_type=jnp.float32
    )


def contract_first(first_operand, second_operand):
    return lax.dot_general(
        first_operand, second_operand, (((0,), (0,)), ((), ())), preferred_element_type=jnp.float32
    )


def to_experts(blocks):
    groups = blocks.shape[0]
    moved = [blocks[0]] + [rotated(blocks[s], "eg", s) for s in range(1, groups)]
    return jnp.stack(moved)


def to_owners(blocks, weights):
    groups, capacity, width = blocks.shape
    rows = [blocks[0]]
    sums = [weights[0]]
    for s in range(1, groups):
        high = weights[s].astype(jnp.bfloat16)
        low = (weights[s] - high.astype(jnp.float32)).astype(jnp.bfloat16)
        packed = jnp.pad(jnp.stack([high, low]), ((0, 0), (0, width - capacity)))
        block = jnp.concatenate([blocks[s].astype(jnp.bfloat16), packed], axis=0)
        got = rotated(block, "eg", -s).astype(jnp.float32)
        rows.append(got[:capacity])
        sums.append(got[capacity, :capacity] + got[capacity + 1, :capacity])
    return jnp.stack(rows), jnp.stack(sums)


def relayed(block):
    width = block.shape[-1]
    return lax.axis_size("ej") == 4 and width >= 256 and width % 256 == 0


def gather_quad(blocks):
    staged = to_experts(blocks)
    quad = lax.axis_size("ej")
    if not relayed(staged):
        return jnp.stack([staged] + [flipped(staged, "ej", t) for t in range(1, quad)])
    half = staged.shape[-1] // 2
    first = flipped(staged, "ej", 1)
    second = flipped(staged, "ej", 2)
    diagonal = jnp.concatenate(
        [flipped(first[..., :half], "ej", 2), flipped(second[..., half:], "ej", 1)], axis=-1
    )
    return jnp.stack([staged, first, second, diagonal])


def reduce_quad(parts):
    quad = parts.shape[0]
    total = parts[0].astype(jnp.float32)
    if not relayed(parts):
        for t in range(1, quad):
            total = total + flipped(parts[t], "ej", t).astype(jnp.float32)
        return total
    half = parts.shape[-1] // 2
    from_first = flipped(parts[3][..., :half], "ej", 1).astype(jnp.float32)
    from_second = flipped(parts[3][..., half:], "ej", 2).astype(jnp.float32)
    toward_second = jnp.concatenate(
        [(parts[2][..., :half].astype(jnp.float32) + from_first).astype(parts.dtype), parts[2][..., half:]],
        axis=-1,
    )
    toward_first = jnp.concatenate(
        [parts[1][..., :half], (parts[1][..., half:].astype(jnp.float32) + from_second).astype(parts.dtype)],
        axis=-1,
    )
    total = total + flipped(toward_second, "ej", 2).astype(jnp.float32)
    return total + flipped(toward_first, "ej", 1).astype(jnp.float32)


def local(
    saved_inputs,
    output_grads,
    entry_grads,
    norm_gain,
    expert_ids,
    keep_flags,
    combine_weights,
    gate_weight,
    up_weight,
    down_weight,
):
    sections = lax.axis_size("pipe")
    is_last = lax.axis_index("pipe") == sections - 1
    groups = lax.axis_size("eg")
    me = lax.axis_index("eg")
    micro_count = saved_inputs.shape[1]
    token_rows = saved_inputs.shape[2]
    feature_count = saved_inputs.shape[3]
    pick_count = expert_ids.shape[3]
    capacity = max(2, 3 * token_rows * pick_count // (2 * groups))
    slot_count = groups * capacity
    low_half = lax.axis_index("dp") == 0

    def whole_rows(stored):
        if lax.axis_size("dp") != 2:
            return lax.all_gather(stored, "dp", axis=1, tiled=True)
        partner = flipped(stored, "dp", 1)
        return jnp.where(
            low_half,
            jnp.concatenate([stored, partner], axis=1),
            jnp.concatenate([partner, stored], axis=1),
        )

    gate_full, up_full, down_full = (
        whole_rows(gate_weight[0]),
        whole_rows(up_weight[0]),
        whole_rows(down_weight[0]),
    )
    hidden_count = gate_full.shape[0]
    paired_weights = jnp.concatenate([gate_full, up_full], axis=0)
    gain_row = norm_gain[0][None, :]
    slot_ids = jnp.arange(slot_count, dtype=jnp.int32)
    expert_range = jnp.arange(groups, dtype=jnp.int32)

    def prepare(moment):
        inputs = saved_inputs[0, moment].astype(jnp.float32)
        scales = lax.rsqrt(jnp.mean(inputs * inputs, axis=1, keepdims=True) + EPSILON)
        normed = (inputs * scales * gain_row).astype(jnp.bfloat16)
        chosen = expert_ids[0, moment].reshape(-1)
        onehot = (chosen[:, None] == expert_range[None, :]).astype(jnp.int32)
        rank_values = jnp.sum((jnp.cumsum(onehot, axis=0) - 1) * onehot, axis=1)
        places = ((chosen - me) % groups) * capacity + rank_values
        placing = places[:, None] == slot_ids[None, :]
        token_map = jnp.any(placing.reshape(token_rows, pick_count, slot_count), axis=1)
        selector = token_map.T.astype(jnp.bfloat16)
        keeping = keep_flags[0, moment].reshape(-1)
        scaled = (combine_weights[0, moment].reshape(-1) * keeping.astype(jnp.bfloat16)).astype(
            jnp.float32
        )
        weight_slots = jnp.sum(jnp.where(placing, scaled[:, None], 0.0), axis=0).astype(
            jnp.bfloat16
        )
        return (inputs, scales, normed, places, selector, keeping, weight_slots)

    def dispatch_rows(selector, source_rows):
        picked = jnp.dot(selector, source_rows, preferred_element_type=jnp.float32)
        return picked.astype(jnp.bfloat16).reshape(groups, capacity, feature_count)

    prepared = [prepare(moment) for moment in range(micro_count)]
    first_incoming = jnp.where(is_last, output_grads[0], entry_grads[0])
    rows_gathered = [gather_quad(dispatch_rows(prepared[0][4], prepared[0][2]))]
    first_grads = gather_quad(dispatch_rows(prepared[0][4], first_incoming))
    weights_gathered = [gather_quad(prepared[0][6].reshape(groups, capacity))]
    for current in prepared[1:]:
        later_rows, later_weights, _ = lax.optimization_barrier(
            (dispatch_rows(current[4], current[2]), current[6], first_grads)
        )
        rows_gathered.append(gather_quad(later_rows))
        weights_gathered.append(gather_quad(later_weights.reshape(groups, capacity)))
    leaving_list = []
    combine_list = []
    kept_list = []
    previous = entry_grads[0]
    for moment in range(micro_count):
        current = prepared[moment]
        if moment == 0:
            incoming = first_incoming
            grads_in = first_grads
        else:
            arriving = shifted(previous, "pipe", -1)
            incoming = jnp.where(is_last, output_grads[moment], arriving)
            grads_in = gather_quad(dispatch_rows(current[4], incoming))
        flat_rows = rows_gathered[moment].reshape(-1, feature_count)
        flat_grads = grads_in.reshape(-1, feature_count)
        scale_column = weights_gathered[moment].reshape(-1, 1).astype(jnp.float32)
        gate_value = contract_last(flat_rows, gate_full)
        upward = contract_last(flat_rows, up_full)
        backward = contract_last(flat_grads, down_full)
        active, derivative = silu_parts(gate_value)
        hidden = active * upward
        part_weight = jnp.sum(hidden * backward, axis=1).astype(jnp.bfloat16)
        grad_up = (scale_column * backward * active).astype(jnp.bfloat16)
        grad_gate = (scale_column * backward * upward * derivative).astype(jnp.bfloat16)
        grad_pair = jnp.concatenate([grad_gate, grad_up], axis=1)
        part_rows = jnp.dot(grad_pair, paired_weights, preferred_element_type=jnp.float32).astype(
            jnp.bfloat16
        )
        hidden_scaled = (hidden * scale_column).astype(jnp.bfloat16)
        kept_list.append((grad_pair, hidden_scaled, flat_rows, flat_grads))
        rows_back, weights_back = to_owners(
            reduce_quad(part_rows.reshape(-1, groups, capacity, feature_count)),
            reduce_quad(part_weight.reshape(-1, groups, capacity)),
        )
        (
            finish_inputs,
            finish_scales,
            finish_normed,
            finish_places,
            finish_selector,
            finish_keeping,
            finish_weight_slots,
        ) = current
        summed = rows_back.reshape(slot_count, feature_count)
        weight_sums = weights_back.reshape(slot_count)
        expert_rows = jnp.sum(
            jnp.take(summed, finish_places, axis=0).reshape(token_rows, pick_count, feature_count),
            axis=1,
        )
        combine_grad = (
            jnp.take(weight_sums, finish_places) * finish_keeping.astype(jnp.float32)
        ).reshape(token_rows, pick_count)
        gained = gain_row * expert_rows
        mixed_mean = jnp.mean(finish_inputs * gained, axis=1, keepdims=True)
        leaving = (
            incoming.astype(jnp.float32)
            + finish_scales * gained
            - finish_inputs * (finish_scales * finish_scales * finish_scales) * mixed_mean
        ).astype(jnp.bfloat16)
        previous = leaving
        leaving_list.append(leaving)
        combine_list.append(combine_grad)
    pair_all = jnp.concatenate([kept[0] for kept in kept_list], axis=0)
    scaled_all = jnp.concatenate([kept[1] for kept in kept_list], axis=0)
    rows_all = jnp.concatenate([kept[2] for kept in kept_list], axis=0)
    grads_all = jnp.concatenate([kept[3] for kept in kept_list], axis=0)
    pair_total = contract_first(pair_all, rows_all).reshape(2, hidden_count, feature_count)
    down_total = contract_first(scaled_all, grads_all)[None]
    pair_reduced, down_reduced = (
        lax.psum_scatter(
            pair_total.astype(jnp.bfloat16), "dp", scatter_dimension=2, tiled=True
        ).astype(jnp.float32),
        lax.psum_scatter(
            down_total.astype(jnp.bfloat16), "dp", scatter_dimension=2, tiled=True
        ).astype(jnp.float32),
    )
    return (
        jnp.stack(leaving_list)[None],
        jnp.stack(combine_list)[None],
        pair_reduced[0:1].astype(jnp.bfloat16),
        pair_reduced[1:2].astype(jnp.bfloat16),
        down_reduced.astype(jnp.bfloat16),
    )


def solution(mesh):
    sizes = dict(zip(mesh.axis_names, mesh.devices.shape))
    members = sizes["expert"]
    grid = mesh.devices.reshape(sizes["pipe"], members // HSPLIT, HSPLIT, sizes["dp"])
    fine = Mesh(grid, ("pipe", "eg", "ej", "dp"))
    tokens = ("eg", "ej", "dp")
    rows = ("eg", "ej")
    in_specs = (
        P("pipe", None, tokens, None),
        P(None, tokens, None),
        P("pipe", tokens, None),
        P("pipe", None),
        P("pipe", None, tokens, None),
        P("pipe", None, tokens, None),
        P("pipe", None, tokens, None),
        P("pipe", rows, "dp"),
        P("pipe", rows, "dp"),
        P("pipe", rows, "dp"),
    )
    out_specs = (
        P("pipe", None, tokens, None),
        P("pipe", None, tokens, None),
        P("pipe", rows, "dp"),
        P("pipe", rows, "dp"),
        P("pipe", rows, "dp"),
    )
    return jax.shard_map(local, mesh=fine, in_specs=in_specs, out_specs=out_specs, check_vma=False)
```
